128 devices in a mesh: seq: 32 (over x, y, core), wa: 4 (over z).
Axes of the slice: x: 4, y: 4, z: 4, core: 2. Of those that a mesh axis runs over, the one named last changes fastest.
Arguments:
- hidden_in: bfloat16 [16384, 2048], P('seq', 'wa'), may hold values from -6 to 6
- request_spans: int32 [4, 2], replicated, may hold values from 0 to 16384, as said below
- owners: int32 [4], replicated, may hold values from 0 to 31, as said below
- mixer_gain: float32 [2048], replicated, may hold values from 0.1 to 1.9
- query_weight: bfloat16 [2048, 2048], P(None, 'wa'), may hold values from -0.125 to 0.125
- forget_weight: bfloat16 [2048, 2048], P(None, 'wa'), may hold values from -0.0625 to 0.0625
- input_weight: bfloat16 [2048, 2048], P(None, 'wa'), may hold values from -0.125 to 0.125
- gate_weight: bfloat16 [2048, 2048], P(None, 'wa'), may hold values from -0.125 to 0.125
- forget_bias: float32 [2048], P('wa')
- output_weight: bfloat16 [2048, 2048], P('wa'), may hold values from -0.125 to 0.125
- swiglu_gain: float32 [2048], replicated, may hold values from 0.1 to 1.9
- swiglu_gate: bfloat16 [2048, 3072], P(None, 'wa'), may hold values from -0.125 to 0.125
- swiglu_up: bfloat16 [2048, 3072], P(None, 'wa'), may hold values from -0.125 to 0.125
- swiglu_down: bfloat16 [3072, 2048], P('wa'), may hold values from -0.109375 to 0.109375
Outputs:
- hidden_out: bfloat16 [16384, 2048], P('seq', 'wa')
- handed_state: float32 [32, 16, 128, 128], P('seq', 'wa')
The draws below stay inside these ranges and needn't reach their ends.
Inputs may be any that keep to these rules, and one draw needn't show every extreme that they name: Requests lie back to back in order: request_spans[0, 0] = 0, each request's end equals the next one's start, the last end is 16384, and every request holds at least 64 tokens. The owners are distinct indices along seq; the last request's owner is the index half of 32 minus one; the first request's owner is the index just before that of the device holding the first request's last token, counted round; the index 31 is always an owner.
All inputs are finite; a program needn't handle non-finite values.
Results may differ from the reference program's by a relative error of at most 0.009.
Values may be sent and summed in bfloat16 or wider, within the bound.
No kernel may reach another device: no remote copies, remote signals or barrier semaphores. Data moves between devices by JAX's collectives and lax.ppermute only.
A program may use at most 128 MiB of HBM per device.

```python
import jax
import jax.numpy as jnp
from jax import lax

D = 2048
H = 16
HEAD = 128
FF = 3072
GROUP = 64
REQS = 4
TOK_DEV = 512
TOKENS = 16384
N_SEQ = 32


def draw_request_spans(key, part):
    key_length, key_place = jax.random.split(key)
    lowest = max(GROUP, TOK_DEV // 4)
    shorter = jax.random.randint(key_length, (REQS,), lowest, lowest + TOK_DEV // 2 + 1)
    long_place = jax.random.randint(key_place, (), 0, REQS)
    ranks = jnp.arange(REQS)
    others = jnp.sum(jnp.where(ranks == long_place, 0, shorter))
    lengths = jnp.where(ranks == long_place, TOKENS - others, shorter).astype(jnp.int32)
    end_rows = jnp.cumsum(lengths).astype(jnp.int32)
    return jnp.stack([end_rows - lengths, end_rows], axis=1).astype(jnp.int32)


def draw_owners(key, part):
    spans = draw_request_spans(key, part)
    across = N_SEQ // 2 - 1
    first_device = ((spans[0, 1] - 1) // TOK_DEV).astype(jnp.int32)
    first_owner = jnp.where(first_device == 0, N_SEQ - 1, first_device - 1).astype(jnp.int32)
    shuffled = jax.random.permutation(jax.random.fold_in(key, 7), N_SEQ).astype(jnp.int32)
    ranked = jnp.arange(N_SEQ, dtype=jnp.int32)
    taken = (ranked == first_owner) | (ranked == across)
    scores = jnp.where(taken, N_SEQ + ranked, jnp.where(ranked == N_SEQ - 1, -1, shuffled)).astype(jnp.int32)
    picked = jnp.argsort(scores, stable=True)[:REQS - 2].astype(jnp.int32)
    return jnp.concatenate([first_owner[None], picked, jnp.array([across], jnp.int32)]).astype(jnp.int32)


def draw_forget_bias(key, part):
    key_head, key_rate = jax.random.split(key)
    picked = jax.random.uniform(key_head, (H,), jnp.float32)
    slow_heads = picked < 0.5
    slow_mask = jnp.repeat(slow_heads, HEAD)
    placing = jax.random.uniform(key_rate, (H * HEAD,), jnp.float32)
    slow_rate = jnp.exp(jnp.log(0.3 / TOKENS) + placing * jnp.log(2.0 / 0.3))
    fast_rate = jnp.exp(jnp.log(1.0 / 30.0) - placing * jnp.log(TOK_DEV / 30.0))
    chosen_rate = jnp.where(slow_mask, slow_rate, fast_rate)
    return jnp.log(1.0 / chosen_rate - 1.0).astype(jnp.float32)


def block_levels(rng, shape, cuts, least, largest):
    def one(dim, blocks):
        steps = jax.random.uniform(jax.random.fold_in(jax.random.fold_in(rng, 6), dim), (blocks,), jnp.float32, least / len(cuts), largest / len(cuts))
        return jnp.repeat(jnp.exp(steps), shape[dim] // blocks).reshape((-1,) + (1,) * (len(shape) - dim - 1))

    level = one(*cuts[0])
    for cut in cuts[1:]:
        level = level * one(*cut)
    return level


def gaussian(rng, dims, deviation, limit, cuts=(), held_as=jnp.bfloat16):
    gain = block_levels(rng, dims, cuts, -0.22, 0.18) if cuts else 1.0
    values = jax.random.normal(rng, dims, jnp.float32) * deviation * gain
    return jnp.minimum(jnp.maximum(values, -limit), limit).astype(held_as)


def setup_inputs(seed: int = 0) -> dict:
    arg_keys = jax.random.split(jax.random.key(seed), 15)
    hidden_in = gaussian(arg_keys[0], (TOKENS, D), 1.0, 6.0, ((0, 32), (1, 4)))
    request_spans = draw_request_spans(jax.random.fold_in(arg_keys[14], 71), 0)
    owners = draw_owners(jax.random.fold_in(arg_keys[14], 71), 0)
    mixer_gain = jnp.clip(1.0 + 0.18 * jax.random.normal(arg_keys[3], (D,), jnp.float32), 0.1, 1.9)
    query_weight = gaussian(arg_keys[4], (D, D), D ** -0.5, 0.125, ((1, 4),))
    forget_weight = gaussian(arg_keys[5], (D, D), (4 * D) ** -0.5, 0.0625, ((1, 4),))
    input_weight = gaussian(arg_keys[6], (D, D), D ** -0.5, 0.125, ((1, 4),))
    gate_weight = gaussian(arg_keys[7], (D, D), D ** -0.5, 0.125, ((1, 4),))
    forget_bias = draw_forget_bias(jax.random.fold_in(arg_keys[14], 71), 0)
    output_weight = gaussian(arg_keys[9], (D, D), D ** -0.5, 0.125, ((0, 4),))
    swiglu_gain = jnp.clip(1.0 + 0.18 * jax.random.normal(arg_keys[10], (D,), jnp.float32), 0.1, 1.9)
    swiglu_gate = gaussian(arg_keys[11], (D, FF), D ** -0.5, 0.125, ((1, 4),))
    swiglu_up = gaussian(arg_keys[12], (D, FF), D ** -0.5, 0.125, ((1, 4),))
    swiglu_down = gaussian(arg_keys[13], (FF, D), FF ** -0.5, 0.109375, ((0, 4),))
    return dict(hidden_in=hidden_in, request_spans=request_spans, owners=owners, mixer_gain=mixer_gain, query_weight=query_weight, forget_weight=forget_weight, input_weight=input_weight, gate_weight=gate_weight, forget_bias=forget_bias, output_weight=output_weight, swiglu_gain=swiglu_gain, swiglu_gate=swiglu_gate, swiglu_up=swiglu_up, swiglu_down=swiglu_down)


EPS = 1e-06
HIGH = lax.Precision.HIGHEST

def rms_rows(matrix, scaling):
    matrix = matrix.astype(jnp.float32)
    rescale = lax.rsqrt(lax.optimization_barrier(jnp.mean(matrix * matrix, axis=-1, keepdims=True)) + EPS)
    return (matrix * rescale * scaling).astype(jnp.bfloat16)

def project(matrix, weight):
    return jnp.dot(matrix, weight, preferred_element_type=jnp.float32)

def reference(hidden_in, request_spans, owners, mixer_gain, query_weight, forget_weight, input_weight, gate_weight, forget_bias, output_weight, swiglu_gain, swiglu_gate, swiglu_up, swiglu_down):
    normed = rms_rows(hidden_in, mixer_gain)
    queries = jax.nn.silu(project(normed, query_weight))
    forget_logit = project(normed, forget_weight) + forget_bias
    log_decay = jax.nn.log_sigmoid(forget_logit)
    key_rows = jax.nn.sigmoid(-forget_logit)
    value_rows = project(normed, input_weight)
    gate_logit = project(normed, gate_weight)
    position = jnp.arange(TOKENS, dtype=jnp.int32)
    start_rows = request_spans[:, 0].astype(jnp.int32)
    end_rows = request_spans[:, 1].astype(jnp.int32)
    is_start = jnp.any(position[:, None] == start_rows[None, :], axis=1)
    segment = (lax.optimization_barrier(jnp.sum((start_rows[None, :] <= position[:, None]).astype(jnp.int32), axis=1)) - 1).astype(jnp.int32)
    block_count = TOKENS // GROUP
    shape_four = (block_count, GROUP, H, HEAD)
    scanned = (queries.reshape(shape_four), log_decay.reshape(shape_four), key_rows.reshape(shape_four), value_rows.reshape(shape_four), segment.reshape(block_count, GROUP), (1.0 - is_start.astype(jnp.float32)).reshape(block_count, GROUP), jnp.arange(block_count, dtype=jnp.int32) * GROUP)
    offsets = jnp.arange(GROUP, dtype=jnp.int32)
    causal = offsets[:, None] >= offsets[None, :]

    def advance(carried, blocked):
        running, handed = carried
        query_part, decay_part, key_part, value_part, segment_part, keep_mask, first_row = blocked
        cum_decay = jnp.cumsum(decay_part, axis=0)
        surviving = jnp.cumprod(keep_mask)
        query_tilde = query_part * jnp.exp(cum_decay)
        key_tilde = key_part * jnp.exp(-cum_decay)
        same_doc = causal & (segment_part[:, None] == segment_part[None, :])
        scores = jnp.einsum('ihc,jhc->hij', query_tilde, key_tilde, precision=HIGH)
        scores = jnp.where(same_doc[None], scores, 0.0)
        result = jnp.einsum('hij,jhd->ihd', scores, value_part, precision=HIGH)
        result = result + surviving[:, None, None] * jnp.einsum('ihc,hcd->ihd', query_tilde, running, precision=HIGH)
        tail_mask = (segment_part == segment_part[-1]).astype(jnp.float32)
        fresh = jnp.einsum('jhc,jhd->hcd', key_tilde * tail_mask[:, None, None], value_part, precision=HIGH)
        new_state = jnp.exp(cum_decay[-1])[:, :, None] * (surviving[-1] * running + fresh)
        local_end = (end_rows - 1 - first_row).astype(jnp.int32)
        inside = (local_end >= 0) & (local_end < GROUP)
        end_row = jnp.sum(jnp.where(inside, local_end, 0)).astype(jnp.int32)
        decay_end = lax.dynamic_index_in_dim(cum_decay, end_row, 0, keepdims=False)
        segment_end = lax.dynamic_index_in_dim(segment_part, end_row, 0, keepdims=False)
        alive_end = lax.dynamic_index_in_dim(surviving, end_row, 0, keepdims=False)
        upto_mask = ((offsets <= end_row) & (segment_part == segment_end)).astype(jnp.float32)
        partial_end = jnp.einsum('jhc,jhd->hcd', key_tilde * upto_mask[:, None, None], value_part, precision=HIGH)
        end_state = jnp.exp(decay_end)[:, :, None] * (alive_end * running + partial_end)
        handed = handed + inside.astype(jnp.float32)[:, None, None, None] * end_state[None]
        return ((new_state, handed), result)
    zero_state = jnp.zeros((H, HEAD, HEAD), jnp.float32)
    zero_handed = jnp.zeros((REQS, H, HEAD, HEAD), jnp.float32)
    (final_state, handed), outputs = lax.scan(advance, (zero_state, zero_handed), scanned)
    mixer_out = outputs.reshape(TOKENS, H, HEAD)
    rescale = lax.rsqrt(lax.optimization_barrier(jnp.mean(mixer_out * mixer_out, axis=-1, keepdims=True)) + EPS)
    mixed_rows = (mixer_out * rescale * jax.nn.silu(gate_logit.reshape(TOKENS, H, HEAD))).reshape(TOKENS, D).astype(jnp.bfloat16)
    residual = (hidden_in.astype(jnp.float32) + project(mixed_rows, output_weight)).astype(jnp.bfloat16)
    normed_ffn = rms_rows(residual, swiglu_gain)
    hidden = (jax.nn.silu(project(normed_ffn, swiglu_gate)) * project(normed_ffn, swiglu_up)).astype(jnp.bfloat16)
    hidden_out = (residual.astype(jnp.float32) + project(hidden, swiglu_down)).astype(jnp.bfloat16)
    handed_state = jnp.zeros((N_SEQ, H, HEAD, HEAD), jnp.float32).at[owners.astype(jnp.int32)].set(handed)
    return (hidden_out, handed_state)
```

```python
import jax
import jax.numpy as jnp
from jax import lax
from jax.sharding import PartitionSpec as P

HEAD = 128
GROUP = 64
REQS = 4


EPS = 1e-06
HIGH = lax.Precision.HIGHEST


def entering(decay, state, axis):
    count, mine = (lax.axis_size(axis), lax.axis_index(axis))
    step_one = [(i, i + 1) for i in range(count - 1)]
    decay = jnp.where(mine == 0, 1.0, lax.ppermute(decay, axis, step_one))
    state = lax.ppermute(state, axis, step_one)
    stride = 1
    while stride < count:
        pairs = [(i, i + stride) for i in range(count - stride)]
        decay_in = lax.ppermute(decay, axis, pairs)
        state_in = lax.ppermute(state, axis, pairs)
        has = mine >= stride
        state = jnp.where(has, decay[..., None] * state_in + state, state)
        decay = jnp.where(has, decay_in * decay, decay)
        stride *= 2
    return state


def route_states(end_states, end_rows, owners, tok_rows, axis):
    count, mine = (lax.axis_size(axis), lax.axis_index(axis))
    moved = end_states.astype(jnp.bfloat16)
    left = [(i, (i - 1) % count) for i in range(count)]
    first = lax.ppermute(moved[0], axis, left)
    last = lax.ppermute(moved[-1], axis, [(count - 1, count // 2 - 1)])
    middle = moved[1:-1]
    place = ((end_rows - 1) // tok_rows)[1:-1]
    offset = (owners[1:-1] - place) % count
    for bit in range((count - 1).bit_length()):
        stride = 1 << bit
        moving = ((offset >> bit) & 1) == 1
        go = (moving & (place == mine))[:, None, None, None]
        sent = jnp.where(go, middle, jnp.zeros_like(middle))
        got = lax.ppermute(sent, axis, [(i, (i + stride) % count) for i in range(count)])
        middle = jnp.where(go, jnp.zeros_like(middle), middle) + got
        place = jnp.where(moving, (place + stride) % count, place)
    zero = jnp.zeros_like(first)
    held = jnp.where(owners[0] == mine, first, zero) + jnp.where(owners[-1] == mine, last, zero)
    held = held + jnp.sum(middle, axis=0)
    return held.astype(jnp.float32)[None]


def rms_rows(matrix, scaling):
    matrix = matrix.astype(jnp.float32)
    rescale = lax.rsqrt(jnp.mean(matrix * matrix, axis=-1, keepdims=True) + EPS)
    return (matrix * rescale * scaling).astype(jnp.bfloat16)


def project(matrix, weight):
    return jnp.dot(matrix, weight, preferred_element_type=jnp.float32)


def widen_rows(shard_part):
    return lax.all_gather(shard_part, "wa", axis=1, tiled=True)


def narrow_sum(partial_terms):
    return lax.psum_scatter(partial_terms, "wa", scatter_dimension=1, tiled=True)


def local(
    hidden_in,
    request_spans,
    owners,
    mixer_gain,
    query_weight,
    forget_weight,
    input_weight,
    gate_weight,
    forget_bias,
    output_weight,
    swiglu_gain,
    swiglu_gate,
    swiglu_up,
    swiglu_down,
):
    tok_rows = hidden_in.shape[0]
    head_count = query_weight.shape[1] // HEAD
    block_count = tok_rows // GROUP
    gathered = widen_rows(hidden_in)
    normed = rms_rows(gathered, mixer_gain)
    queries = jax.nn.silu(project(normed, query_weight))
    forget_logit = project(normed, forget_weight) + forget_bias
    log_decay = jax.nn.log_sigmoid(forget_logit)
    key_rows = jax.nn.sigmoid(-forget_logit)
    value_rows = project(normed, input_weight)
    gate_logit = project(normed, gate_weight)
    first_row = lax.axis_index("seq") * tok_rows
    position = first_row + jnp.arange(tok_rows, dtype=jnp.int32)
    start_rows = request_spans[:, 0]
    end_rows = request_spans[:, 1]
    is_start = jnp.any(position[:, None] == start_rows[None, :], axis=1)
    segment = jnp.sum((start_rows[None, :] <= position[:, None]).astype(jnp.int32), axis=1) - 1
    shape_four = (block_count, GROUP, head_count, HEAD)
    query_parts = queries.reshape(shape_four)
    key_parts = key_rows.reshape(shape_four)
    value_parts = value_rows.reshape(shape_four)
    segment_parts = segment.reshape(block_count, GROUP)
    keep_mask = (1.0 - is_start.astype(jnp.float32)).reshape(block_count, GROUP)
    cum_decay = jnp.cumsum(log_decay.reshape(shape_four), axis=1)
    surviving = jnp.cumprod(keep_mask, axis=1)
    query_tilde = query_parts * jnp.exp(cum_decay)
    key_tilde = key_parts * jnp.exp(-cum_decay)
    offsets = jnp.arange(GROUP, dtype=jnp.int32)
    causal = offsets[:, None] >= offsets[None, :]
    same_doc = causal[None] & (segment_parts[:, :, None] == segment_parts[:, None, :])
    scores = jnp.einsum("nihc,njhc->nhij", query_tilde, key_tilde, precision=HIGH)
    scores = jnp.where(same_doc[:, None], scores, 0.0)
    inner_out = jnp.einsum("nhij,njhd->nihd", scores, value_parts, precision=HIGH)
    tail_mask = (segment_parts == segment_parts[:, -1:]).astype(jnp.float32)
    last_decay = jnp.exp(cum_decay[:, -1])
    fresh = last_decay[..., None] * jnp.einsum(
        "njhc,njhd->nhcd", key_tilde * tail_mask[:, :, None, None], value_parts, precision=HIGH
    )
    shrink = surviving[:, -1][:, None, None] * last_decay

    def advance(carried, blocked):
        running, product = carried
        shrink_part, fresh_part = blocked
        return (
            (shrink_part[..., None] * running + fresh_part, product * shrink_part),
            (running, product),
        )

    initial = (
        jnp.zeros((head_count, HEAD, HEAD), jnp.float32),
        jnp.ones((head_count, HEAD), jnp.float32),
    )
    (local_state, device_decay), (start_state, start_decay) = lax.scan(
        advance, initial, (shrink, fresh)
    )

    incoming = entering(device_decay, local_state, "seq")
    block_state = start_state + start_decay[..., None] * incoming[None]
    carried_out = jnp.einsum("nihc,nhcd->nihd", query_tilde, block_state, precision=HIGH)
    mixer_out = (inner_out + surviving[:, :, None, None] * carried_out).reshape(
        tok_rows, head_count, HEAD
    )
    rescale = lax.rsqrt(jnp.mean(mixer_out * mixer_out, axis=-1, keepdims=True) + EPS)
    gate_heads = jax.nn.silu(gate_logit.reshape(tok_rows, head_count, HEAD))
    mixed_rows = (
        (mixer_out * rescale * gate_heads).reshape(tok_rows, head_count * HEAD).astype(jnp.bfloat16)
    )
    collected = []
    for request in range(REQS):
        local_end = end_rows[request] - 1 - first_row
        inside = (local_end >= 0) & (local_end < tok_rows)
        end_row = jnp.clip(local_end, 0, tok_rows - 1)
        block_index = end_row // GROUP
        within = end_row % GROUP
        decay_block = lax.dynamic_index_in_dim(cum_decay, block_index, 0, keepdims=False)
        key_block = lax.dynamic_index_in_dim(key_tilde, block_index, 0, keepdims=False)
        value_block = lax.dynamic_index_in_dim(value_parts, block_index, 0, keepdims=False)
        segment_block = lax.dynamic_index_in_dim(segment_parts, block_index, 0, keepdims=False)
        alive_block = lax.dynamic_index_in_dim(surviving, block_index, 0, keepdims=False)
        state_block = lax.dynamic_index_in_dim(block_state, block_index, 0, keepdims=False)
        decay_end = lax.dynamic_index_in_dim(decay_block, within, 0, keepdims=False)
        segment_end = lax.dynamic_index_in_dim(segment_block, within, 0, keepdims=False)
        alive_end = lax.dynamic_index_in_dim(alive_block, within, 0, keepdims=False)
        upto_mask = ((offsets <= within) & (segment_block == segment_end)).astype(jnp.float32)
        partial_end = jnp.einsum(
            "jhc,jhd->hcd", key_block * upto_mask[:, None, None], value_block, precision=HIGH
        )
        end_state = jnp.exp(decay_end)[..., None] * (alive_end * state_block + partial_end)
        collected.append(jnp.where(inside, end_state, 0.0))
    end_states = jnp.stack(collected)
    handed_state = route_states(end_states, end_rows, owners, tok_rows, "seq")
    partial_terms = project(mixed_rows, output_weight)
    residual = (hidden_in.astype(jnp.float32) + narrow_sum(partial_terms)).astype(jnp.bfloat16)
    widened = widen_rows(residual)
    normed_ffn = rms_rows(widened, swiglu_gain)
    hidden = (
        jax.nn.silu(project(normed_ffn, swiglu_gate)) * project(normed_ffn, swiglu_up)
    ).astype(jnp.bfloat16)
    hidden_out = (residual.astype(jnp.float32) + narrow_sum(project(hidden, swiglu_down))).astype(
        jnp.bfloat16
    )
    return (hidden_out, handed_state)


def solution(mesh):
    in_specs = (
        P("seq", "wa"),
        P(),
        P(),
        P(),
        P(None, "wa"),
        P(None, "wa"),
        P(None, "wa"),
        P(None, "wa"),
        P("wa"),
        P("wa", None),
        P(),
        P(None, "wa"),
        P(None, "wa"),
        P("wa", None),
    )
    out_specs = (P("seq", "wa"), P("seq", "wa", None, None))
    return jax.shard_map(local, mesh=mesh, in_specs=in_specs, out_specs=out_specs, check_vma=False)
```

```python
import jax
import jax.numpy as jnp
from jax import lax
from jax.sharding import PartitionSpec as P

HEAD = 128
GROUP = 64
REQS = 4


EPS = 1e-06
HIGH = lax.Precision.HIGHEST


def entering(decay, state, axis):
    count, mine = (lax.axis_size(axis), lax.axis_index(axis))
    rows = state.shape[1]

    def pack(d, s):
        return jnp.concatenate([s, d[:, None, :]], axis=1)

    window = 1
    while 2 * window < count - 1:
        pairs = [(i, i + window) for i in range(count - window)]
        got = lax.ppermute(pack(decay, state), axis, pairs)
        has = mine >= window
        state = jnp.where(has, decay[..., None] * got[:, :rows] + state, state)
        decay = jnp.where(has, got[:, rows] * decay, decay)
        window *= 2
    near = lax.ppermute(pack(decay, state), axis, [(i, i + 1) for i in range(count - 1)])
    far = lax.ppermute(state, axis, [(i, i + 1 + window) for i in range(count - 1 - window)])
    reach = mine >= 1 + window
    return near[:, :rows] + jnp.where(reach, near[:, rows][..., None] * far, 0.0)


def route_states(end_states, end_rows, owners, tok_rows, axis):
    count, mine = (lax.axis_size(axis), lax.axis_index(axis))
    moved = end_states.astype(jnp.bfloat16)
    left = [(i, (i - 1) % count) for i in range(count)]
    first = lax.ppermute(moved[0], axis, left)
    last = lax.ppermute(moved[-1], axis, [(count - 1, count // 2 - 1)])
    middle = moved[1:-1]
    place = ((end_rows - 1) // tok_rows)[1:-1]
    offset = (owners[1:-1] - place) % count
    for bit in range((count - 1).bit_length()):
        stride = 1 << bit
        moving = ((offset >> bit) & 1) == 1
        go = (moving & (place == mine))[:, None, None, None]
        sent = jnp.where(go, middle, jnp.zeros_like(middle))
        got = lax.ppermute(sent, axis, [(i, (i + stride) % count) for i in range(count)])
        middle = jnp.where(go, jnp.zeros_like(middle), middle) + got
        place = jnp.where(moving, (place + stride) % count, place)
    zero = jnp.zeros_like(first)
    held = jnp.where(owners[0] == mine, first, zero) + jnp.where(owners[-1] == mine, last, zero)
    held = held + jnp.sum(middle, axis=0)
    return held.astype(jnp.float32)[None]


def rms_rows(matrix, scaling):
    matrix = matrix.astype(jnp.float32)
    rescale = lax.rsqrt(jnp.mean(matrix * matrix, axis=-1, keepdims=True) + EPS)
    return (matrix * rescale * scaling).astype(jnp.bfloat16)


def project(matrix, weight):
    return jnp.dot(matrix, weight, preferred_element_type=jnp.float32)


def widen_rows(shard_part):
    return lax.all_gather(shard_part, "wa", axis=1, tiled=True)


def narrow_sum(partial_terms):
    rows, cols = partial_terms.shape
    count = lax.axis_size("wa")
    pieces = partial_terms.astype(jnp.bfloat16).reshape(rows, count, cols // count)
    got = lax.all_to_all(pieces, "wa", 1, 1)
    return jnp.sum(got.astype(jnp.float32), axis=1)


def local(
    hidden_in,
    request_spans,
    owners,
    mixer_gain,
    query_weight,
    forget_weight,
    input_weight,
    gate_weight,
    forget_bias,
    output_weight,
    swiglu_gain,
    swiglu_gate,
    swiglu_up,
    swiglu_down,
):
    tok_rows = hidden_in.shape[0]
    head_count = query_weight.shape[1] // HEAD
    block_count = tok_rows // GROUP
    gathered = widen_rows(hidden_in)
    normed = rms_rows(gathered, mixer_gain)
    queries = jax.nn.silu(project(normed, query_weight))
    forget_logit = project(normed, forget_weight) + forget_bias
    log_decay = jax.nn.log_sigmoid(forget_logit)
    key_rows = jax.nn.sigmoid(-forget_logit)
    value_rows = project(normed, input_weight)
    gate_logit = project(normed, gate_weight)
    first_row = lax.axis_index("seq") * tok_rows
    position = first_row + jnp.arange(tok_rows, dtype=jnp.int32)
    start_rows = request_spans[:, 0]
    end_rows = request_spans[:, 1]
    is_start = jnp.any(position[:, None] == start_rows[None, :], axis=1)
    segment = jnp.sum((start_rows[None, :] <= position[:, None]).astype(jnp.int32), axis=1) - 1
    shape_four = (block_count, GROUP, head_count, HEAD)
    query_parts = queries.reshape(shape_four)
    key_parts = key_rows.reshape(shape_four)
    value_parts = value_rows.reshape(shape_four)
    segment_parts = segment.reshape(block_count, GROUP)
    keep_mask = (1.0 - is_start.astype(jnp.float32)).reshape(block_count, GROUP)
    cum_decay = jnp.cumsum(log_decay.reshape(shape_four), axis=1)
    surviving = jnp.cumprod(keep_mask, axis=1)
    query_tilde = query_parts * jnp.exp(cum_decay)
    key_tilde = key_parts * jnp.exp(-cum_decay)
    offsets = jnp.arange(GROUP, dtype=jnp.int32)
    causal = offsets[:, None] >= offsets[None, :]
    same_doc = causal[None] & (segment_parts[:, :, None] == segment_parts[:, None, :])
    scores = jnp.einsum("nihc,njhc->nhij", query_tilde, key_tilde, precision=HIGH)
    scores = jnp.where(same_doc[:, None], scores, 0.0)
    inner_out = jnp.einsum("nhij,njhd->nihd", scores, value_parts, precision=HIGH)
    tail_mask = (segment_parts == segment_parts[:, -1:]).astype(jnp.float32)
    last_decay = jnp.exp(cum_decay[:, -1])
    fresh = last_decay[..., None] * jnp.einsum(
        "njhc,njhd->nhcd", key_tilde * tail_mask[:, :, None, None], value_parts, precision=HIGH
    )
    shrink = surviving[:, -1][:, None, None] * last_decay

    def advance(carried, blocked):
        running, product = carried
        shrink_part, fresh_part = blocked
        return (
            (shrink_part[..., None] * running + fresh_part, product * shrink_part),
            (running, product),
        )

    initial = (
        jnp.zeros((head_count, HEAD, HEAD), jnp.float32),
        jnp.ones((head_count, HEAD), jnp.float32),
    )
    (local_state, device_decay), (start_state, start_decay) = lax.scan(
        advance, initial, (shrink, fresh), unroll=True
    )

    incoming = entering(device_decay, local_state, "seq")
    block_state = start_state + start_decay[..., None] * incoming[None]
    carried_out = jnp.einsum("nihc,nhcd->nihd", query_tilde, block_state, precision=HIGH)
    mixer_out = (inner_out + surviving[:, :, None, None] * carried_out).reshape(
        tok_rows, head_count, HEAD
    )
    rescale = lax.rsqrt(jnp.mean(mixer_out * mixer_out, axis=-1, keepdims=True) + EPS)
    gate_heads = jax.nn.silu(gate_logit.reshape(tok_rows, head_count, HEAD))
    mixed_rows = (
        (mixer_out * rescale * gate_heads).reshape(tok_rows, head_count * HEAD).astype(jnp.bfloat16)
    )
    collected = []
    for request in range(REQS):
        local_end = end_rows[request] - 1 - first_row
        inside = (local_end >= 0) & (local_end < tok_rows)
        end_row = jnp.clip(local_end, 0, tok_rows - 1)
        block_index = end_row // GROUP
        within = end_row % GROUP
        decay_block = lax.dynamic_index_in_dim(cum_decay, block_index, 0, keepdims=False)
        key_block = lax.dynamic_index_in_dim(key_tilde, block_index, 0, keepdims=False)
        value_block = lax.dynamic_index_in_dim(value_parts, block_index, 0, keepdims=False)
        segment_block = lax.dynamic_index_in_dim(segment_parts, block_index, 0, keepdims=False)
        alive_block = lax.dynamic_index_in_dim(surviving, block_index, 0, keepdims=False)
        state_block = lax.dynamic_index_in_dim(block_state, block_index, 0, keepdims=False)
        decay_end = lax.dynamic_index_in_dim(decay_block, within, 0, keepdims=False)
        segment_end = lax.dynamic_index_in_dim(segment_block, within, 0, keepdims=False)
        alive_end = lax.dynamic_index_in_dim(alive_block, within, 0, keepdims=False)
        upto_mask = ((offsets <= within) & (segment_block == segment_end)).astype(jnp.float32)
        partial_end = jnp.einsum(
            "jhc,jhd->hcd", key_block * upto_mask[:, None, None], value_block, precision=HIGH
        )
        end_state = jnp.exp(decay_end)[..., None] * (alive_end * state_block + partial_end)
        collected.append(jnp.where(inside, end_state, 0.0))
    end_states = jnp.stack(collected)
    end_states, mixed_rows = lax.optimization_barrier((end_states, mixed_rows))
    partial_terms = project(mixed_rows, output_weight)
    handed_state = route_states(end_states, end_rows, owners, tok_rows, "seq")
    residual = (hidden_in.astype(jnp.float32) + narrow_sum(partial_terms)).astype(jnp.bfloat16)
    widened = widen_rows(residual)
    normed_ffn = rms_rows(widened, swiglu_gain)
    hidden = (
        jax.nn.silu(project(normed_ffn, swiglu_gate)) * project(normed_ffn, swiglu_up)
    ).astype(jnp.bfloat16)
    hidden_out = (residual.astype(jnp.float32) + narrow_sum(project(hidden, swiglu_down))).astype(
        jnp.bfloat16
    )
    return (hidden_out, handed_state)


def solution(mesh):
    in_specs = (
        P("seq", "wa"),
        P(),
        P(),
        P(),
        P(None, "wa"),
        P(None, "wa"),
        P(None, "wa"),
        P(None, "wa"),
        P("wa"),
        P("wa", None),
        P(),
        P(None, "wa"),
        P(None, "wa"),
        P("wa", None),
    )
    out_specs = (P("seq", "wa"), P("seq", "wa", None, None))
    return jax.shard_map(local, mesh=mesh, in_specs=in_specs, out_specs=out_specs, check_vma=False)
```

```python
import jax
import jax.numpy as jnp
from jax import lax
from jax.sharding import PartitionSpec as P

HEAD = 128
GROUP = 64
REQS = 4


EPS = 1e-06
HIGH = lax.Precision.HIGH


def entering(decay, state, axis):
    count, mine = (lax.axis_size(axis), lax.axis_index(axis))
    rows = state.shape[1]

    def pack(d, s):
        return jnp.concatenate([s, d[:, None, :]], axis=1)

    window = 1
    while 2 * window < count - 1:
        sent = pack(decay, state)
        fresh_decay, fresh_state = decay, state
        for hop in range(1, 4):
            shift = hop * window
            if shift >= count:
                break
            got = lax.ppermute(sent, axis, [(i, i + shift) for i in range(count - shift)])
            has = mine >= shift
            fresh_state = jnp.where(has, fresh_decay[..., None] * got[:, :rows] + fresh_state, fresh_state)
            fresh_decay = jnp.where(has, got[:, rows] * fresh_decay, fresh_decay)
        decay, state = fresh_decay, fresh_state
        window *= 4
    near = lax.ppermute(pack(decay, state), axis, [(i, i + 1) for i in range(count - 1)])
    far = lax.ppermute(state, axis, [(i, i + 1 + window) for i in range(count - 1 - window)])
    reach = mine >= 1 + window
    return near[:, :rows] + jnp.where(reach, near[:, rows][..., None] * far, 0.0)


def route_states(end_states, end_rows, owners, tok_rows, axis):
    count, mine = (lax.axis_size(axis), lax.axis_index(axis))
    moved = end_states.astype(jnp.bfloat16)
    left = [(i, (i - 1) % count) for i in range(count)]
    first = lax.ppermute(moved[0], axis, left)
    last = lax.ppermute(moved[-1], axis, [(count - 1, count // 2 - 1)])
    middle = moved[1:-1]
    place = ((end_rows - 1) // tok_rows)[1:-1]
    offset = (owners[1:-1] - place) % count
    base = 1
    while base < count:
        digit = (offset // base) % 4
        holder = place == mine
        stays = jnp.where((holder & (digit != 0))[:, None, None, None], jnp.zeros_like(middle), middle)
        for hop in range(1, 4):
            shift = hop * base
            if shift >= count:
                break
            go = (holder & (digit == hop))[:, None, None, None]
            sent = jnp.where(go, middle, jnp.zeros_like(middle))
            stays = stays + lax.ppermute(sent, axis, [(i, (i + shift) % count) for i in range(count)])
        middle = stays
        place = (place + digit * base) % count
        base *= 4
    zero = jnp.zeros_like(first)
    held = jnp.where(owners[0] == mine, first, zero) + jnp.where(owners[-1] == mine, last, zero)
    held = held + jnp.sum(middle, axis=0)
    return held.astype(jnp.float32)[None]


def rms_rows(matrix, scaling):
    matrix = matrix.astype(jnp.float32)
    rescale = lax.rsqrt(jnp.mean(matrix * matrix, axis=-1, keepdims=True) + EPS)
    return (matrix * rescale * scaling).astype(jnp.bfloat16)


def project(matrix, weight):
    return jnp.dot(matrix, weight, preferred_element_type=jnp.float32)


def widen_rows(shard_part):
    return lax.all_gather(shard_part, "wa", axis=1, tiled=True)


def narrow_sum(partial_terms):
    rows, cols = partial_terms.shape
    count = lax.axis_size("wa")
    pieces = partial_terms.astype(jnp.bfloat16).reshape(rows, count, cols // count)
    got = lax.all_to_all(pieces, "wa", 1, 1)
    return jnp.sum(got.astype(jnp.float32), axis=1)


def local(
    hidden_in,
    request_spans,
    owners,
    mixer_gain,
    query_weight,
    forget_weight,
    input_weight,
    gate_weight,
    forget_bias,
    output_weight,
    swiglu_gain,
    swiglu_gate,
    swiglu_up,
    swiglu_down,
):
    tok_rows = hidden_in.shape[0]
    head_count = query_weight.shape[1] // HEAD
    block_count = tok_rows // GROUP
    gathered = widen_rows(hidden_in)
    normed = rms_rows(gathered, mixer_gain)
    queries = jax.nn.silu(project(normed, query_weight))
    forget_logit = project(normed, forget_weight) + forget_bias
    log_decay = jax.nn.log_sigmoid(forget_logit)
    key_rows = jax.nn.sigmoid(-forget_logit)
    value_rows = project(normed, input_weight)
    gate_logit = project(normed, gate_weight)
    first_row = lax.axis_index("seq") * tok_rows
    position = first_row + jnp.arange(tok_rows, dtype=jnp.int32)
    start_rows = request_spans[:, 0]
    end_rows = request_spans[:, 1]
    is_start = jnp.any(position[:, None] == start_rows[None, :], axis=1)
    segment = jnp.sum((start_rows[None, :] <= position[:, None]).astype(jnp.int32), axis=1) - 1
    shape_four = (block_count, GROUP, head_count, HEAD)
    query_parts = queries.reshape(shape_four)
    key_parts = key_rows.reshape(shape_four)
    value_parts = value_rows.reshape(shape_four)
    segment_parts = segment.reshape(block_count, GROUP)
    keep_mask = (1.0 - is_start.astype(jnp.float32)).reshape(block_count, GROUP)
    cum_decay = jnp.cumsum(log_decay.reshape(shape_four), axis=1)
    surviving = jnp.cumprod(keep_mask, axis=1)
    query_tilde = query_parts * jnp.exp(cum_decay)
    key_tilde = key_parts * jnp.exp(-cum_decay)
    offsets = jnp.arange(GROUP, dtype=jnp.int32)
    causal = offsets[:, None] >= offsets[None, :]
    same_doc = causal[None] & (segment_parts[:, :, None] == segment_parts[:, None, :])
    scores = jnp.einsum("nihc,njhc->nhij", query_tilde, key_tilde, precision=HIGH)
    scores = jnp.where(same_doc[:, None], scores, 0.0)
    inner_out = jnp.einsum("nhij,njhd->nihd", scores, value_parts, precision=HIGH)
    tail_mask = (segment_parts == segment_parts[:, -1:]).astype(jnp.float32)
    last_decay = jnp.exp(cum_decay[:, -1])
    fresh = last_decay[..., None] * jnp.einsum(
        "njhc,njhd->nhcd", key_tilde * tail_mask[:, :, None, None], value_parts, precision=HIGH
    )
    shrink = surviving[:, -1][:, None, None] * last_decay

    def advance(carried, blocked):
        running, product = carried
        shrink_part, fresh_part = blocked
        return (
            (shrink_part[..., None] * running + fresh_part, product * shrink_part),
            (running, product),
        )

    initial = (
        jnp.zeros((head_count, HEAD, HEAD), jnp.float32),
        jnp.ones((head_count, HEAD), jnp.float32),
    )
    (local_state, device_decay), (start_state, start_decay) = lax.scan(
        advance, initial, (shrink, fresh), unroll=True
    )

    incoming = entering(device_decay, local_state, "seq")
    block_state = start_state + start_decay[..., None] * incoming[None]
    carried_out = jnp.einsum("nihc,nhcd->nihd", query_tilde, block_state, precision=HIGH)
    mixer_out = (inner_out + surviving[:, :, None, None] * carried_out).reshape(
        tok_rows, head_count, HEAD
    )
    rescale = lax.rsqrt(jnp.mean(mixer_out * mixer_out, axis=-1, keepdims=True) + EPS)
    gate_heads = jax.nn.silu(gate_logit.reshape(tok_rows, head_count, HEAD))
    mixed_rows = (
        (mixer_out * rescale * gate_heads).reshape(tok_rows, head_count * HEAD).astype(jnp.bfloat16)
    )
    collected = []
    for request in range(REQS):
        local_end = end_rows[request] - 1 - first_row
        inside = (local_end >= 0) & (local_end < tok_rows)
        end_row = jnp.clip(local_end, 0, tok_rows - 1)
        block_index = end_row // GROUP
        within = end_row % GROUP
        decay_block = lax.dynamic_index_in_dim(cum_decay, block_index, 0, keepdims=False)
        key_block = lax.dynamic_index_in_dim(key_tilde, block_index, 0, keepdims=False)
        value_block = lax.dynamic_index_in_dim(value_parts, block_index, 0, keepdims=False)
        segment_block = lax.dynamic_index_in_dim(segment_parts, block_index, 0, keepdims=False)
        alive_block = lax.dynamic_index_in_dim(surviving, block_index, 0, keepdims=False)
        state_block = lax.dynamic_index_in_dim(block_state, block_index, 0, keepdims=False)
        decay_end = lax.dynamic_index_in_dim(decay_block, within, 0, keepdims=False)
        segment_end = lax.dynamic_index_in_dim(segment_block, within, 0, keepdims=False)
        alive_end = lax.dynamic_index_in_dim(alive_block, within, 0, keepdims=False)
        upto_mask = ((offsets <= within) & (segment_block == segment_end)).astype(jnp.float32)
        partial_end = jnp.einsum(
            "jhc,jhd->hcd", key_block * upto_mask[:, None, None], value_block, precision=HIGH
        )
        end_state = jnp.exp(decay_end)[..., None] * (alive_end * state_block + partial_end)
        collected.append(jnp.where(inside, end_state, 0.0))
    end_states = jnp.stack(collected)
    end_states, mixed_rows = lax.optimization_barrier((end_states, mixed_rows))
    partial_terms = project(mixed_rows, output_weight)
    handed_state = route_states(end_states, end_rows, owners, tok_rows, "seq")
    residual = (hidden_in.astype(jnp.float32) + narrow_sum(partial_terms)).astype(jnp.bfloat16)
    widened = widen_rows(residual)
    normed_ffn = rms_rows(widened, swiglu_gain)
    hidden = (
        jax.nn.silu(project(normed_ffn, swiglu_gate)) * project(normed_ffn, swiglu_up)
    ).astype(jnp.bfloat16)
    hidden_out = (residual.astype(jnp.float32) + narrow_sum(project(hidden, swiglu_down))).astype(
        jnp.bfloat16
    )
    return (hidden_out, handed_state)


def solution(mesh):
    in_specs = (
        P("seq", "wa"),
        P(),
        P(),
        P(),
        P(None, "wa"),
        P(None, "wa"),
        P(None, "wa"),
        P(None, "wa"),
        P("wa"),
        P("wa", None),
        P(),
        P(None, "wa"),
        P(None, "wa"),
        P("wa", None),
    )
    out_specs = (P("seq", "wa"), P("seq", "wa", None, None))
    return jax.shard_map(local, mesh=mesh, in_specs=in_specs, out_specs=out_specs, check_vma=False)
```

```python
import jax
import jax.numpy as jnp
from jax import lax
from jax.sharding import PartitionSpec as P

HEAD = 128
GROUP = 64
REQS = 4


EPS = 1e-06
HIGH = lax.Precision.HIGH


def entering(decay, state, axis):
    count, mine = (lax.axis_size(axis), lax.axis_index(axis))
    rows = state.shape[1]
    high = decay.astype(jnp.bfloat16)
    low = (decay - high.astype(jnp.float32)).astype(jnp.bfloat16)
    packed = jnp.concatenate([state.astype(jnp.bfloat16), high[:, None, :], low[:, None, :]], axis=1)
    every = lax.all_gather(packed, axis)
    decays = every[:, :, rows].astype(jnp.float32) + every[:, :, rows + 1].astype(jnp.float32)
    ranks = jnp.arange(count, dtype=jnp.int32)
    between = (ranks[None, :] > ranks[:, None]) & (ranks[None, :] < mine)
    weights = jnp.prod(jnp.where(between[:, :, None, None], decays[None], 1.0), axis=1)
    weights = jnp.where((ranks < mine)[:, None, None], weights, 0.0)
    return jnp.sum(weights[..., None] * every[:, :, :rows].astype(jnp.float32), axis=0)


def route_states(end_states, end_rows, owners, tok_rows, axis):
    count, mine = (lax.axis_size(axis), lax.axis_index(axis))
    moved = end_states.astype(jnp.bfloat16)
    left = [(i, (i - 1) % count) for i in range(count)]
    first = lax.ppermute(moved[0], axis, left)
    last = lax.ppermute(moved[-1], axis, [(count - 1, count // 2 - 1)])
    middle = moved[1:-1]
    place = ((end_rows - 1) // tok_rows)[1:-1]
    offset = (owners[1:-1] - place) % count
    base = 1
    while base < count:
        digit = (offset // base) % 4
        holder = place == mine
        stays = jnp.where((holder & (digit != 0))[:, None, None, None], jnp.zeros_like(middle), middle)
        for hop in range(1, 4):
            shift = hop * base
            if shift >= count:
                break
            go = (holder & (digit == hop))[:, None, None, None]
            sent = jnp.where(go, middle, jnp.zeros_like(middle))
            stays = stays + lax.ppermute(sent, axis, [(i, (i + shift) % count) for i in range(count)])
        middle = stays
        place = (place + digit * base) % count
        base *= 4
    zero = jnp.zeros_like(first)
    held = jnp.where(owners[0] == mine, first, zero) + jnp.where(owners[-1] == mine, last, zero)
    held = held + jnp.sum(middle, axis=0)
    return held.astype(jnp.float32)[None]


def rms_rows(matrix, scaling):
    matrix = matrix.astype(jnp.float32)
    rescale = lax.rsqrt(jnp.mean(matrix * matrix, axis=-1, keepdims=True) + EPS)
    return (matrix * rescale * scaling).astype(jnp.bfloat16)


def project(matrix, weight):
    return jnp.dot(matrix, weight, preferred_element_type=jnp.float32)


def widen_rows(shard_part):
    return lax.all_gather(shard_part, "wa", axis=1, tiled=True)


def narrow_sum(partial_terms):
    rows, cols = partial_terms.shape
    count = lax.axis_size("wa")
    pieces = partial_terms.astype(jnp.bfloat16).reshape(rows, count, cols // count)
    got = lax.all_to_all(pieces, "wa", 1, 1)
    return jnp.sum(got.astype(jnp.float32), axis=1)


def local(
    hidden_in,
    request_spans,
    owners,
    mixer_gain,
    query_weight,
    forget_weight,
    input_weight,
    gate_weight,
    forget_bias,
    output_weight,
    swiglu_gain,
    swiglu_gate,
    swiglu_up,
    swiglu_down,
):
    tok_rows = hidden_in.shape[0]
    head_count = query_weight.shape[1] // HEAD
    block_count = tok_rows // GROUP
    half = tok_rows // 2
    first_half = widen_rows(hidden_in[:half])
    first_half, second_in = lax.optimization_barrier((first_half, hidden_in[half:]))
    halves = (rms_rows(first_half, mixer_gain), rms_rows(widen_rows(second_in), mixer_gain))

    def both(weight):
        return jnp.concatenate([project(part, weight) for part in halves], axis=0)

    queries = jax.nn.silu(both(query_weight))
    forget_logit = both(forget_weight) + forget_bias
    log_decay = jax.nn.log_sigmoid(forget_logit)
    key_rows = jax.nn.sigmoid(-forget_logit)
    value_rows = both(input_weight)
    gate_logit = both(gate_weight)
    first_row = lax.axis_index("seq") * tok_rows
    position = first_row + jnp.arange(tok_rows, dtype=jnp.int32)
    start_rows = request_spans[:, 0]
    end_rows = request_spans[:, 1]
    is_start = jnp.any(position[:, None] == start_rows[None, :], axis=1)
    segment = jnp.sum((start_rows[None, :] <= position[:, None]).astype(jnp.int32), axis=1) - 1
    shape_four = (block_count, GROUP, head_count, HEAD)
    query_parts = queries.reshape(shape_four)
    key_parts = key_rows.reshape(shape_four)
    value_parts = value_rows.reshape(shape_four)
    segment_parts = segment.reshape(block_count, GROUP)
    keep_mask = (1.0 - is_start.astype(jnp.float32)).reshape(block_count, GROUP)
    cum_decay = jnp.cumsum(log_decay.reshape(shape_four), axis=1)
    surviving = jnp.cumprod(keep_mask, axis=1)
    query_tilde = query_parts * jnp.exp(cum_decay)
    key_tilde = key_parts * jnp.exp(-cum_decay)
    offsets = jnp.arange(GROUP, dtype=jnp.int32)
    causal = offsets[:, None] >= offsets[None, :]
    same_doc = causal[None] & (segment_parts[:, :, None] == segment_parts[:, None, :])
    scores = jnp.einsum("nihc,njhc->nhij", query_tilde, key_tilde, precision=HIGH)
    scores = jnp.where(same_doc[:, None], scores, 0.0)
    inner_out = jnp.einsum("nhij,njhd->nihd", scores, value_parts, precision=HIGH)
    tail_mask = (segment_parts == segment_parts[:, -1:]).astype(jnp.float32)
    last_decay = jnp.exp(cum_decay[:, -1])
    fresh = last_decay[..., None] * jnp.einsum(
        "njhc,njhd->nhcd", key_tilde * tail_mask[:, :, None, None], value_parts, precision=HIGH
    )
    shrink = surviving[:, -1][:, None, None] * last_decay

    def advance(carried, blocked):
        running, product = carried
        shrink_part, fresh_part = blocked
        return (
            (shrink_part[..., None] * running + fresh_part, product * shrink_part),
            (running, product),
        )

    initial = (
        jnp.zeros((head_count, HEAD, HEAD), jnp.float32),
        jnp.ones((head_count, HEAD), jnp.float32),
    )
    (local_state, device_decay), (start_state, start_decay) = lax.scan(
        advance, initial, (shrink, fresh), unroll=True
    )

    incoming = entering(device_decay, local_state, "seq")
    block_state = start_state + start_decay[..., None] * incoming[None]
    carried_out = jnp.einsum("nihc,nhcd->nihd", query_tilde, block_state, precision=HIGH)
    mixer_out = (inner_out + surviving[:, :, None, None] * carried_out).reshape(
        tok_rows, head_count, HEAD
    )
    rescale = lax.rsqrt(jnp.mean(mixer_out * mixer_out, axis=-1, keepdims=True) + EPS)
    gate_heads = jax.nn.silu(gate_logit.reshape(tok_rows, head_count, HEAD))
    mixed_rows = (
        (mixer_out * rescale * gate_heads).reshape(tok_rows, head_count * HEAD).astype(jnp.bfloat16)
    )
    collected = []
    for request in range(REQS):
        local_end = end_rows[request] - 1 - first_row
        inside = (local_end >= 0) & (local_end < tok_rows)
        end_row = jnp.clip(local_end, 0, tok_rows - 1)
        block_index = end_row // GROUP
        within = end_row % GROUP
        decay_block = lax.dynamic_index_in_dim(cum_decay, block_index, 0, keepdims=False)
        key_block = lax.dynamic_index_in_dim(key_tilde, block_index, 0, keepdims=False)
        value_block = lax.dynamic_index_in_dim(value_parts, block_index, 0, keepdims=False)
        segment_block = lax.dynamic_index_in_dim(segment_parts, block_index, 0, keepdims=False)
        alive_block = lax.dynamic_index_in_dim(surviving, block_index, 0, keepdims=False)
        state_block = lax.dynamic_index_in_dim(block_state, block_index, 0, keepdims=False)
        decay_end = lax.dynamic_index_in_dim(decay_block, within, 0, keepdims=False)
        segment_end = lax.dynamic_index_in_dim(segment_block, within, 0, keepdims=False)
        alive_end = lax.dynamic_index_in_dim(alive_block, within, 0, keepdims=False)
        upto_mask = ((offsets <= within) & (segment_block == segment_end)).astype(jnp.float32)
        partial_end = jnp.einsum(
            "jhc,jhd->hcd", key_block * upto_mask[:, None, None], value_block, precision=HIGH
        )
        end_state = jnp.exp(decay_end)[..., None] * (alive_end * state_block + partial_end)
        collected.append(jnp.where(inside, end_state, 0.0))
    end_states = jnp.stack(collected)
    end_states, mixed_rows = lax.optimization_barrier((end_states, mixed_rows))
    partial_terms = project(mixed_rows, output_weight)
    handed_state = route_states(end_states, end_rows, owners, tok_rows, "seq")
    residual = (hidden_in.astype(jnp.float32) + narrow_sum(partial_terms)).astype(jnp.bfloat16)
    widened = widen_rows(residual)
    normed_ffn = rms_rows(widened, swiglu_gain)
    hidden = (
        jax.nn.silu(project(normed_ffn, swiglu_gate)) * project(normed_ffn, swiglu_up)
    ).astype(jnp.bfloat16)
    hidden_out = (residual.astype(jnp.float32) + narrow_sum(project(hidden, swiglu_down))).astype(
        jnp.bfloat16
    )
    return (hidden_out, handed_state)


def solution(mesh):
    in_specs = (
        P("seq", "wa"),
        P(),
        P(),
        P(),
        P(None, "wa"),
        P(None, "wa"),
        P(None, "wa"),
        P(None, "wa"),
        P("wa"),
        P("wa", None),
        P(),
        P(None, "wa"),
        P(None, "wa"),
        P("wa", None),
    )
    out_specs = (P("seq", "wa"), P("seq", "wa", None, None))
    return jax.shard_map(local, mesh=mesh, in_specs=in_specs, out_specs=out_specs, check_vma=False)
```

```python
import jax
import jax.numpy as jnp
from jax import lax
from jax.sharding import PartitionSpec as P

HEAD = 128
GROUP = 64
REQS = 4


EPS = 1e-06
HIGH = lax.Precision.HIGH


def hi_lo(values):
    high = values.astype(jnp.bfloat16)
    return high, (values - high.astype(jnp.float32)).astype(jnp.bfloat16)


def entering(decay, state, axis, targets):
    count = lax.axis_size(axis)
    rows = state.shape[1]
    high, low = hi_lo(decay)
    packed = jnp.concatenate([state.astype(jnp.bfloat16), high[:, None, :], low[:, None, :]], axis=1)
    every = lax.all_gather(packed, axis)
    decays = every[:, :, rows].astype(jnp.float32) + every[:, :, rows + 1].astype(jnp.float32)
    states = every[:, :, :rows].astype(jnp.float32)
    ranks = jnp.arange(count, dtype=jnp.int32)
    results = []
    for target in targets:
        between = (ranks[None, :] > ranks[:, None]) & (ranks[None, :] < target)
        weights = jnp.prod(jnp.where(between[:, :, None, None], decays[None], 1.0), axis=1)
        weights = jnp.where((ranks < target)[:, None, None], weights, 0.0)
        results.append(jnp.sum(weights[..., None] * states, axis=0))
    return results


def route_packets(packets, end_rows, owners, tok_rows, axis):
    count, mine = (lax.axis_size(axis), lax.axis_index(axis))
    left = [(i, (i - 1) % count) for i in range(count)]
    first = lax.ppermute(packets[0], axis, left)
    last = lax.ppermute(packets[-1], axis, [(count - 1, count // 2 - 1)])
    middle = packets[1:-1]
    place = ((end_rows - 1) // tok_rows)[1:-1]
    offset = (owners[1:-1] - place) % count
    for bit in range((count - 1).bit_length()):
        stride = 1 << bit
        moving = ((offset >> bit) & 1) == 1
        go = (moving & (place == mine))[:, None, None, None]
        sent = jnp.where(go, middle, jnp.zeros_like(middle))
        got = lax.ppermute(sent, axis, [(i, (i + stride) % count) for i in range(count)])
        middle = jnp.where(go, jnp.zeros_like(middle), middle) + got
        place = jnp.where(moving, (place + stride) % count, place)
    zero = jnp.zeros_like(first)
    held = jnp.where(owners[0] == mine, first, zero) + jnp.where(owners[-1] == mine, last, zero)
    return held + jnp.sum(middle, axis=0)


def rms_rows(matrix, scaling):
    matrix = matrix.astype(jnp.float32)
    rescale = lax.rsqrt(jnp.mean(matrix * matrix, axis=-1, keepdims=True) + EPS)
    return (matrix * rescale * scaling).astype(jnp.bfloat16)


def project(matrix, weight):
    return jnp.dot(matrix, weight, preferred_element_type=jnp.float32)


def widen_rows(shard_part):
    return lax.all_gather(shard_part, "wa", axis=1, tiled=True)


def narrow_sum(partial_terms):
    rows, cols = partial_terms.shape
    count = lax.axis_size("wa")
    pieces = partial_terms.astype(jnp.bfloat16).reshape(rows, count, cols // count)
    got = lax.all_to_all(pieces, "wa", 1, 1)
    return jnp.sum(got.astype(jnp.float32), axis=1)


def local(
    hidden_in,
    request_spans,
    owners,
    mixer_gain,
    query_weight,
    forget_weight,
    input_weight,
    gate_weight,
    forget_bias,
    output_weight,
    swiglu_gain,
    swiglu_gate,
    swiglu_up,
    swiglu_down,
):
    tok_rows = hidden_in.shape[0]
    head_count = query_weight.shape[1] // HEAD
    block_count = tok_rows // GROUP
    gathered = widen_rows(hidden_in)
    normed = rms_rows(gathered, mixer_gain)
    queries = jax.nn.silu(project(normed, query_weight))
    forget_logit = project(normed, forget_weight) + forget_bias
    log_decay = jax.nn.log_sigmoid(forget_logit)
    key_rows = jax.nn.sigmoid(-forget_logit)
    value_rows = project(normed, input_weight)
    gate_logit = project(normed, gate_weight)
    first_row = lax.axis_index("seq") * tok_rows
    position = first_row + jnp.arange(tok_rows, dtype=jnp.int32)
    start_rows = request_spans[:, 0]
    end_rows = request_spans[:, 1]
    is_start = jnp.any(position[:, None] == start_rows[None, :], axis=1)
    segment = jnp.sum((start_rows[None, :] <= position[:, None]).astype(jnp.int32), axis=1) - 1
    shape_four = (block_count, GROUP, head_count, HEAD)
    query_parts = queries.reshape(shape_four)
    key_parts = key_rows.reshape(shape_four)
    value_parts = value_rows.reshape(shape_four)
    segment_parts = segment.reshape(block_count, GROUP)
    keep_mask = (1.0 - is_start.astype(jnp.float32)).reshape(block_count, GROUP)
    cum_decay = jnp.cumsum(log_decay.reshape(shape_four), axis=1)
    surviving = jnp.cumprod(keep_mask, axis=1)
    query_tilde = query_parts * jnp.exp(cum_decay)
    key_tilde = key_parts * jnp.exp(-cum_decay)
    offsets = jnp.arange(GROUP, dtype=jnp.int32)
    causal = offsets[:, None] >= offsets[None, :]
    same_doc = causal[None] & (segment_parts[:, :, None] == segment_parts[:, None, :])
    scores = jnp.einsum("nihc,njhc->nhij", query_tilde, key_tilde, precision=HIGH)
    scores = jnp.where(same_doc[:, None], scores, 0.0)
    inner_out = jnp.einsum("nhij,njhd->nihd", scores, value_parts, precision=HIGH)
    tail_mask = (segment_parts == segment_parts[:, -1:]).astype(jnp.float32)
    last_decay = jnp.exp(cum_decay[:, -1])
    fresh = last_decay[..., None] * jnp.einsum(
        "njhc,njhd->nhcd", key_tilde * tail_mask[:, :, None, None], value_parts, precision=HIGH
    )
    shrink = surviving[:, -1][:, None, None] * last_decay

    def advance(carried, blocked):
        running, product = carried
        shrink_part, fresh_part = blocked
        return (
            (shrink_part[..., None] * running + fresh_part, product * shrink_part),
            (running, product),
        )

    initial = (
        jnp.zeros((head_count, HEAD, HEAD), jnp.float32),
        jnp.ones((head_count, HEAD), jnp.float32),
    )
    (local_state, device_decay), (start_state, start_decay) = lax.scan(
        advance, initial, (shrink, fresh), unroll=True
    )

    packets = []
    for request in range(REQS):
        local_end = end_rows[request] - 1 - first_row
        inside = (local_end >= 0) & (local_end < tok_rows)
        end_row = jnp.clip(local_end, 0, tok_rows - 1)
        block_index = end_row // GROUP
        within = end_row % GROUP
        decay_block = lax.dynamic_index_in_dim(cum_decay, block_index, 0, keepdims=False)
        key_block = lax.dynamic_index_in_dim(key_tilde, block_index, 0, keepdims=False)
        value_block = lax.dynamic_index_in_dim(value_parts, block_index, 0, keepdims=False)
        segment_block = lax.dynamic_index_in_dim(segment_parts, block_index, 0, keepdims=False)
        alive_block = lax.dynamic_index_in_dim(surviving, block_index, 0, keepdims=False)
        start_block = lax.dynamic_index_in_dim(start_state, block_index, 0, keepdims=False)
        carry_block = lax.dynamic_index_in_dim(start_decay, block_index, 0, keepdims=False)
        decay_end = lax.dynamic_index_in_dim(decay_block, within, 0, keepdims=False)
        segment_end = lax.dynamic_index_in_dim(segment_block, within, 0, keepdims=False)
        alive_end = lax.dynamic_index_in_dim(alive_block, within, 0, keepdims=False)
        upto_mask = ((offsets <= within) & (segment_block == segment_end)).astype(jnp.float32)
        partial_end = jnp.einsum(
            "jhc,jhd->hcd", key_block * upto_mask[:, None, None], value_block, precision=HIGH
        )
        grow = jnp.exp(decay_end)
        local_part = grow[..., None] * (alive_end * start_block + partial_end)
        high, low = hi_lo(grow * alive_end * carry_block)
        packet = jnp.concatenate(
            [local_part.astype(jnp.bfloat16), high[:, None, :], low[:, None, :]], axis=1
        )
        packets.append(jnp.where(inside, packet, jnp.zeros_like(packet)))
    held = route_packets(jnp.stack(packets), end_rows, owners, tok_rows, "seq")
    mine = lax.axis_index("seq")
    owned_source = jnp.sum(jnp.where(owners == mine, (end_rows - 1) // tok_rows, 0))
    incoming, owned_incoming = entering(device_decay, local_state, "seq", (mine, owned_source))
    held_coeff = held[:, HEAD].astype(jnp.float32) + held[:, HEAD + 1].astype(jnp.float32)
    handed_state = (held[:, :HEAD].astype(jnp.float32) + held_coeff[..., None] * owned_incoming)[None]
    block_state = start_state + start_decay[..., None] * incoming[None]
    carried_out = jnp.einsum("nihc,nhcd->nihd", query_tilde, block_state, precision=HIGH)
    mixer_out = (inner_out + surviving[:, :, None, None] * carried_out).reshape(
        tok_rows, head_count, HEAD
    )
    rescale = lax.rsqrt(jnp.mean(mixer_out * mixer_out, axis=-1, keepdims=True) + EPS)
    gate_heads = jax.nn.silu(gate_logit.reshape(tok_rows, head_count, HEAD))
    mixed_rows = (
        (mixer_out * rescale * gate_heads).reshape(tok_rows, head_count * HEAD).astype(jnp.bfloat16)
    )
    partial_terms = project(mixed_rows, output_weight)
    residual = (hidden_in.astype(jnp.float32) + narrow_sum(partial_terms)).astype(jnp.bfloat16)
    widened = widen_rows(residual)
    normed_ffn = rms_rows(widened, swiglu_gain)
    hidden = (
        jax.nn.silu(project(normed_ffn, swiglu_gate)) * project(normed_ffn, swiglu_up)
    ).astype(jnp.bfloat16)
    hidden_out = (residual.astype(jnp.float32) + narrow_sum(project(hidden, swiglu_down))).astype(
        jnp.bfloat16
    )
    return (hidden_out, handed_state)


def solution(mesh):
    in_specs = (
        P("seq", "wa"),
        P(),
        P(),
        P(),
        P(None, "wa"),
        P(None, "wa"),
        P(None, "wa"),
        P(None, "wa"),
        P("wa"),
        P("wa", None),
        P(),
        P(None, "wa"),
        P(None, "wa"),
        P("wa", None),
    )
    out_specs = (P("seq", "wa"), P("seq", "wa", None, None))
    return jax.shard_map(local, mesh=mesh, in_specs=in_specs, out_specs=out_specs, check_vma=False)
```

```python
import jax
import jax.numpy as jnp
from jax import lax
from jax.sharding import PartitionSpec as P

HEAD = 128
GROUP = 64
REQS = 4


EPS = 1e-06
HIGH = lax.Precision.HIGH


def hi_lo(values):
    high = values.astype(jnp.bfloat16)
    return high, (values - high.astype(jnp.float32)).astype(jnp.bfloat16)


def entering(decay, state, axis, targets, companion):
    count = lax.axis_size(axis)
    rows = state.shape[1]
    high, low = hi_lo(decay)
    packed = jnp.concatenate([state.astype(jnp.bfloat16), high[:, None, :], low[:, None, :]], axis=1)
    every, companion = lax.optimization_barrier((lax.all_gather(packed, axis), companion))
    decays = every[:, :, rows].astype(jnp.float32) + every[:, :, rows + 1].astype(jnp.float32)
    states = every[:, :, :rows].astype(jnp.float32)
    ranks = jnp.arange(count, dtype=jnp.int32)
    results = []
    for target in targets:
        between = (ranks[None, :] > ranks[:, None]) & (ranks[None, :] < target)
        weights = jnp.prod(jnp.where(between[:, :, None, None], decays[None], 1.0), axis=1)
        weights = jnp.where((ranks < target)[:, None, None], weights, 0.0)
        results.append(jnp.sum(weights[..., None] * states, axis=0))
    return results, companion


def route_packets(packets, end_rows, owners, tok_rows, axis):
    count, mine = (lax.axis_size(axis), lax.axis_index(axis))
    left = [(i, (i - 1) % count) for i in range(count)]
    first = lax.ppermute(packets[0], axis, left)
    last = lax.ppermute(packets[-1], axis, [(count - 1, count // 2 - 1)])
    middle = packets[1:-1]
    place = ((end_rows - 1) // tok_rows)[1:-1]
    offset = (owners[1:-1] - place) % count
    for bit in range((count - 1).bit_length()):
        stride = 1 << bit
        moving = ((offset >> bit) & 1) == 1
        go = (moving & (place == mine))[:, None, None, None]
        sent = jnp.where(go, middle, jnp.zeros_like(middle))
        got = lax.ppermute(sent, axis, [(i, (i + stride) % count) for i in range(count)])
        middle = jnp.where(go, jnp.zeros_like(middle), middle) + got
        place = jnp.where(moving, (place + stride) % count, place)
    zero = jnp.zeros_like(first)
    held = jnp.where(owners[0] == mine, first, zero) + jnp.where(owners[-1] == mine, last, zero)
    return held + jnp.sum(middle, axis=0)


def rms_rows(matrix, scaling):
    matrix = matrix.astype(jnp.float32)
    rescale = lax.rsqrt(jnp.mean(matrix * matrix, axis=-1, keepdims=True) + EPS)
    return (matrix * rescale * scaling).astype(jnp.bfloat16)


def project(matrix, weight):
    return jnp.dot(matrix, weight, preferred_element_type=jnp.float32)


def widen_rows(shard_part):
    return lax.all_gather(shard_part, "wa", axis=1, tiled=True)


def narrow_sum(partial_terms):
    rows, cols = partial_terms.shape
    count = lax.axis_size("wa")
    pieces = partial_terms.astype(jnp.bfloat16).reshape(rows, count, cols // count)
    got = lax.all_to_all(pieces, "wa", 1, 1)
    return jnp.sum(got.astype(jnp.float32), axis=1)


def local(
    hidden_in,
    request_spans,
    owners,
    mixer_gain,
    query_weight,
    forget_weight,
    input_weight,
    gate_weight,
    forget_bias,
    output_weight,
    swiglu_gain,
    swiglu_gate,
    swiglu_up,
    swiglu_down,
):
    tok_rows = hidden_in.shape[0]
    head_count = query_weight.shape[1] // HEAD
    block_count = tok_rows // GROUP
    gathered = widen_rows(hidden_in)
    normed = rms_rows(gathered, mixer_gain)
    queries = jax.nn.silu(project(normed, query_weight))
    forget_logit = project(normed, forget_weight) + forget_bias
    log_decay = jax.nn.log_sigmoid(forget_logit)
    key_rows = jax.nn.sigmoid(-forget_logit)
    value_rows = project(normed, input_weight)
    gate_logit = project(normed, gate_weight)
    first_row = lax.axis_index("seq") * tok_rows
    position = first_row + jnp.arange(tok_rows, dtype=jnp.int32)
    start_rows = request_spans[:, 0]
    end_rows = request_spans[:, 1]
    is_start = jnp.any(position[:, None] == start_rows[None, :], axis=1)
    segment = jnp.sum((start_rows[None, :] <= position[:, None]).astype(jnp.int32), axis=1) - 1
    shape_four = (block_count, GROUP, head_count, HEAD)
    query_parts = queries.reshape(shape_four)
    key_parts = key_rows.reshape(shape_four)
    value_parts = value_rows.reshape(shape_four)
    segment_parts = segment.reshape(block_count, GROUP)
    keep_mask = (1.0 - is_start.astype(jnp.float32)).reshape(block_count, GROUP)
    cum_decay = jnp.cumsum(log_decay.reshape(shape_four), axis=1)
    surviving = jnp.cumprod(keep_mask, axis=1)
    query_tilde = query_parts * jnp.exp(cum_decay)
    key_tilde = key_parts * jnp.exp(-cum_decay)
    offsets = jnp.arange(GROUP, dtype=jnp.int32)
    causal = offsets[:, None] >= offsets[None, :]
    same_doc = causal[None] & (segment_parts[:, :, None] == segment_parts[:, None, :])
    scores = jnp.einsum("nihc,njhc->nhij", query_tilde, key_tilde, precision=HIGH)
    scores = jnp.where(same_doc[:, None], scores, 0.0)
    inner_out = jnp.einsum("nhij,njhd->nihd", scores, value_parts, precision=HIGH)
    tail_mask = (segment_parts == segment_parts[:, -1:]).astype(jnp.float32)
    last_decay = jnp.exp(cum_decay[:, -1])
    fresh = last_decay[..., None] * jnp.einsum(
        "njhc,njhd->nhcd", key_tilde * tail_mask[:, :, None, None], value_parts, precision=HIGH
    )
    shrink = surviving[:, -1][:, None, None] * last_decay

    def advance(carried, blocked):
        running, product = carried
        shrink_part, fresh_part = blocked
        return (
            (shrink_part[..., None] * running + fresh_part, product * shrink_part),
            (running, product),
        )

    initial = (
        jnp.zeros((head_count, HEAD, HEAD), jnp.float32),
        jnp.ones((head_count, HEAD), jnp.float32),
    )
    (local_state, device_decay), (start_state, start_decay) = lax.scan(
        advance, initial, (shrink, fresh), unroll=True
    )

    packets = []
    for request in range(REQS):
        local_end = end_rows[request] - 1 - first_row
        inside = (local_end >= 0) & (local_end < tok_rows)
        end_row = jnp.clip(local_end, 0, tok_rows - 1)
        block_index = end_row // GROUP
        within = end_row % GROUP
        decay_block = lax.dynamic_index_in_dim(cum_decay, block_index, 0, keepdims=False)
        key_block = lax.dynamic_index_in_dim(key_tilde, block_index, 0, keepdims=False)
        value_block = lax.dynamic_index_in_dim(value_parts, block_index, 0, keepdims=False)
        segment_block = lax.dynamic_index_in_dim(segment_parts, block_index, 0, keepdims=False)
        alive_block = lax.dynamic_index_in_dim(surviving, block_index, 0, keepdims=False)
        start_block = lax.dynamic_index_in_dim(start_state, block_index, 0, keepdims=False)
        carry_block = lax.dynamic_index_in_dim(start_decay, block_index, 0, keepdims=False)
        decay_end = lax.dynamic_index_in_dim(decay_block, within, 0, keepdims=False)
        segment_end = lax.dynamic_index_in_dim(segment_block, within, 0, keepdims=False)
        alive_end = lax.dynamic_index_in_dim(alive_block, within, 0, keepdims=False)
        upto_mask = ((offsets <= within) & (segment_block == segment_end)).astype(jnp.float32)
        partial_end = jnp.einsum(
            "jhc,jhd->hcd", key_block * upto_mask[:, None, None], value_block, precision=HIGH
        )
        grow = jnp.exp(decay_end)
        local_part = grow[..., None] * (alive_end * start_block + partial_end)
        high, low = hi_lo(grow * alive_end * carry_block)
        packet = jnp.concatenate(
            [local_part.astype(jnp.bfloat16), high[:, None, :], low[:, None, :]], axis=1
        )
        packets.append(jnp.where(inside, packet, jnp.zeros_like(packet)))
    held = route_packets(jnp.stack(packets), end_rows, owners, tok_rows, "seq")
    mine = lax.axis_index("seq")
    owned_source = jnp.sum(jnp.where(owners == mine, (end_rows - 1) // tok_rows, 0))
    (incoming, owned_incoming), held = entering(
        device_decay, local_state, "seq", (mine, owned_source), held
    )
    held_coeff = held[:, HEAD].astype(jnp.float32) + held[:, HEAD + 1].astype(jnp.float32)
    handed_state = (held[:, :HEAD].astype(jnp.float32) + held_coeff[..., None] * owned_incoming)[None]
    block_state = start_state + start_decay[..., None] * incoming[None]
    carried_out = jnp.einsum("nihc,nhcd->nihd", query_tilde, block_state, precision=HIGH)
    mixer_out = (inner_out + surviving[:, :, None, None] * carried_out).reshape(
        tok_rows, head_count, HEAD
    )
    rescale = lax.rsqrt(jnp.mean(mixer_out * mixer_out, axis=-1, keepdims=True) + EPS)
    gate_heads = jax.nn.silu(gate_logit.reshape(tok_rows, head_count, HEAD))
    mixed_rows = (
        (mixer_out * rescale * gate_heads).reshape(tok_rows, head_count * HEAD).astype(jnp.bfloat16)
    )
    partial_terms = project(mixed_rows, output_weight)
    residual = (hidden_in.astype(jnp.float32) + narrow_sum(partial_terms)).astype(jnp.bfloat16)
    widened = widen_rows(residual)
    normed_ffn = rms_rows(widened, swiglu_gain)
    hidden = (
        jax.nn.silu(project(normed_ffn, swiglu_gate)) * project(normed_ffn, swiglu_up)
    ).astype(jnp.bfloat16)
    hidden_out = (residual.astype(jnp.float32) + narrow_sum(project(hidden, swiglu_down))).astype(
        jnp.bfloat16
    )
    return (hidden_out, handed_state)


def solution(mesh):
    in_specs = (
        P("seq", "wa"),
        P(),
        P(),
        P(),
        P(None, "wa"),
        P(None, "wa"),
        P(None, "wa"),
        P(None, "wa"),
        P("wa"),
        P("wa", None),
        P(),
        P(None, "wa"),
        P(None, "wa"),
        P("wa", None),
    )
    out_specs = (P("seq", "wa"), P("seq", "wa", None, None))
    return jax.shard_map(local, mesh=mesh, in_specs=in_specs, out_specs=out_specs, check_vma=False)
```

```python
import jax
import jax.numpy as jnp
from jax import lax
from jax.sharding import PartitionSpec as P

HEAD = 128
GROUP = 64
REQS = 4


EPS = 1e-06
HIGH = lax.Precision.HIGH


def hi_lo(values):
    high = values.astype(jnp.bfloat16)
    return high, (values - high.astype(jnp.float32)).astype(jnp.bfloat16)


def entering(decay, state, axis, targets):
    count = lax.axis_size(axis)
    rows = state.shape[1]
    high, low = hi_lo(decay)
    packed = jnp.concatenate([state.astype(jnp.bfloat16), high[:, None, :], low[:, None, :]], axis=1)
    every = lax.all_gather(packed, axis)
    decays = every[:, :, rows].astype(jnp.float32) + every[:, :, rows + 1].astype(jnp.float32)
    states = every[:, :, :rows].astype(jnp.float32)
    ranks = jnp.arange(count, dtype=jnp.int32)
    results = []
    for target in targets:
        between = (ranks[None, :] > ranks[:, None]) & (ranks[None, :] < target)
        weights = jnp.prod(jnp.where(between[:, :, None, None], decays[None], 1.0), axis=1)
        weights = jnp.where((ranks < target)[:, None, None], weights, 0.0)
        results.append(jnp.sum(weights[..., None] * states, axis=0))
    return results


def route_packets(packets, end_rows, owners, tok_rows, axis):
    count, mine = (lax.axis_size(axis), lax.axis_index(axis))
    left = [(i, (i - 1) % count) for i in range(count)]
    first = lax.ppermute(packets[0], axis, left)
    last = lax.ppermute(packets[-1], axis, [(count - 1, count // 2 - 1)])
    place = ((end_rows - 1) // tok_rows)[1:-1]
    offset = (owners[1:-1] - place) % count

    def shifter(shift):
        pairs = [(i, (i + shift) % count) for i in range(count)]
        return lambda packet: lax.ppermute(packet, axis, pairs) if shift else packet

    branches = [shifter(shift) for shift in range(count)]
    middle = [lax.switch(offset[slot], branches, packets[1 + slot]) for slot in range(REQS - 2)]
    zero = jnp.zeros_like(first)
    held = jnp.where(owners[0] == mine, first, zero) + jnp.where(owners[-1] == mine, last, zero)
    for part in middle:
        held = held + part
    return held


def rms_rows(matrix, scaling):
    matrix = matrix.astype(jnp.float32)
    rescale = lax.rsqrt(jnp.mean(matrix * matrix, axis=-1, keepdims=True) + EPS)
    return (matrix * rescale * scaling).astype(jnp.bfloat16)


def project(matrix, weight):
    return jnp.dot(matrix, weight, preferred_element_type=jnp.float32)


def widen_rows(shard_part):
    return lax.all_gather(shard_part, "wa", axis=1, tiled=True)


def narrow_sum(partial_terms):
    rows, cols = partial_terms.shape
    count = lax.axis_size("wa")
    pieces = partial_terms.astype(jnp.bfloat16).reshape(rows, count, cols // count)
    got = lax.all_to_all(pieces, "wa", 1, 1)
    return jnp.sum(got.astype(jnp.float32), axis=1)


def local(
    hidden_in,
    request_spans,
    owners,
    mixer_gain,
    query_weight,
    forget_weight,
    input_weight,
    gate_weight,
    forget_bias,
    output_weight,
    swiglu_gain,
    swiglu_gate,
    swiglu_up,
    swiglu_down,
):
    tok_rows = hidden_in.shape[0]
    head_count = query_weight.shape[1] // HEAD
    block_count = tok_rows // GROUP
    gathered = widen_rows(hidden_in)
    normed = rms_rows(gathered, mixer_gain)
    queries = jax.nn.silu(project(normed, query_weight))
    forget_logit = project(normed, forget_weight) + forget_bias
    log_decay = jax.nn.log_sigmoid(forget_logit)
    key_rows = jax.nn.sigmoid(-forget_logit)
    value_rows = project(normed, input_weight)
    gate_logit = project(normed, gate_weight)
    first_row = lax.axis_index("seq") * tok_rows
    position = first_row + jnp.arange(tok_rows, dtype=jnp.int32)
    start_rows = request_spans[:, 0]
    end_rows = request_spans[:, 1]
    is_start = jnp.any(position[:, None] == start_rows[None, :], axis=1)
    segment = jnp.sum((start_rows[None, :] <= position[:, None]).astype(jnp.int32), axis=1) - 1
    shape_four = (block_count, GROUP, head_count, HEAD)
    query_parts = queries.reshape(shape_four)
    key_parts = key_rows.reshape(shape_four)
    value_parts = value_rows.reshape(shape_four)
    segment_parts = segment.reshape(block_count, GROUP)
    keep_mask = (1.0 - is_start.astype(jnp.float32)).reshape(block_count, GROUP)
    cum_decay = jnp.cumsum(log_decay.reshape(shape_four), axis=1)
    surviving = jnp.cumprod(keep_mask, axis=1)
    query_tilde = query_parts * jnp.exp(cum_decay)
    key_tilde = key_parts * jnp.exp(-cum_decay)
    offsets = jnp.arange(GROUP, dtype=jnp.int32)
    causal = offsets[:, None] >= offsets[None, :]
    same_doc = causal[None] & (segment_parts[:, :, None] == segment_parts[:, None, :])
    scores = jnp.einsum("nihc,njhc->nhij", query_tilde, key_tilde, precision=HIGH)
    scores = jnp.where(same_doc[:, None], scores, 0.0)
    inner_out = jnp.einsum("nhij,njhd->nihd", scores, value_parts, precision=HIGH)
    tail_mask = (segment_parts == segment_parts[:, -1:]).astype(jnp.float32)
    last_decay = jnp.exp(cum_decay[:, -1])
    fresh = last_decay[..., None] * jnp.einsum(
        "njhc,njhd->nhcd", key_tilde * tail_mask[:, :, None, None], value_parts, precision=HIGH
    )
    shrink = surviving[:, -1][:, None, None] * last_decay

    def advance(carried, blocked):
        running, product = carried
        shrink_part, fresh_part = blocked
        return (
            (shrink_part[..., None] * running + fresh_part, product * shrink_part),
            (running, product),
        )

    initial = (
        jnp.zeros((head_count, HEAD, HEAD), jnp.float32),
        jnp.ones((head_count, HEAD), jnp.float32),
    )
    (local_state, device_decay), (start_state, start_decay) = lax.scan(
        advance, initial, (shrink, fresh), unroll=True
    )

    packets = []
    for request in range(REQS):
        local_end = end_rows[request] - 1 - first_row
        inside = (local_end >= 0) & (local_end < tok_rows)
        end_row = jnp.clip(local_end, 0, tok_rows - 1)
        block_index = end_row // GROUP
        within = end_row % GROUP
        decay_block = lax.dynamic_index_in_dim(cum_decay, block_index, 0, keepdims=False)
        key_block = lax.dynamic_index_in_dim(key_tilde, block_index, 0, keepdims=False)
        value_block = lax.dynamic_index_in_dim(value_parts, block_index, 0, keepdims=False)
        segment_block = lax.dynamic_index_in_dim(segment_parts, block_index, 0, keepdims=False)
        alive_block = lax.dynamic_index_in_dim(surviving, block_index, 0, keepdims=False)
        start_block = lax.dynamic_index_in_dim(start_state, block_index, 0, keepdims=False)
        carry_block = lax.dynamic_index_in_dim(start_decay, block_index, 0, keepdims=False)
        decay_end = lax.dynamic_index_in_dim(decay_block, within, 0, keepdims=False)
        segment_end = lax.dynamic_index_in_dim(segment_block, within, 0, keepdims=False)
        alive_end = lax.dynamic_index_in_dim(alive_block, within, 0, keepdims=False)
        upto_mask = ((offsets <= within) & (segment_block == segment_end)).astype(jnp.float32)
        partial_end = jnp.einsum(
            "jhc,jhd->hcd", key_block * upto_mask[:, None, None], value_block, precision=HIGH
        )
        grow = jnp.exp(decay_end)
        local_part = grow[..., None] * (alive_end * start_block + partial_end)
        high, low = hi_lo(grow * alive_end * carry_block)
        packet = jnp.concatenate(
            [local_part.astype(jnp.bfloat16), high[:, None, :], low[:, None, :]], axis=1
        )
        packets.append(jnp.where(inside, packet, jnp.zeros_like(packet)))
    held = route_packets(jnp.stack(packets), end_rows, owners, tok_rows, "seq")
    mine = lax.axis_index("seq")
    owned_source = jnp.sum(jnp.where(owners == mine, (end_rows - 1) // tok_rows, 0))
    incoming, owned_incoming = entering(device_decay, local_state, "seq", (mine, owned_source))
    held_coeff = held[:, HEAD].astype(jnp.float32) + held[:, HEAD + 1].astype(jnp.float32)
    handed_state = (held[:, :HEAD].astype(jnp.float32) + held_coeff[..., None] * owned_incoming)[None]
    block_state = start_state + start_decay[..., None] * incoming[None]
    carried_out = jnp.einsum("nihc,nhcd->nihd", query_tilde, block_state, precision=HIGH)
    mixer_out = (inner_out + surviving[:, :, None, None] * carried_out).reshape(
        tok_rows, head_count, HEAD
    )
    rescale = lax.rsqrt(jnp.mean(mixer_out * mixer_out, axis=-1, keepdims=True) + EPS)
    gate_heads = jax.nn.silu(gate_logit.reshape(tok_rows, head_count, HEAD))
    mixed_rows = (
        (mixer_out * rescale * gate_heads).reshape(tok_rows, head_count * HEAD).astype(jnp.bfloat16)
    )
    partial_terms = project(mixed_rows, output_weight)
    residual = (hidden_in.astype(jnp.float32) + narrow_sum(partial_terms)).astype(jnp.bfloat16)
    widened = widen_rows(residual)
    normed_ffn = rms_rows(widened, swiglu_gain)
    hidden = (
        jax.nn.silu(project(normed_ffn, swiglu_gate)) * project(normed_ffn, swiglu_up)
    ).astype(jnp.bfloat16)
    hidden_out = (residual.astype(jnp.float32) + narrow_sum(project(hidden, swiglu_down))).astype(
        jnp.bfloat16
    )
    return (hidden_out, handed_state)


def solution(mesh):
    in_specs = (
        P("seq", "wa"),
        P(),
        P(),
        P(),
        P(None, "wa"),
        P(None, "wa"),
        P(None, "wa"),
        P(None, "wa"),
        P("wa"),
        P("wa", None),
        P(),
        P(None, "wa"),
        P(None, "wa"),
        P("wa", None),
    )
    out_specs = (P("seq", "wa"), P("seq", "wa", None, None))
    return jax.shard_map(local, mesh=mesh, in_specs=in_specs, out_specs=out_specs, check_vma=False)
```

```python
import jax
import jax.numpy as jnp
from jax import lax
from jax.sharding import PartitionSpec as P

HEAD = 128
GROUP = 64
REQS = 4


EPS = 1e-06
HIGH = lax.Precision.HIGH


def hi_lo(values):
    high = values.astype(jnp.bfloat16)
    return high, (values - high.astype(jnp.float32)).astype(jnp.bfloat16)


def entering(decay, state, axis, targets, companion):
    count = lax.axis_size(axis)
    rows = state.shape[1]
    high, low = hi_lo(decay)
    packed = jnp.concatenate([state.astype(jnp.bfloat16), high[:, None, :], low[:, None, :]], axis=1)
    every, companion = lax.optimization_barrier((lax.all_gather(packed, axis), companion))
    decays = every[:, :, rows].astype(jnp.float32) + every[:, :, rows + 1].astype(jnp.float32)
    states = every[:, :, :rows].astype(jnp.float32)
    ranks = jnp.arange(count, dtype=jnp.int32)
    results = []
    for target in targets:
        between = (ranks[None, :] > ranks[:, None]) & (ranks[None, :] < target)
        weights = jnp.prod(jnp.where(between[:, :, None, None], decays[None], 1.0), axis=1)
        weights = jnp.where((ranks < target)[:, None, None], weights, 0.0)
        results.append(jnp.sum(weights[..., None] * states, axis=0))
    return results, companion


def route_packets(packets, end_rows, owners, tok_rows, axis):
    count, mine = (lax.axis_size(axis), lax.axis_index(axis))
    left = [(i, (i - 1) % count) for i in range(count)]
    first = lax.ppermute(packets[0], axis, left)
    last = lax.ppermute(packets[-1], axis, [(count - 1, count // 2 - 1)])
    place = ((end_rows - 1) // tok_rows)[1:-1]
    offset = (owners[1:-1] - place) % count

    def shifter(shift):
        pairs = [(i, (i + shift) % count) for i in range(count)]
        return lambda packet: lax.ppermute(packet, axis, pairs) if shift else packet

    branches = [shifter(shift) for shift in range(count)]
    middle = [lax.switch(offset[slot], branches, packets[1 + slot]) for slot in range(REQS - 2)]
    zero = jnp.zeros_like(first)
    held = jnp.where(owners[0] == mine, first, zero) + jnp.where(owners[-1] == mine, last, zero)
    for part in middle:
        held = held + part
    return held


def rms_rows(matrix, scaling):
    matrix = matrix.astype(jnp.float32)
    rescale = lax.rsqrt(jnp.mean(matrix * matrix, axis=-1, keepdims=True) + EPS)
    return (matrix * rescale * scaling).astype(jnp.bfloat16)


def project(matrix, weight):
    return jnp.dot(matrix, weight, preferred_element_type=jnp.float32)


def widen_rows(shard_part):
    return lax.all_gather(shard_part, "wa", axis=1, tiled=True)


def narrow_sum(partial_terms):
    rows, cols = partial_terms.shape
    count = lax.axis_size("wa")
    pieces = partial_terms.astype(jnp.bfloat16).reshape(rows, count, cols // count)
    got = lax.all_to_all(pieces, "wa", 1, 1)
    return jnp.sum(got.astype(jnp.float32), axis=1)


def local(
    hidden_in,
    request_spans,
    owners,
    mixer_gain,
    query_weight,
    forget_weight,
    input_weight,
    gate_weight,
    forget_bias,
    output_weight,
    swiglu_gain,
    swiglu_gate,
    swiglu_up,
    swiglu_down,
):
    tok_rows = hidden_in.shape[0]
    head_count = query_weight.shape[1] // HEAD
    block_count = tok_rows // GROUP
    gathered = widen_rows(hidden_in)
    normed = rms_rows(gathered, mixer_gain)
    queries = jax.nn.silu(project(normed, query_weight))
    forget_logit = project(normed, forget_weight) + forget_bias
    log_decay = jax.nn.log_sigmoid(forget_logit)
    key_rows = jax.nn.sigmoid(-forget_logit)
    value_rows = project(normed, input_weight)
    gate_logit = project(normed, gate_weight)
    first_row = lax.axis_index("seq") * tok_rows
    position = first_row + jnp.arange(tok_rows, dtype=jnp.int32)
    start_rows = request_spans[:, 0]
    end_rows = request_spans[:, 1]
    is_start = jnp.any(position[:, None] == start_rows[None, :], axis=1)
    segment = jnp.sum((start_rows[None, :] <= position[:, None]).astype(jnp.int32), axis=1) - 1
    shape_four = (block_count, GROUP, head_count, HEAD)
    query_parts = queries.reshape(shape_four)
    key_parts = key_rows.reshape(shape_four)
    value_parts = value_rows.reshape(shape_four)
    segment_parts = segment.reshape(block_count, GROUP)
    keep_mask = (1.0 - is_start.astype(jnp.float32)).reshape(block_count, GROUP)
    cum_decay = jnp.cumsum(log_decay.reshape(shape_four), axis=1)
    surviving = jnp.cumprod(keep_mask, axis=1)
    query_tilde = query_parts * jnp.exp(cum_decay)
    key_tilde = key_parts * jnp.exp(-cum_decay)
    offsets = jnp.arange(GROUP, dtype=jnp.int32)
    causal = offsets[:, None] >= offsets[None, :]
    same_doc = causal[None] & (segment_parts[:, :, None] == segment_parts[:, None, :])
    scores = jnp.einsum("nihc,njhc->nhij", query_tilde, key_tilde, precision=HIGH)
    scores = jnp.where(same_doc[:, None], scores, 0.0)
    inner_out = jnp.einsum("nhij,njhd->nihd", scores, value_parts, precision=HIGH)
    tail_mask = (segment_parts == segment_parts[:, -1:]).astype(jnp.float32)
    last_decay = jnp.exp(cum_decay[:, -1])
    fresh = last_decay[..., None] * jnp.einsum(
        "njhc,njhd->nhcd", key_tilde * tail_mask[:, :, None, None], value_parts, precision=HIGH
    )
    shrink = surviving[:, -1][:, None, None] * last_decay

    def advance(carried, blocked):
        running, product = carried
        shrink_part, fresh_part = blocked
        return (
            (shrink_part[..., None] * running + fresh_part, product * shrink_part),
            (running, product),
        )

    initial = (
        jnp.zeros((head_count, HEAD, HEAD), jnp.float32),
        jnp.ones((head_count, HEAD), jnp.float32),
    )
    (local_state, device_decay), (start_state, start_decay) = lax.scan(
        advance, initial, (shrink, fresh), unroll=True
    )

    packets = []
    for request in range(REQS):
        local_end = end_rows[request] - 1 - first_row
        inside = (local_end >= 0) & (local_end < tok_rows)
        end_row = jnp.clip(local_end, 0, tok_rows - 1)
        block_index = end_row // GROUP
        within = end_row % GROUP
        decay_block = lax.dynamic_index_in_dim(cum_decay, block_index, 0, keepdims=False)
        key_block = lax.dynamic_index_in_dim(key_tilde, block_index, 0, keepdims=False)
        value_block = lax.dynamic_index_in_dim(value_parts, block_index, 0, keepdims=False)
        segment_block = lax.dynamic_index_in_dim(segment_parts, block_index, 0, keepdims=False)
        alive_block = lax.dynamic_index_in_dim(surviving, block_index, 0, keepdims=False)
        start_block = lax.dynamic_index_in_dim(start_state, block_index, 0, keepdims=False)
        carry_block = lax.dynamic_index_in_dim(start_decay, block_index, 0, keepdims=False)
        decay_end = lax.dynamic_index_in_dim(decay_block, within, 0, keepdims=False)
        segment_end = lax.dynamic_index_in_dim(segment_block, within, 0, keepdims=False)
        alive_end = lax.dynamic_index_in_dim(alive_block, within, 0, keepdims=False)
        upto_mask = ((offsets <= within) & (segment_block == segment_end)).astype(jnp.float32)
        partial_end = jnp.einsum(
            "jhc,jhd->hcd", key_block * upto_mask[:, None, None], value_block, precision=HIGH
        )
        grow = jnp.exp(decay_end)
        local_part = grow[..., None] * (alive_end * start_block + partial_end)
        high, low = hi_lo(grow * alive_end * carry_block)
        packet = jnp.concatenate(
            [local_part.astype(jnp.bfloat16), high[:, None, :], low[:, None, :]], axis=1
        )
        packets.append(jnp.where(inside, packet, jnp.zeros_like(packet)))
    held = route_packets(jnp.stack(packets), end_rows, owners, tok_rows, "seq")
    mine = lax.axis_index("seq")
    owned_source = jnp.sum(jnp.where(owners == mine, (end_rows - 1) // tok_rows, 0))
    (incoming, owned_incoming), held = entering(
        device_decay, local_state, "seq", (mine, owned_source), held
    )
    held_coeff = held[:, HEAD].astype(jnp.float32) + held[:, HEAD + 1].astype(jnp.float32)
    handed_state = (held[:, :HEAD].astype(jnp.float32) + held_coeff[..., None] * owned_incoming)[None]
    block_state = start_state + start_decay[..., None] * incoming[None]
    carried_out = jnp.einsum("nihc,nhcd->nihd", query_tilde, block_state, precision=HIGH)
    mixer_out = (inner_out + surviving[:, :, None, None] * carried_out).reshape(
        tok_rows, head_count, HEAD
    )
    rescale = lax.rsqrt(jnp.mean(mixer_out * mixer_out, axis=-1, keepdims=True) + EPS)
    gate_heads = jax.nn.silu(gate_logit.reshape(tok_rows, head_count, HEAD))
    mixed_rows = (
        (mixer_out * rescale * gate_heads).reshape(tok_rows, head_count * HEAD).astype(jnp.bfloat16)
    )
    partial_terms = project(mixed_rows, output_weight)
    residual = (hidden_in.astype(jnp.float32) + narrow_sum(partial_terms)).astype(jnp.bfloat16)
    widened = widen_rows(residual)
    normed_ffn = rms_rows(widened, swiglu_gain)
    hidden = (
        jax.nn.silu(project(normed_ffn, swiglu_gate)) * project(normed_ffn, swiglu_up)
    ).astype(jnp.bfloat16)
    hidden_out = (residual.astype(jnp.float32) + narrow_sum(project(hidden, swiglu_down))).astype(
        jnp.bfloat16
    )
    return (hidden_out, handed_state)


def solution(mesh):
    in_specs = (
        P("seq", "wa"),
        P(),
        P(),
        P(),
        P(None, "wa"),
        P(None, "wa"),
        P(None, "wa"),
        P(None, "wa"),
        P("wa"),
        P("wa", None),
        P(),
        P(None, "wa"),
        P(None, "wa"),
        P("wa", None),
    )
    out_specs = (P("seq", "wa"), P("seq", "wa", None, None))
    return jax.shard_map(local, mesh=mesh, in_specs=in_specs, out_specs=out_specs, check_vma=False)
```

```python
import jax
import jax.numpy as jnp
from jax import lax
from jax.sharding import PartitionSpec as P

HEAD = 128
GROUP = 64
REQS = 4


EPS = 1e-06
HIGH = lax.Precision.HIGH


def hi_lo(values):
    high = values.astype(jnp.bfloat16)
    return high, (values - high.astype(jnp.float32)).astype(jnp.bfloat16)


def entering(decay, state, axis, targets):
    count = lax.axis_size(axis)
    rows = state.shape[1]
    high, low = hi_lo(decay)
    packed = jnp.concatenate([state.astype(jnp.bfloat16), high[:, None, :], low[:, None, :]], axis=1)
    every = lax.all_gather(packed, axis)
    decays = every[:, :, rows].astype(jnp.float32) + every[:, :, rows + 1].astype(jnp.float32)
    states = every[:, :, :rows].astype(jnp.float32)
    ranks = jnp.arange(count, dtype=jnp.int32)
    results = []
    for target in targets:
        between = (ranks[None, :] > ranks[:, None]) & (ranks[None, :] < target)
        weights = jnp.prod(jnp.where(between[:, :, None, None], decays[None], 1.0), axis=1)
        weights = jnp.where((ranks < target)[:, None, None], weights, 0.0)
        results.append(jnp.sum(weights[..., None] * states, axis=0))
    return results


def route_packets(packets, end_rows, owners, tok_rows, axis):
    count, mine = (lax.axis_size(axis), lax.axis_index(axis))
    left = [(i, (i - 1) % count) for i in range(count)]
    first = lax.ppermute(packets[0], axis, left)
    last = lax.ppermute(packets[-1], axis, [(count - 1, count // 2 - 1)])
    place = ((end_rows - 1) // tok_rows)[1:-1]
    offset = (owners[1:-1] - place) % count

    def shifter(shift):
        pairs = [(i, (i + shift) % count) for i in range(count)]
        return lambda packet: lax.ppermute(packet, axis, pairs) if shift else packet

    fine = 4
    near = [shifter(shift) for shift in range(fine)]
    far = [shifter(shift * fine) for shift in range(count // fine)]
    middle = [
        lax.switch(offset[slot] // fine, far, lax.switch(offset[slot] % fine, near, packets[1 + slot]))
        for slot in range(REQS - 2)
    ]
    zero = jnp.zeros_like(first)
    held = jnp.where(owners[0] == mine, first, zero) + jnp.where(owners[-1] == mine, last, zero)
    for part in middle:
        held = held + part
    return held


def rms_rows(matrix, scaling):
    matrix = matrix.astype(jnp.float32)
    rescale = lax.rsqrt(jnp.mean(matrix * matrix, axis=-1, keepdims=True) + EPS)
    return (matrix * rescale * scaling).astype(jnp.bfloat16)


def project(matrix, weight):
    return jnp.dot(matrix, weight, preferred_element_type=jnp.float32)


def widen_rows(shard_part):
    return lax.all_gather(shard_part, "wa", axis=1, tiled=True)


def narrow_sum(partial_terms):
    rows, cols = partial_terms.shape
    count = lax.axis_size("wa")
    pieces = partial_terms.astype(jnp.bfloat16).reshape(rows, count, cols // count)
    got = lax.all_to_all(pieces, "wa", 1, 1)
    return jnp.sum(got.astype(jnp.float32), axis=1)


def local(
    hidden_in,
    request_spans,
    owners,
    mixer_gain,
    query_weight,
    forget_weight,
    input_weight,
    gate_weight,
    forget_bias,
    output_weight,
    swiglu_gain,
    swiglu_gate,
    swiglu_up,
    swiglu_down,
):
    tok_rows = hidden_in.shape[0]
    head_count = query_weight.shape[1] // HEAD
    block_count = tok_rows // GROUP
    gathered = widen_rows(hidden_in)
    normed = rms_rows(gathered, mixer_gain)
    queries = jax.nn.silu(project(normed, query_weight))
    forget_logit = project(normed, forget_weight) + forget_bias
    log_decay = jax.nn.log_sigmoid(forget_logit)
    key_rows = jax.nn.sigmoid(-forget_logit)
    value_rows = project(normed, input_weight)
    gate_logit = project(normed, gate_weight)
    first_row = lax.axis_index("seq") * tok_rows
    position = first_row + jnp.arange(tok_rows, dtype=jnp.int32)
    start_rows = request_spans[:, 0]
    end_rows = request_spans[:, 1]
    is_start = jnp.any(position[:, None] == start_rows[None, :], axis=1)
    segment = jnp.sum((start_rows[None, :] <= position[:, None]).astype(jnp.int32), axis=1) - 1
    shape_four = (block_count, GROUP, head_count, HEAD)
    query_parts = queries.reshape(shape_four)
    key_parts = key_rows.reshape(shape_four)
    value_parts = value_rows.reshape(shape_four)
    segment_parts = segment.reshape(block_count, GROUP)
    keep_mask = (1.0 - is_start.astype(jnp.float32)).reshape(block_count, GROUP)
    cum_decay = jnp.cumsum(log_decay.reshape(shape_four), axis=1)
    surviving = jnp.cumprod(keep_mask, axis=1)
    query_tilde = query_parts * jnp.exp(cum_decay)
    key_tilde = key_parts * jnp.exp(-cum_decay)
    offsets = jnp.arange(GROUP, dtype=jnp.int32)
    causal = offsets[:, None] >= offsets[None, :]
    same_doc = causal[None] & (segment_parts[:, :, None] == segment_parts[:, None, :])
    scores = jnp.einsum("nihc,njhc->nhij", query_tilde, key_tilde, precision=HIGH)
    scores = jnp.where(same_doc[:, None], scores, 0.0)
    inner_out = jnp.einsum("nhij,njhd->nihd", scores, value_parts, precision=HIGH)
    tail_mask = (segment_parts == segment_parts[:, -1:]).astype(jnp.float32)
    last_decay = jnp.exp(cum_decay[:, -1])
    fresh = last_decay[..., None] * jnp.einsum(
        "njhc,njhd->nhcd", key_tilde * tail_mask[:, :, None, None], value_parts, precision=HIGH
    )
    shrink = surviving[:, -1][:, None, None] * last_decay

    def advance(carried, blocked):
        running, product = carried
        shrink_part, fresh_part = blocked
        return (
            (shrink_part[..., None] * running + fresh_part, product * shrink_part),
            (running, product),
        )

    initial = (
        jnp.zeros((head_count, HEAD, HEAD), jnp.float32),
        jnp.ones((head_count, HEAD), jnp.float32),
    )
    (local_state, device_decay), (start_state, start_decay) = lax.scan(
        advance, initial, (shrink, fresh), unroll=True
    )

    packets = []
    for request in range(REQS):
        local_end = end_rows[request] - 1 - first_row
        inside = (local_end >= 0) & (local_end < tok_rows)
        end_row = jnp.clip(local_end, 0, tok_rows - 1)
        block_index = end_row // GROUP
        within = end_row % GROUP
        decay_block = lax.dynamic_index_in_dim(cum_decay, block_index, 0, keepdims=False)
        key_block = lax.dynamic_index_in_dim(key_tilde, block_index, 0, keepdims=False)
        value_block = lax.dynamic_index_in_dim(value_parts, block_index, 0, keepdims=False)
        segment_block = lax.dynamic_index_in_dim(segment_parts, block_index, 0, keepdims=False)
        alive_block = lax.dynamic_index_in_dim(surviving, block_index, 0, keepdims=False)
        start_block = lax.dynamic_index_in_dim(start_state, block_index, 0, keepdims=False)
        carry_block = lax.dynamic_index_in_dim(start_decay, block_index, 0, keepdims=False)
        decay_end = lax.dynamic_index_in_dim(decay_block, within, 0, keepdims=False)
        segment_end = lax.dynamic_index_in_dim(segment_block, within, 0, keepdims=False)
        alive_end = lax.dynamic_index_in_dim(alive_block, within, 0, keepdims=False)
        upto_mask = ((offsets <= within) & (segment_block == segment_end)).astype(jnp.float32)
        partial_end = jnp.einsum(
            "jhc,jhd->hcd", key_block * upto_mask[:, None, None], value_block, precision=HIGH
        )
        grow = jnp.exp(decay_end)
        local_part = grow[..., None] * (alive_end * start_block + partial_end)
        high, low = hi_lo(grow * alive_end * carry_block)
        packet = jnp.concatenate(
            [local_part.astype(jnp.bfloat16), high[:, None, :], low[:, None, :]], axis=1
        )
        packets.append(jnp.where(inside, packet, jnp.zeros_like(packet)))
    held = route_packets(jnp.stack(packets), end_rows, owners, tok_rows, "seq")
    mine = lax.axis_index("seq")
    owned_source = jnp.sum(jnp.where(owners == mine, (end_rows - 1) // tok_rows, 0))
    incoming, owned_incoming = entering(device_decay, local_state, "seq", (mine, owned_source))
    held_coeff = held[:, HEAD].astype(jnp.float32) + held[:, HEAD + 1].astype(jnp.float32)
    handed_state = (held[:, :HEAD].astype(jnp.float32) + held_coeff[..., None] * owned_incoming)[None]
    block_state = start_state + start_decay[..., None] * incoming[None]
    carried_out = jnp.einsum("nihc,nhcd->nihd", query_tilde, block_state, precision=HIGH)
    mixer_out = (inner_out + surviving[:, :, None, None] * carried_out).reshape(
        tok_rows, head_count, HEAD
    )
    rescale = lax.rsqrt(jnp.mean(mixer_out * mixer_out, axis=-1, keepdims=True) + EPS)
    gate_heads = jax.nn.silu(gate_logit.reshape(tok_rows, head_count, HEAD))
    mixed_rows = (
        (mixer_out * rescale * gate_heads).reshape(tok_rows, head_count * HEAD).astype(jnp.bfloat16)
    )
    partial_terms = project(mixed_rows, output_weight)
    residual = (hidden_in.astype(jnp.float32) + narrow_sum(partial_terms)).astype(jnp.bfloat16)
    widened = widen_rows(residual)
    normed_ffn = rms_rows(widened, swiglu_gain)
    hidden = (
        jax.nn.silu(project(normed_ffn, swiglu_gate)) * project(normed_ffn, swiglu_up)
    ).astype(jnp.bfloat16)
    hidden_out = (residual.astype(jnp.float32) + narrow_sum(project(hidden, swiglu_down))).astype(
        jnp.bfloat16
    )
    return (hidden_out, handed_state)


def solution(mesh):
    in_specs = (
        P("seq", "wa"),
        P(),
        P(),
        P(),
        P(None, "wa"),
        P(None, "wa"),
        P(None, "wa"),
        P(None, "wa"),
        P("wa"),
        P("wa", None),
        P(),
        P(None, "wa"),
        P(None, "wa"),
        P("wa", None),
    )
    out_specs = (P("seq", "wa"), P("seq", "wa", None, None))
    return jax.shard_map(local, mesh=mesh, in_specs=in_specs, out_specs=out_specs, check_vma=False)
```

```python
import jax
import jax.numpy as jnp
from jax import lax
from jax.sharding import PartitionSpec as P

HEAD = 128
GROUP = 64
REQS = 4


EPS = 1e-06
HIGH = lax.Precision.HIGH


def hi_lo(values):
    high = values.astype(jnp.bfloat16)
    return high, (values - high.astype(jnp.float32)).astype(jnp.bfloat16)


def entering(decay, state, axis, targets):
    count = lax.axis_size(axis)
    rows = state.shape[1]
    high, low = hi_lo(decay)
    packed = jnp.concatenate([state.astype(jnp.bfloat16), high[:, None, :], low[:, None, :]], axis=1)
    every = lax.all_gather(packed, axis)
    decays = every[:, :, rows].astype(jnp.float32) + every[:, :, rows + 1].astype(jnp.float32)
    states = every[:, :, :rows].astype(jnp.float32)
    ranks = jnp.arange(count, dtype=jnp.int32)
    results = []
    for target in targets:
        between = (ranks[None, :] > ranks[:, None]) & (ranks[None, :] < target)
        weights = jnp.prod(jnp.where(between[:, :, None, None], decays[None], 1.0), axis=1)
        weights = jnp.where((ranks < target)[:, None, None], weights, 0.0)
        results.append(jnp.sum(weights[..., None] * states, axis=0))
    return results


def route_packets(packets, end_rows, owners, tok_rows, axis):
    count, mine = (lax.axis_size(axis), lax.axis_index(axis))
    left = [(i, (i - 1) % count) for i in range(count)]
    first = lax.ppermute(packets[0], axis, left)
    last = lax.ppermute(packets[-1], axis, [(count - 1, count // 2 - 1)])
    place = ((end_rows - 1) // tok_rows)[1:-1]
    offset = (owners[1:-1] - place) % count

    def shifter(shift):
        pairs = [(i, (i + shift) % count) for i in range(count)]
        return lambda packet: lax.ppermute(packet, axis, pairs) if shift else packet

    branches = [shifter(shift) for shift in range(count)]
    middle = [lax.switch(offset[slot], branches, packets[1 + slot]) for slot in range(REQS - 2)]
    zero = jnp.zeros_like(first)
    held = jnp.where(owners[0] == mine, first, zero) + jnp.where(owners[-1] == mine, last, zero)
    for part in middle:
        held = held + part
    return held


def rms_rows(matrix, scaling):
    matrix = matrix.astype(jnp.float32)
    rescale = lax.rsqrt(jnp.mean(matrix * matrix, axis=-1, keepdims=True) + EPS)
    return (matrix * rescale * scaling).astype(jnp.bfloat16)


def project(matrix, weight):
    return jnp.dot(matrix, weight, preferred_element_type=jnp.float32)


def widen_rows(shard_part):
    return lax.all_gather(shard_part, "wa", axis=1, tiled=True)


def narrow_sum(partial_terms):
    rows, cols = partial_terms.shape
    count = lax.axis_size("wa")
    pieces = partial_terms.astype(jnp.bfloat16).reshape(rows, count, cols // count)
    got = lax.all_to_all(pieces, "wa", 1, 1)
    return jnp.sum(got.astype(jnp.float32), axis=1)


def local(
    hidden_in,
    request_spans,
    owners,
    mixer_gain,
    query_weight,
    forget_weight,
    input_weight,
    gate_weight,
    forget_bias,
    output_weight,
    swiglu_gain,
    swiglu_gate,
    swiglu_up,
    swiglu_down,
):
    tok_rows = hidden_in.shape[0]
    head_count = query_weight.shape[1] // HEAD
    block_count = tok_rows // GROUP
    gathered = widen_rows(hidden_in)
    normed = rms_rows(gathered, mixer_gain)

    def heads(weight):
        split = weight.reshape(weight.shape[0], head_count, HEAD)
        return jnp.einsum("tk,khd->htd", normed, split, preferred_element_type=jnp.float32)

    queries = jax.nn.silu(heads(query_weight))
    forget_logit = heads(forget_weight) + forget_bias.reshape(head_count, 1, HEAD)
    log_decay = jax.nn.log_sigmoid(forget_logit)
    key_rows = jax.nn.sigmoid(-forget_logit)
    value_rows = heads(input_weight)
    gate_logit = heads(gate_weight)
    first_row = lax.axis_index("seq") * tok_rows
    position = first_row + jnp.arange(tok_rows, dtype=jnp.int32)
    start_rows = request_spans[:, 0]
    end_rows = request_spans[:, 1]
    is_start = jnp.any(position[:, None] == start_rows[None, :], axis=1)
    segment = jnp.sum((start_rows[None, :] <= position[:, None]).astype(jnp.int32), axis=1) - 1
    shape_four = (head_count, block_count, GROUP, HEAD)
    query_parts = queries.reshape(shape_four)
    key_parts = key_rows.reshape(shape_four)
    value_parts = value_rows.reshape(shape_four)
    segment_parts = segment.reshape(block_count, GROUP)
    keep_mask = (1.0 - is_start.astype(jnp.float32)).reshape(block_count, GROUP)
    cum_decay = jnp.cumsum(log_decay.reshape(shape_four), axis=2)
    surviving = jnp.cumprod(keep_mask, axis=1)
    query_tilde = query_parts * jnp.exp(cum_decay)
    key_tilde = key_parts * jnp.exp(-cum_decay)
    offsets = jnp.arange(GROUP, dtype=jnp.int32)
    causal = offsets[:, None] >= offsets[None, :]
    same_doc = causal[None] & (segment_parts[:, :, None] == segment_parts[:, None, :])
    scores = jnp.einsum("hnic,hnjc->hnij", query_tilde, key_tilde, precision=HIGH)
    scores = jnp.where(same_doc[None], scores, 0.0)
    inner_out = jnp.einsum("hnij,hnjd->hnid", scores, value_parts, precision=HIGH)
    tail_mask = (segment_parts == segment_parts[:, -1:]).astype(jnp.float32)
    last_decay = jnp.exp(cum_decay[:, :, -1])
    fresh = last_decay[..., None] * jnp.einsum(
        "hnjc,hnjd->hncd", key_tilde * tail_mask[None, :, :, None], value_parts, precision=HIGH
    )
    shrink = surviving[:, -1][None, :, None] * last_decay
    running = jnp.zeros((head_count, HEAD, HEAD), jnp.float32)
    product = jnp.ones((head_count, HEAD), jnp.float32)
    starts, carries = [], []
    for block in range(block_count):
        starts.append(running)
        carries.append(product)
        running = shrink[:, block, :, None] * running + fresh[:, block]
        product = product * shrink[:, block]
    local_state, device_decay = running, product
    start_state = jnp.stack(starts, axis=1)
    start_decay = jnp.stack(carries, axis=1)

    packets = []
    for request in range(REQS):
        local_end = end_rows[request] - 1 - first_row
        inside = (local_end >= 0) & (local_end < tok_rows)
        end_row = jnp.clip(local_end, 0, tok_rows - 1)
        block_index = end_row // GROUP
        within = end_row % GROUP
        decay_block = lax.dynamic_index_in_dim(cum_decay, block_index, 1, keepdims=False)
        key_block = lax.dynamic_index_in_dim(key_tilde, block_index, 1, keepdims=False)
        value_block = lax.dynamic_index_in_dim(value_parts, block_index, 1, keepdims=False)
        segment_block = lax.dynamic_index_in_dim(segment_parts, block_index, 0, keepdims=False)
        alive_block = lax.dynamic_index_in_dim(surviving, block_index, 0, keepdims=False)
        start_block = lax.dynamic_index_in_dim(start_state, block_index, 1, keepdims=False)
        carry_block = lax.dynamic_index_in_dim(start_decay, block_index, 1, keepdims=False)
        decay_end = lax.dynamic_index_in_dim(decay_block, within, 1, keepdims=False)
        segment_end = lax.dynamic_index_in_dim(segment_block, within, 0, keepdims=False)
        alive_end = lax.dynamic_index_in_dim(alive_block, within, 0, keepdims=False)
        upto_mask = ((offsets <= within) & (segment_block == segment_end)).astype(jnp.float32)
        partial_end = jnp.einsum(
            "hjc,hjd->hcd", key_block * upto_mask[None, :, None], value_block, precision=HIGH
        )
        grow = jnp.exp(decay_end)
        local_part = grow[..., None] * (alive_end * start_block + partial_end)
        high, low = hi_lo(grow * alive_end * carry_block)
        packet = jnp.concatenate(
            [local_part.astype(jnp.bfloat16), high[:, None, :], low[:, None, :]], axis=1
        )
        packets.append(jnp.where(inside, packet, jnp.zeros_like(packet)))
    held = route_packets(jnp.stack(packets), end_rows, owners, tok_rows, "seq")
    mine = lax.axis_index("seq")
    owned_source = jnp.sum(jnp.where(owners == mine, (end_rows - 1) // tok_rows, 0))
    incoming, owned_incoming = entering(device_decay, local_state, "seq", (mine, owned_source))
    held_coeff = held[:, HEAD].astype(jnp.float32) + held[:, HEAD + 1].astype(jnp.float32)
    handed_state = (held[:, :HEAD].astype(jnp.float32) + held_coeff[..., None] * owned_incoming)[None]
    block_state = start_state + start_decay[..., None] * incoming[:, None]
    carried_out = jnp.einsum("hnic,hncd->hnid", query_tilde, block_state, precision=HIGH)
    mixer_out = (inner_out + surviving[None, :, :, None] * carried_out).reshape(
        head_count, tok_rows, HEAD
    )
    rescale = lax.rsqrt(jnp.mean(mixer_out * mixer_out, axis=-1, keepdims=True) + EPS)
    mixed = (mixer_out * rescale * jax.nn.silu(gate_logit)).astype(jnp.bfloat16)
    out_split = output_weight.reshape(head_count, HEAD, output_weight.shape[1])
    partial_terms = jnp.einsum("htd,hdo->to", mixed, out_split, preferred_element_type=jnp.float32)
    residual = (hidden_in.astype(jnp.float32) + narrow_sum(partial_terms)).astype(jnp.bfloat16)
    widened = widen_rows(residual)
    normed_ffn = rms_rows(widened, swiglu_gain)
    hidden = (
        jax.nn.silu(project(normed_ffn, swiglu_gate)) * project(normed_ffn, swiglu_up)
    ).astype(jnp.bfloat16)
    hidden_out = (residual.astype(jnp.float32) + narrow_sum(project(hidden, swiglu_down))).astype(
        jnp.bfloat16
    )
    return (hidden_out, handed_state)


def solution(mesh):
    in_specs = (
        P("seq", "wa"),
        P(),
        P(),
        P(),
        P(None, "wa"),
        P(None, "wa"),
        P(None, "wa"),
        P(None, "wa"),
        P("wa"),
        P("wa", None),
        P(),
        P(None, "wa"),
        P(None, "wa"),
        P("wa", None),
    )
    out_specs = (P("seq", "wa"), P("seq", "wa", None, None))
    return jax.shard_map(local, mesh=mesh, in_specs=in_specs, out_specs=out_specs, check_vma=False)
```

```python
import jax
import jax.numpy as jnp
from jax import lax
from jax.sharding import PartitionSpec as P

HEAD = 128
GROUP = 64
REQS = 4


EPS = 1e-06
HIGH = lax.Precision.HIGH


def hi_lo(values):
    high = values.astype(jnp.bfloat16)
    return high, (values - high.astype(jnp.float32)).astype(jnp.bfloat16)


def entering(decay, state, axis, targets, companion):
    count = lax.axis_size(axis)
    rows = state.shape[1]
    high, low = hi_lo(decay)
    packed = jnp.concatenate([state.astype(jnp.bfloat16), high[:, None, :], low[:, None, :]], axis=1)
    every, companion = lax.optimization_barrier((lax.all_gather(packed, axis), companion))
    decays = every[:, :, rows].astype(jnp.float32) + every[:, :, rows + 1].astype(jnp.float32)
    states = every[:, :, :rows].astype(jnp.float32)
    ranks = jnp.arange(count, dtype=jnp.int32)
    results = []
    for target in targets:
        between = (ranks[None, :] > ranks[:, None]) & (ranks[None, :] < target)
        weights = jnp.prod(jnp.where(between[:, :, None, None], decays[None], 1.0), axis=1)
        weights = jnp.where((ranks < target)[:, None, None], weights, 0.0)
        results.append(jnp.sum(weights[..., None] * states, axis=0))
    return results, companion


def route_packets(packets, end_rows, owners, tok_rows, axis):
    count, mine = (lax.axis_size(axis), lax.axis_index(axis))
    left = [(i, (i - 1) % count) for i in range(count)]
    first = lax.ppermute(packets[0], axis, left)
    last = lax.ppermute(packets[-1], axis, [(count - 1, count // 2 - 1)])
    place = ((end_rows - 1) // tok_rows)[1:-1]
    offset = (owners[1:-1] - place) % count

    def shifter(shift):
        pairs = [(i, (i + shift) % count) for i in range(count)]
        return lambda packet: lax.ppermute(packet, axis, pairs) if shift else packet

    branches = [shifter(shift) for shift in range(count)]

    def carry_one(slot, held):
        packet = lax.dynamic_index_in_dim(packets, slot + 1, 0, keepdims=False)
        return held + lax.switch(lax.dynamic_index_in_dim(offset, slot, 0, keepdims=False), branches, packet)

    zero = jnp.zeros_like(first)
    held = jnp.where(owners[0] == mine, first, zero) + jnp.where(owners[-1] == mine, last, zero)
    return lax.fori_loop(0, REQS - 2, carry_one, held)


def rms_rows(matrix, scaling):
    matrix = matrix.astype(jnp.float32)
    rescale = lax.rsqrt(jnp.mean(matrix * matrix, axis=-1, keepdims=True) + EPS)
    return (matrix * rescale * scaling).astype(jnp.bfloat16)


def project(matrix, weight):
    return jnp.dot(matrix, weight, preferred_element_type=jnp.float32)


def widen_rows(shard_part):
    return lax.all_gather(shard_part, "wa", axis=1, tiled=True)


def narrow_sum(partial_terms):
    rows, cols = partial_terms.shape
    count = lax.axis_size("wa")
    pieces = partial_terms.astype(jnp.bfloat16).reshape(rows, count, cols // count)
    got = lax.all_to_all(pieces, "wa", 1, 1)
    return jnp.sum(got.astype(jnp.float32), axis=1)


def local(
    hidden_in,
    request_spans,
    owners,
    mixer_gain,
    query_weight,
    forget_weight,
    input_weight,
    gate_weight,
    forget_bias,
    output_weight,
    swiglu_gain,
    swiglu_gate,
    swiglu_up,
    swiglu_down,
):
    tok_rows = hidden_in.shape[0]
    head_count = query_weight.shape[1] // HEAD
    block_count = tok_rows // GROUP
    gathered = widen_rows(hidden_in)
    normed = rms_rows(gathered, mixer_gain)

    def heads(weight):
        split = weight.reshape(weight.shape[0], head_count, HEAD)
        return jnp.einsum("tk,khd->htd", normed, split, preferred_element_type=jnp.float32)

    queries = jax.nn.silu(heads(query_weight))
    forget_logit = heads(forget_weight) + forget_bias.reshape(head_count, 1, HEAD)
    log_decay = jax.nn.log_sigmoid(forget_logit)
    key_rows = jax.nn.sigmoid(-forget_logit)
    value_rows = heads(input_weight)
    gate_logit = heads(gate_weight)
    first_row = lax.axis_index("seq") * tok_rows
    position = first_row + jnp.arange(tok_rows, dtype=jnp.int32)
    start_rows = request_spans[:, 0]
    end_rows = request_spans[:, 1]
    is_start = jnp.any(position[:, None] == start_rows[None, :], axis=1)
    segment = jnp.sum((start_rows[None, :] <= position[:, None]).astype(jnp.int32), axis=1) - 1
    shape_four = (head_count, block_count, GROUP, HEAD)
    query_parts = queries.reshape(shape_four)
    key_parts = key_rows.reshape(shape_four)
    value_parts = value_rows.reshape(shape_four)
    segment_parts = segment.reshape(block_count, GROUP)
    keep_mask = (1.0 - is_start.astype(jnp.float32)).reshape(block_count, GROUP)
    cum_decay = jnp.cumsum(log_decay.reshape(shape_four), axis=2)
    surviving = jnp.cumprod(keep_mask, axis=1)
    query_tilde = query_parts * jnp.exp(cum_decay)
    key_tilde = key_parts * jnp.exp(-cum_decay)
    offsets = jnp.arange(GROUP, dtype=jnp.int32)
    causal = offsets[:, None] >= offsets[None, :]
    same_doc = causal[None] & (segment_parts[:, :, None] == segment_parts[:, None, :])
    scores = jnp.einsum("hnic,hnjc->hnij", query_tilde, key_tilde, precision=HIGH)
    scores = jnp.where(same_doc[None], scores, 0.0)
    inner_out = jnp.einsum("hnij,hnjd->hnid", scores, value_parts, precision=HIGH)
    tail_mask = (segment_parts == segment_parts[:, -1:]).astype(jnp.float32)
    last_decay = jnp.exp(cum_decay[:, :, -1])
    fresh = last_decay[..., None] * jnp.einsum(
        "hnjc,hnjd->hncd", key_tilde * tail_mask[None, :, :, None], value_parts, precision=HIGH
    )
    shrink = surviving[:, -1][None, :, None] * last_decay
    running = jnp.zeros((head_count, HEAD, HEAD), jnp.float32)
    product = jnp.ones((head_count, HEAD), jnp.float32)
    starts, carries = [], []
    for block in range(block_count):
        starts.append(running)
        carries.append(product)
        running = shrink[:, block, :, None] * running + fresh[:, block]
        product = product * shrink[:, block]
    local_state, device_decay = running, product
    start_state = jnp.stack(starts, axis=1)
    start_decay = jnp.stack(carries, axis=1)

    packets = []
    for request in range(REQS):
        local_end = end_rows[request] - 1 - first_row
        inside = (local_end >= 0) & (local_end < tok_rows)
        end_row = jnp.clip(local_end, 0, tok_rows - 1)
        block_index = end_row // GROUP
        within = end_row % GROUP
        decay_block = lax.dynamic_index_in_dim(cum_decay, block_index, 1, keepdims=False)
        key_block = lax.dynamic_index_in_dim(key_tilde, block_index, 1, keepdims=False)
        value_block = lax.dynamic_index_in_dim(value_parts, block_index, 1, keepdims=False)
        segment_block = lax.dynamic_index_in_dim(segment_parts, block_index, 0, keepdims=False)
        alive_block = lax.dynamic_index_in_dim(surviving, block_index, 0, keepdims=False)
        start_block = lax.dynamic_index_in_dim(start_state, block_index, 1, keepdims=False)
        carry_block = lax.dynamic_index_in_dim(start_decay, block_index, 1, keepdims=False)
        decay_end = lax.dynamic_index_in_dim(decay_block, within, 1, keepdims=False)
        segment_end = lax.dynamic_index_in_dim(segment_block, within, 0, keepdims=False)
        alive_end = lax.dynamic_index_in_dim(alive_block, within, 0, keepdims=False)
        upto_mask = ((offsets <= within) & (segment_block == segment_end)).astype(jnp.float32)
        partial_end = jnp.einsum(
            "hjc,hjd->hcd", key_block * upto_mask[None, :, None], value_block, precision=HIGH
        )
        grow = jnp.exp(decay_end)
        local_part = grow[..., None] * (alive_end * start_block + partial_end)
        high, low = hi_lo(grow * alive_end * carry_block)
        packet = jnp.concatenate(
            [local_part.astype(jnp.bfloat16), high[:, None, :], low[:, None, :]], axis=1
        )
        packets.append(jnp.where(inside, packet, jnp.zeros_like(packet)))
    mine = lax.axis_index("seq")
    owned_source = jnp.sum(jnp.where(owners == mine, (end_rows - 1) // tok_rows, 0))
    (incoming, owned_incoming), packets = entering(
        device_decay, local_state, "seq", (mine, owned_source), jnp.stack(packets)
    )
    held = route_packets(packets, end_rows, owners, tok_rows, "seq")
    held_coeff = held[:, HEAD].astype(jnp.float32) + held[:, HEAD + 1].astype(jnp.float32)
    handed_state = (held[:, :HEAD].astype(jnp.float32) + held_coeff[..., None] * owned_incoming)[None]
    block_state = start_state + start_decay[..., None] * incoming[:, None]
    carried_out = jnp.einsum("hnic,hncd->hnid", query_tilde, block_state, precision=HIGH)
    mixer_out = (inner_out + surviving[None, :, :, None] * carried_out).reshape(
        head_count, tok_rows, HEAD
    )
    rescale = lax.rsqrt(jnp.mean(mixer_out * mixer_out, axis=-1, keepdims=True) + EPS)
    mixed = (mixer_out * rescale * jax.nn.silu(gate_logit)).astype(jnp.bfloat16)
    out_split = output_weight.reshape(head_count, HEAD, output_weight.shape[1])
    partial_terms = jnp.einsum("htd,hdo->to", mixed, out_split, preferred_element_type=jnp.float32)
    residual = (hidden_in.astype(jnp.float32) + narrow_sum(partial_terms)).astype(jnp.bfloat16)
    widened = widen_rows(residual)
    normed_ffn = rms_rows(widened, swiglu_gain)
    hidden = (
        jax.nn.silu(project(normed_ffn, swiglu_gate)) * project(normed_ffn, swiglu_up)
    ).astype(jnp.bfloat16)
    hidden_out = (residual.astype(jnp.float32) + narrow_sum(project(hidden, swiglu_down))).astype(
        jnp.bfloat16
    )
    return (hidden_out, handed_state)


def solution(mesh):
    in_specs = (
        P("seq", "wa"),
        P(),
        P(),
        P(),
        P(None, "wa"),
        P(None, "wa"),
        P(None, "wa"),
        P(None, "wa"),
        P("wa"),
        P("wa", None),
        P(),
        P(None, "wa"),
        P(None, "wa"),
        P("wa", None),
    )
    out_specs = (P("seq", "wa"), P("seq", "wa", None, None))
    return jax.shard_map(local, mesh=mesh, in_specs=in_specs, out_specs=out_specs, check_vma=False)
```

```python
import jax
import jax.numpy as jnp
from jax import lax
from jax.sharding import PartitionSpec as P

HEAD = 128
GROUP = 64
REQS = 4


EPS = 1e-06
HIGH = lax.Precision.HIGH


def hi_lo(values):
    high = values.astype(jnp.bfloat16)
    return high, (values - high.astype(jnp.float32)).astype(jnp.bfloat16)


def pair_up(decay, state, axis):
    mine = lax.axis_index(axis)
    rows = state.shape[1]
    swap = [(i, i ^ 1) for i in range(lax.axis_size(axis))]
    other = lax.ppermute(jnp.concatenate([state, decay[:, None, :]], axis=1), axis, swap)
    second = mine % 2 == 1
    first_decay = jnp.where(second, other[:, rows], decay)
    first_state = jnp.where(second, other[:, :rows], state)
    last_decay = jnp.where(second, decay, other[:, rows])
    last_state = jnp.where(second, state, other[:, :rows])
    pair_decay = first_decay * last_decay
    pair_state = last_decay[..., None] * first_state + last_state
    share = state.shape[0] // 2
    start = (mine % 2) * share
    high, low = hi_lo(lax.dynamic_slice_in_dim(pair_decay, start, share, 0))
    piece = lax.dynamic_slice_in_dim(pair_state, start, share, 0).astype(jnp.bfloat16)
    packed = jnp.concatenate([piece, high[:, None, :], low[:, None, :]], axis=1)
    return first_decay, first_state, packed


def entering(packed, axis, targets):
    count = lax.axis_size(axis)
    share, rows = packed.shape[0], packed.shape[1] - 2
    every = lax.all_gather(packed, axis).reshape(count // 2, 2 * share, rows + 2, packed.shape[2])
    decays = every[:, :, rows].astype(jnp.float32) + every[:, :, rows + 1].astype(jnp.float32)
    states = every[:, :, :rows].astype(jnp.float32)
    ranks = jnp.arange(count // 2, dtype=jnp.int32)
    results = []
    for target in targets:
        between = (ranks[None, :] > ranks[:, None]) & (ranks[None, :] < target)
        weights = jnp.prod(jnp.where(between[:, :, None, None], decays[None], 1.0), axis=1)
        weights = jnp.where((ranks < target)[:, None, None], weights, 0.0)
        results.append(jnp.sum(weights[..., None] * states, axis=0))
    return results


def route_packets(packets, end_rows, owners, tok_rows, axis):
    count, mine = (lax.axis_size(axis), lax.axis_index(axis))
    left = [(i, (i - 1) % count) for i in range(count)]
    first = lax.ppermute(packets[0], axis, left)
    last = lax.ppermute(packets[-1], axis, [(count - 1, count // 2 - 1)])
    place = ((end_rows - 1) // tok_rows)[1:-1]
    offset = (owners[1:-1] - place) % count

    def shifter(shift):
        pairs = [(i, (i + shift) % count) for i in range(count)]
        return lambda packet: lax.ppermute(packet, axis, pairs) if shift else packet

    branches = [shifter(shift) for shift in range(count)]
    middle = [lax.switch(offset[slot], branches, packets[1 + slot]) for slot in range(REQS - 2)]
    zero = jnp.zeros_like(first)
    held = jnp.where(owners[0] == mine, first, zero) + jnp.where(owners[-1] == mine, last, zero)
    for part in middle:
        held = held + part
    return held


def rms_rows(matrix, scaling):
    matrix = matrix.astype(jnp.float32)
    rescale = lax.rsqrt(jnp.mean(matrix * matrix, axis=-1, keepdims=True) + EPS)
    return (matrix * rescale * scaling).astype(jnp.bfloat16)


def project(matrix, weight):
    return jnp.dot(matrix, weight, preferred_element_type=jnp.float32)


def widen_rows(shard_part):
    return lax.all_gather(shard_part, "wa", axis=1, tiled=True)


def narrow_sum(partial_terms):
    rows, cols = partial_terms.shape
    count = lax.axis_size("wa")
    pieces = partial_terms.astype(jnp.bfloat16).reshape(rows, count, cols // count)
    got = lax.all_to_all(pieces, "wa", 1, 1)
    return jnp.sum(got.astype(jnp.float32), axis=1)


def local(
    hidden_in,
    request_spans,
    owners,
    mixer_gain,
    query_weight,
    forget_weight,
    input_weight,
    gate_weight,
    forget_bias,
    output_weight,
    swiglu_gain,
    swiglu_gate,
    swiglu_up,
    swiglu_down,
):
    tok_rows = hidden_in.shape[0]
    head_count = query_weight.shape[1] // HEAD
    block_count = tok_rows // GROUP
    gathered = widen_rows(hidden_in)
    normed = rms_rows(gathered, mixer_gain)

    def heads(weight):
        split = weight.reshape(weight.shape[0], head_count, HEAD)
        return jnp.einsum("tk,khd->htd", normed, split, preferred_element_type=jnp.float32)

    queries = jax.nn.silu(heads(query_weight))
    forget_logit = heads(forget_weight) + forget_bias.reshape(head_count, 1, HEAD)
    log_decay = jax.nn.log_sigmoid(forget_logit)
    key_rows = jax.nn.sigmoid(-forget_logit)
    value_rows = heads(input_weight)
    gate_logit = heads(gate_weight)
    first_row = lax.axis_index("seq") * tok_rows
    position = first_row + jnp.arange(tok_rows, dtype=jnp.int32)
    start_rows = request_spans[:, 0]
    end_rows = request_spans[:, 1]
    is_start = jnp.any(position[:, None] == start_rows[None, :], axis=1)
    segment = jnp.sum((start_rows[None, :] <= position[:, None]).astype(jnp.int32), axis=1) - 1
    shape_four = (head_count, block_count, GROUP, HEAD)
    query_parts = queries.reshape(shape_four)
    key_parts = key_rows.reshape(shape_four)
    value_parts = value_rows.reshape(shape_four)
    segment_parts = segment.reshape(block_count, GROUP)
    keep_mask = (1.0 - is_start.astype(jnp.float32)).reshape(block_count, GROUP)
    cum_decay = jnp.cumsum(log_decay.reshape(shape_four), axis=2)
    surviving = jnp.cumprod(keep_mask, axis=1)
    query_tilde = query_parts * jnp.exp(cum_decay)
    key_tilde = key_parts * jnp.exp(-cum_decay)
    offsets = jnp.arange(GROUP, dtype=jnp.int32)
    causal = offsets[:, None] >= offsets[None, :]
    same_doc = causal[None] & (segment_parts[:, :, None] == segment_parts[:, None, :])
    scores = jnp.einsum("hnic,hnjc->hnij", query_tilde, key_tilde, precision=HIGH)
    scores = jnp.where(same_doc[None], scores, 0.0)
    inner_out = jnp.einsum("hnij,hnjd->hnid", scores, value_parts, precision=HIGH)
    tail_mask = (segment_parts == segment_parts[:, -1:]).astype(jnp.float32)
    last_decay = jnp.exp(cum_decay[:, :, -1])
    fresh = last_decay[..., None] * jnp.einsum(
        "hnjc,hnjd->hncd", key_tilde * tail_mask[None, :, :, None], value_parts, precision=HIGH
    )
    shrink = surviving[:, -1][None, :, None] * last_decay
    running = jnp.zeros((head_count, HEAD, HEAD), jnp.float32)
    product = jnp.ones((head_count, HEAD), jnp.float32)
    starts, carries = [], []
    for block in range(block_count):
        starts.append(running)
        carries.append(product)
        running = shrink[:, block, :, None] * running + fresh[:, block]
        product = product * shrink[:, block]
    local_state, device_decay = running, product
    start_state = jnp.stack(starts, axis=1)
    start_decay = jnp.stack(carries, axis=1)

    first_decay, first_state, packed = pair_up(device_decay, local_state, "seq")
    second = lax.axis_index("seq") % 2 == 1
    packets = []
    for request in range(REQS):
        local_end = end_rows[request] - 1 - first_row
        inside = (local_end >= 0) & (local_end < tok_rows)
        end_row = jnp.clip(local_end, 0, tok_rows - 1)
        block_index = end_row // GROUP
        within = end_row % GROUP
        decay_block = lax.dynamic_index_in_dim(cum_decay, block_index, 1, keepdims=False)
        key_block = lax.dynamic_index_in_dim(key_tilde, block_index, 1, keepdims=False)
        value_block = lax.dynamic_index_in_dim(value_parts, block_index, 1, keepdims=False)
        segment_block = lax.dynamic_index_in_dim(segment_parts, block_index, 0, keepdims=False)
        alive_block = lax.dynamic_index_in_dim(surviving, block_index, 0, keepdims=False)
        start_block = lax.dynamic_index_in_dim(start_state, block_index, 1, keepdims=False)
        carry_block = lax.dynamic_index_in_dim(start_decay, block_index, 1, keepdims=False)
        decay_end = lax.dynamic_index_in_dim(decay_block, within, 1, keepdims=False)
        segment_end = lax.dynamic_index_in_dim(segment_block, within, 0, keepdims=False)
        alive_end = lax.dynamic_index_in_dim(alive_block, within, 0, keepdims=False)
        upto_mask = ((offsets <= within) & (segment_block == segment_end)).astype(jnp.float32)
        partial_end = jnp.einsum(
            "hjc,hjd->hcd", key_block * upto_mask[None, :, None], value_block, precision=HIGH
        )
        grow = jnp.exp(decay_end)
        local_part = grow[..., None] * (alive_end * start_block + partial_end)
        coeff = grow * alive_end * carry_block
        local_part = jnp.where(second, local_part + coeff[..., None] * first_state, local_part)
        high, low = hi_lo(jnp.where(second, coeff * first_decay, coeff))
        packet = jnp.concatenate(
            [local_part.astype(jnp.bfloat16), high[:, None, :], low[:, None, :]], axis=1
        )
        packets.append(jnp.where(inside, packet, jnp.zeros_like(packet)))
    held = route_packets(jnp.stack(packets), end_rows, owners, tok_rows, "seq")
    mine = lax.axis_index("seq")
    owned_source = jnp.sum(jnp.where(owners == mine, (end_rows - 1) // tok_rows, 0))
    chip_prefix, owned_incoming = entering(packed, "seq", (mine // 2, owned_source // 2))
    incoming = jnp.where(second, first_decay[..., None] * chip_prefix + first_state, chip_prefix)
    held_coeff = held[:, HEAD].astype(jnp.float32) + held[:, HEAD + 1].astype(jnp.float32)
    handed_state = (held[:, :HEAD].astype(jnp.float32) + held_coeff[..., None] * owned_incoming)[None]
    block_state = start_state + start_decay[..., None] * incoming[:, None]
    carried_out = jnp.einsum("hnic,hncd->hnid", query_tilde, block_state, precision=HIGH)
    mixer_out = (inner_out + surviving[None, :, :, None] * carried_out).reshape(
        head_count, tok_rows, HEAD
    )
    rescale = lax.rsqrt(jnp.mean(mixer_out * mixer_out, axis=-1, keepdims=True) + EPS)
    mixed = (mixer_out * rescale * jax.nn.silu(gate_logit)).astype(jnp.bfloat16)
    out_split = output_weight.reshape(head_count, HEAD, output_weight.shape[1])
    partial_terms = jnp.einsum("htd,hdo->to", mixed, out_split, preferred_element_type=jnp.float32)
    residual = (hidden_in.astype(jnp.float32) + narrow_sum(partial_terms)).astype(jnp.bfloat16)
    widened = widen_rows(residual)
    normed_ffn = rms_rows(widened, swiglu_gain)
    hidden = (
        jax.nn.silu(project(normed_ffn, swiglu_gate)) * project(normed_ffn, swiglu_up)
    ).astype(jnp.bfloat16)
    hidden_out = (residual.astype(jnp.float32) + narrow_sum(project(hidden, swiglu_down))).astype(
        jnp.bfloat16
    )
    return (hidden_out, handed_state)


def solution(mesh):
    in_specs = (
        P("seq", "wa"),
        P(),
        P(),
        P(),
        P(None, "wa"),
        P(None, "wa"),
        P(None, "wa"),
        P(None, "wa"),
        P("wa"),
        P("wa", None),
        P(),
        P(None, "wa"),
        P(None, "wa"),
        P("wa", None),
    )
    out_specs = (P("seq", "wa"), P("seq", "wa", None, None))
    return jax.shard_map(local, mesh=mesh, in_specs=in_specs, out_specs=out_specs, check_vma=False)
```

```python
import jax
import jax.numpy as jnp
from jax import lax
from jax.sharding import PartitionSpec as P

HEAD = 128
GROUP = 64
REQS = 4


EPS = 1e-06
HIGH = lax.Precision.HIGH


def hi_lo(values):
    high = values.astype(jnp.bfloat16)
    return high, (values - high.astype(jnp.float32)).astype(jnp.bfloat16)


def entering(decay, state, axis, targets):
    count = lax.axis_size(axis)
    rows = state.shape[1]
    high, low = hi_lo(decay)
    packed = jnp.concatenate([state.astype(jnp.bfloat16), high[:, None, :], low[:, None, :]], axis=1)
    every = lax.all_gather(packed, axis)
    decays = every[:, :, rows].astype(jnp.float32) + every[:, :, rows + 1].astype(jnp.float32)
    states = every[:, :, :rows].astype(jnp.float32)
    ranks = jnp.arange(count, dtype=jnp.int32)
    results = []
    for target in targets:
        between = (ranks[None, :] > ranks[:, None]) & (ranks[None, :] < target)
        weights = jnp.prod(jnp.where(between[:, :, None, None], decays[None], 1.0), axis=1)
        weights = jnp.where((ranks < target)[:, None, None], weights, 0.0)
        results.append(jnp.sum(weights[..., None] * states, axis=0))
    return results


def route_packets(packets, end_rows, owners, tok_rows, axis):
    count, mine = (lax.axis_size(axis), lax.axis_index(axis))
    left = [(i, (i - 1) % count) for i in range(count)]
    first = lax.ppermute(packets[0], axis, left)
    last = lax.ppermute(packets[-1], axis, [(count - 1, count // 2 - 1)])
    place = ((end_rows - 1) // tok_rows)[1:-1]
    offset = (owners[1:-1] - place) % count

    def shifter(shift):
        pairs = [(i, (i + shift) % count) for i in range(count)]
        return lambda packet: lax.ppermute(packet, axis, pairs) if shift else packet

    branches = [shifter(shift) for shift in range(count)]
    middle = [lax.switch(offset[slot], branches, packets[1 + slot]) for slot in range(REQS - 2)]
    zero = jnp.zeros_like(first)
    held = jnp.where(owners[0] == mine, first, zero) + jnp.where(owners[-1] == mine, last, zero)
    for part in middle:
        held = held + part
    return held


def rms_rows(matrix, scaling):
    matrix = matrix.astype(jnp.float32)
    rescale = lax.rsqrt(jnp.mean(matrix * matrix, axis=-1, keepdims=True) + EPS)
    return (matrix * rescale * scaling).astype(jnp.bfloat16)


def project(matrix, weight):
    return jnp.dot(matrix, weight, preferred_element_type=jnp.float32)


def widen_rows(shard_part):
    return lax.all_gather(shard_part, "wa", axis=1, tiled=True)


def narrow_sum(partial_terms):
    rows, cols = partial_terms.shape
    count = lax.axis_size("wa")
    pieces = partial_terms.astype(jnp.bfloat16).reshape(rows, count, cols // count)
    got = lax.all_to_all(pieces, "wa", 1, 1)
    return jnp.sum(got.astype(jnp.float32), axis=1)


def local(
    hidden_in,
    request_spans,
    owners,
    mixer_gain,
    query_weight,
    forget_weight,
    input_weight,
    gate_weight,
    forget_bias,
    output_weight,
    swiglu_gain,
    swiglu_gate,
    swiglu_up,
    swiglu_down,
):
    tok_rows = hidden_in.shape[0]
    head_count = query_weight.shape[1] // HEAD
    block_count = tok_rows // GROUP
    half = tok_rows // 2
    count = lax.axis_size("wa")
    lower = hidden_in[half:]
    copies = jnp.broadcast_to(lower[None], (count,) + lower.shape)
    spread = lax.all_to_all(copies, "wa", 0, 0)
    spread = jnp.moveaxis(spread, 0, 1).reshape(tok_rows - half, count * lower.shape[1])
    gathered = jnp.concatenate([widen_rows(hidden_in[:half]), spread], axis=0)
    normed = rms_rows(gathered, mixer_gain)

    def heads(weight):
        split = weight.reshape(weight.shape[0], head_count, HEAD)
        return jnp.einsum("tk,khd->htd", normed, split, preferred_element_type=jnp.float32)

    queries = jax.nn.silu(heads(query_weight))
    forget_logit = heads(forget_weight) + forget_bias.reshape(head_count, 1, HEAD)
    log_decay = jax.nn.log_sigmoid(forget_logit)
    key_rows = jax.nn.sigmoid(-forget_logit)
    value_rows = heads(input_weight)
    gate_logit = heads(gate_weight)
    first_row = lax.axis_index("seq") * tok_rows
    position = first_row + jnp.arange(tok_rows, dtype=jnp.int32)
    start_rows = request_spans[:, 0]
    end_rows = request_spans[:, 1]
    is_start = jnp.any(position[:, None] == start_rows[None, :], axis=1)
    segment = jnp.sum((start_rows[None, :] <= position[:, None]).astype(jnp.int32), axis=1) - 1
    shape_four = (head_count, block_count, GROUP, HEAD)
    query_parts = queries.reshape(shape_four)
    key_parts = key_rows.reshape(shape_four)
    value_parts = value_rows.reshape(shape_four)
    segment_parts = segment.reshape(block_count, GROUP)
    keep_mask = (1.0 - is_start.astype(jnp.float32)).reshape(block_count, GROUP)
    cum_decay = jnp.cumsum(log_decay.reshape(shape_four), axis=2)
    surviving = jnp.cumprod(keep_mask, axis=1)
    query_tilde = query_parts * jnp.exp(cum_decay)
    key_tilde = key_parts * jnp.exp(-cum_decay)
    offsets = jnp.arange(GROUP, dtype=jnp.int32)
    causal = offsets[:, None] >= offsets[None, :]
    same_doc = causal[None] & (segment_parts[:, :, None] == segment_parts[:, None, :])
    scores = jnp.einsum("hnic,hnjc->hnij", query_tilde, key_tilde, precision=HIGH)
    scores = jnp.where(same_doc[None], scores, 0.0)
    inner_out = jnp.einsum("hnij,hnjd->hnid", scores, value_parts, precision=HIGH)
    tail_mask = (segment_parts == segment_parts[:, -1:]).astype(jnp.float32)
    last_decay = jnp.exp(cum_decay[:, :, -1])
    fresh = last_decay[..., None] * jnp.einsum(
        "hnjc,hnjd->hncd", key_tilde * tail_mask[None, :, :, None], value_parts, precision=HIGH
    )
    shrink = surviving[:, -1][None, :, None] * last_decay
    running = jnp.zeros((head_count, HEAD, HEAD), jnp.float32)
    product = jnp.ones((head_count, HEAD), jnp.float32)
    starts, carries = [], []
    for block in range(block_count):
        starts.append(running)
        carries.append(product)
        running = shrink[:, block, :, None] * running + fresh[:, block]
        product = product * shrink[:, block]
    local_state, device_decay = running, product
    start_state = jnp.stack(starts, axis=1)
    start_decay = jnp.stack(carries, axis=1)

    packets = []
    for request in range(REQS):
        local_end = end_rows[request] - 1 - first_row
        inside = (local_end >= 0) & (local_end < tok_rows)
        end_row = jnp.clip(local_end, 0, tok_rows - 1)
        block_index = end_row // GROUP
        within = end_row % GROUP
        decay_block = lax.dynamic_index_in_dim(cum_decay, block_index, 1, keepdims=False)
        key_block = lax.dynamic_index_in_dim(key_tilde, block_index, 1, keepdims=False)
        value_block = lax.dynamic_index_in_dim(value_parts, block_index, 1, keepdims=False)
        segment_block = lax.dynamic_index_in_dim(segment_parts, block_index, 0, keepdims=False)
        alive_block = lax.dynamic_index_in_dim(surviving, block_index, 0, keepdims=False)
        start_block = lax.dynamic_index_in_dim(start_state, block_index, 1, keepdims=False)
        carry_block = lax.dynamic_index_in_dim(start_decay, block_index, 1, keepdims=False)
        decay_end = lax.dynamic_index_in_dim(decay_block, within, 1, keepdims=False)
        segment_end = lax.dynamic_index_in_dim(segment_block, within, 0, keepdims=False)
        alive_end = lax.dynamic_index_in_dim(alive_block, within, 0, keepdims=False)
        upto_mask = ((offsets <= within) & (segment_block == segment_end)).astype(jnp.float32)
        partial_end = jnp.einsum(
            "hjc,hjd->hcd", key_block * upto_mask[None, :, None], value_block, precision=HIGH
        )
        grow = jnp.exp(decay_end)
        local_part = grow[..., None] * (alive_end * start_block + partial_end)
        high, low = hi_lo(grow * alive_end * carry_block)
        packet = jnp.concatenate(
            [local_part.astype(jnp.bfloat16), high[:, None, :], low[:, None, :]], axis=1
        )
        packets.append(jnp.where(inside, packet, jnp.zeros_like(packet)))
    held = route_packets(jnp.stack(packets), end_rows, owners, tok_rows, "seq")
    mine = lax.axis_index("seq")
    owned_source = jnp.sum(jnp.where(owners == mine, (end_rows - 1) // tok_rows, 0))
    incoming, owned_incoming = entering(device_decay, local_state, "seq", (mine, owned_source))
    held_coeff = held[:, HEAD].astype(jnp.float32) + held[:, HEAD + 1].astype(jnp.float32)
    handed_state = (held[:, :HEAD].astype(jnp.float32) + held_coeff[..., None] * owned_incoming)[None]
    block_state = start_state + start_decay[..., None] * incoming[:, None]
    carried_out = jnp.einsum("hnic,hncd->hnid", query_tilde, block_state, precision=HIGH)
    mixer_out = (inner_out + surviving[None, :, :, None] * carried_out).reshape(
        head_count, tok_rows, HEAD
    )
    rescale = lax.rsqrt(jnp.mean(mixer_out * mixer_out, axis=-1, keepdims=True) + EPS)
    mixed = (mixer_out * rescale * jax.nn.silu(gate_logit)).astype(jnp.bfloat16)
    out_split = output_weight.reshape(head_count, HEAD, output_weight.shape[1])
    partial_terms = jnp.einsum("htd,hdo->to", mixed, out_split, preferred_element_type=jnp.float32)
    residual = (hidden_in.astype(jnp.float32) + narrow_sum(partial_terms)).astype(jnp.bfloat16)
    widened = widen_rows(residual)
    normed_ffn = rms_rows(widened, swiglu_gain)
    hidden = (
        jax.nn.silu(project(normed_ffn, swiglu_gate)) * project(normed_ffn, swiglu_up)
    ).astype(jnp.bfloat16)
    hidden_out = (residual.astype(jnp.float32) + narrow_sum(project(hidden, swiglu_down))).astype(
        jnp.bfloat16
    )
    return (hidden_out, handed_state)


def solution(mesh):
    in_specs = (
        P("seq", "wa"),
        P(),
        P(),
        P(),
        P(None, "wa"),
        P(None, "wa"),
        P(None, "wa"),
        P(None, "wa"),
        P("wa"),
        P("wa", None),
        P(),
        P(None, "wa"),
        P(None, "wa"),
        P("wa", None),
    )
    out_specs = (P("seq", "wa"), P("seq", "wa", None, None))
    return jax.shard_map(local, mesh=mesh, in_specs=in_specs, out_specs=out_specs, check_vma=False)
```

```python
import jax
import jax.numpy as jnp
from jax import lax
from jax.sharding import PartitionSpec as P

HEAD = 128
GROUP = 64
REQS = 4


EPS = 1e-06
HIGH = lax.Precision.HIGH


def hi_lo(values):
    high = values.astype(jnp.bfloat16)
    return high, (values - high.astype(jnp.float32)).astype(jnp.bfloat16)


def entering(decay, state, axis, targets):
    count = lax.axis_size(axis)
    rows = state.shape[1]
    high, low = hi_lo(decay)
    packed = jnp.concatenate([state.astype(jnp.bfloat16), high[:, None, :], low[:, None, :]], axis=1)
    every = lax.all_gather(packed, axis)
    decays = every[:, :, rows].astype(jnp.float32) + every[:, :, rows + 1].astype(jnp.float32)
    states = every[:, :, :rows].astype(jnp.float32)
    ranks = jnp.arange(count, dtype=jnp.int32)
    results = []
    for target in targets:
        between = (ranks[None, :] > ranks[:, None]) & (ranks[None, :] < target)
        weights = jnp.prod(jnp.where(between[:, :, None, None], decays[None], 1.0), axis=1)
        weights = jnp.where((ranks < target)[:, None, None], weights, 0.0)
        results.append(jnp.sum(weights[..., None] * states, axis=0))
    return results


def route_packets(packets, end_rows, owners, tok_rows, axis):
    count, mine = (lax.axis_size(axis), lax.axis_index(axis))
    left = [(i, (i - 1) % count) for i in range(count)]
    first = lax.ppermute(packets[0], axis, left)
    last = lax.ppermute(packets[-1], axis, [(count - 1, count // 2 - 1)])
    place = ((end_rows - 1) // tok_rows)[1:-1]
    offset = (owners[1:-1] - place) % count

    def shifter(shift):
        pairs = [(i, (i + shift) % count) for i in range(count)]
        return lambda packet: lax.ppermute(packet, axis, pairs) if shift else packet

    branches = [shifter(shift) for shift in range(count)]
    middle = [lax.switch(offset[slot], branches, packets[1 + slot]) for slot in range(REQS - 2)]
    zero = jnp.zeros_like(first)
    held = jnp.where(owners[0] == mine, first, zero) + jnp.where(owners[-1] == mine, last, zero)
    for part in middle:
        held = held + part
    return held


def rms_rows(matrix, scaling):
    matrix = matrix.astype(jnp.float32)
    rescale = lax.rsqrt(jnp.mean(matrix * matrix, axis=-1, keepdims=True) + EPS)
    return (matrix * rescale * scaling).astype(jnp.bfloat16)


def project(matrix, weight):
    return jnp.dot(matrix, weight, preferred_element_type=jnp.float32)


def widen_rows(shard_part):
    return lax.all_gather(shard_part, "wa", axis=1, tiled=True)


def narrow_sum(partial_terms):
    rows, cols = partial_terms.shape
    count = lax.axis_size("wa")
    pieces = partial_terms.astype(jnp.bfloat16).reshape(rows, count, cols // count)
    got = lax.all_to_all(pieces, "wa", 1, 1)
    return jnp.sum(got.astype(jnp.float32), axis=1)


def local(
    hidden_in,
    request_spans,
    owners,
    mixer_gain,
    query_weight,
    forget_weight,
    input_weight,
    gate_weight,
    forget_bias,
    output_weight,
    swiglu_gain,
    swiglu_gate,
    swiglu_up,
    swiglu_down,
):
    tok_rows = hidden_in.shape[0]
    head_count = query_weight.shape[1] // HEAD
    block_count = tok_rows // GROUP
    half = tok_rows // 2
    count = lax.axis_size("wa")
    lower = hidden_in[half:]
    copies = jnp.broadcast_to(lower[None], (count,) + lower.shape)
    spread = lax.all_to_all(copies, "wa", 0, 0)
    spread = jnp.moveaxis(spread, 0, 1).reshape(tok_rows - half, count * lower.shape[1])
    gathered = jnp.concatenate([widen_rows(hidden_in[:half]), spread], axis=0)
    normed = rms_rows(gathered, mixer_gain)

    def heads(weight):
        split = weight.reshape(weight.shape[0], head_count, HEAD)
        return jnp.einsum("tk,khd->htd", normed, split, preferred_element_type=jnp.float32)

    queries = jax.nn.silu(heads(query_weight))
    forget_logit = heads(forget_weight) + forget_bias.reshape(head_count, 1, HEAD)
    log_decay = jax.nn.log_sigmoid(forget_logit)
    key_rows = jax.nn.sigmoid(-forget_logit)
    value_rows = heads(input_weight)
    gate_logit = heads(gate_weight)
    first_row = lax.axis_index("seq") * tok_rows
    position = first_row + jnp.arange(tok_rows, dtype=jnp.int32)
    start_rows = request_spans[:, 0]
    end_rows = request_spans[:, 1]
    is_start = jnp.any(position[:, None] == start_rows[None, :], axis=1)
    segment = jnp.sum((start_rows[None, :] <= position[:, None]).astype(jnp.int32), axis=1) - 1
    shape_four = (head_count, block_count, GROUP, HEAD)
    query_parts = queries.reshape(shape_four)
    key_parts = key_rows.reshape(shape_four)
    value_parts = value_rows.reshape(shape_four)
    segment_parts = segment.reshape(block_count, GROUP)
    keep_mask = (1.0 - is_start.astype(jnp.float32)).reshape(block_count, GROUP)
    cum_decay = jnp.cumsum(log_decay.reshape(shape_four), axis=2)
    surviving = jnp.cumprod(keep_mask, axis=1)
    query_tilde = query_parts * jnp.exp(cum_decay)
    key_tilde = key_parts * jnp.exp(-cum_decay)
    offsets = jnp.arange(GROUP, dtype=jnp.int32)
    causal = offsets[:, None] >= offsets[None, :]
    same_doc = causal[None] & (segment_parts[:, :, None] == segment_parts[:, None, :])
    scores = jnp.einsum("hnic,hnjc->hnij", query_tilde, key_tilde, precision=HIGH)
    scores = jnp.where(same_doc[None], scores, 0.0)
    inner_out = jnp.einsum("hnij,hnjd->hnid", scores, value_parts, precision=HIGH)
    tail_mask = (segment_parts == segment_parts[:, -1:]).astype(jnp.float32)
    last_decay = jnp.exp(cum_decay[:, :, -1])
    fresh = last_decay[..., None] * jnp.einsum(
        "hnjc,hnjd->hncd", key_tilde * tail_mask[None, :, :, None], value_parts, precision=HIGH
    )
    shrink = surviving[:, -1][None, :, None] * last_decay
    running = jnp.zeros((head_count, HEAD, HEAD), jnp.float32)
    product = jnp.ones((head_count, HEAD), jnp.float32)
    starts, carries = [], []
    for block in range(block_count):
        starts.append(running)
        carries.append(product)
        running = shrink[:, block, :, None] * running + fresh[:, block]
        product = product * shrink[:, block]
    local_state, device_decay = running, product
    start_state = jnp.stack(starts, axis=1)
    start_decay = jnp.stack(carries, axis=1)

    packets = []
    for request in range(REQS):
        local_end = end_rows[request] - 1 - first_row
        inside = (local_end >= 0) & (local_end < tok_rows)
        end_row = jnp.clip(local_end, 0, tok_rows - 1)
        block_index = end_row // GROUP
        within = end_row % GROUP
        decay_block = lax.dynamic_index_in_dim(cum_decay, block_index, 1, keepdims=False)
        key_block = lax.dynamic_index_in_dim(key_tilde, block_index, 1, keepdims=False)
        value_block = lax.dynamic_index_in_dim(value_parts, block_index, 1, keepdims=False)
        segment_block = lax.dynamic_index_in_dim(segment_parts, block_index, 0, keepdims=False)
        alive_block = lax.dynamic_index_in_dim(surviving, block_index, 0, keepdims=False)
        start_block = lax.dynamic_index_in_dim(start_state, block_index, 1, keepdims=False)
        carry_block = lax.dynamic_index_in_dim(start_decay, block_index, 1, keepdims=False)
        decay_end = lax.dynamic_index_in_dim(decay_block, within, 1, keepdims=False)
        segment_end = lax.dynamic_index_in_dim(segment_block, within, 0, keepdims=False)
        alive_end = lax.dynamic_index_in_dim(alive_block, within, 0, keepdims=False)
        upto_mask = ((offsets <= within) & (segment_block == segment_end)).astype(jnp.float32)
        partial_end = jnp.einsum(
            "hjc,hjd->hcd", key_block * upto_mask[None, :, None], value_block, precision=HIGH
        )
        grow = jnp.exp(decay_end)
        local_part = grow[..., None] * (alive_end * start_block + partial_end)
        high, low = hi_lo(grow * alive_end * carry_block)
        packet = jnp.concatenate(
            [local_part.astype(jnp.bfloat16), high[:, None, :], low[:, None, :]], axis=1
        )
        packets.append(jnp.where(inside, packet, jnp.zeros_like(packet)))
    held = route_packets(jnp.stack(packets), end_rows, owners, tok_rows, "seq")
    mine = lax.axis_index("seq")
    owned_source = jnp.sum(jnp.where(owners == mine, (end_rows - 1) // tok_rows, 0))
    incoming, owned_incoming = entering(device_decay, local_state, "seq", (mine, owned_source))
    held_coeff = held[:, HEAD].astype(jnp.float32) + held[:, HEAD + 1].astype(jnp.float32)
    handed_state = (held[:, :HEAD].astype(jnp.float32) + held_coeff[..., None] * owned_incoming)[None]
    block_state = start_state + start_decay[..., None] * incoming[:, None]
    carried_out = jnp.einsum("hnic,hncd->hnid", query_tilde, block_state, precision=HIGH)
    mixer_out = (inner_out + surviving[None, :, :, None] * carried_out).reshape(
        head_count, tok_rows, HEAD
    )
    rescale = lax.rsqrt(jnp.mean(mixer_out * mixer_out, axis=-1, keepdims=True) + EPS)
    mixed = (mixer_out * rescale * jax.nn.silu(gate_logit)).astype(jnp.bfloat16)
    out_split = output_weight.reshape(head_count, HEAD, output_weight.shape[1])
    partial_terms = jnp.einsum("htd,hdo->to", mixed, out_split, preferred_element_type=jnp.float32)
    summed = lax.psum(partial_terms.astype(jnp.bfloat16), "wa")
    widened = (gathered.astype(jnp.float32) + summed.astype(jnp.float32)).astype(jnp.bfloat16)
    columns = hidden_in.shape[1]
    residual = lax.dynamic_slice_in_dim(widened, lax.axis_index("wa") * columns, columns, 1)
    normed_ffn = rms_rows(widened, swiglu_gain)
    hidden = (
        jax.nn.silu(project(normed_ffn, swiglu_gate)) * project(normed_ffn, swiglu_up)
    ).astype(jnp.bfloat16)
    hidden_out = (residual.astype(jnp.float32) + narrow_sum(project(hidden, swiglu_down))).astype(
        jnp.bfloat16
    )
    return (hidden_out, handed_state)


def solution(mesh):
    in_specs = (
        P("seq", "wa"),
        P(),
        P(),
        P(),
        P(None, "wa"),
        P(None, "wa"),
        P(None, "wa"),
        P(None, "wa"),
        P("wa"),
        P("wa", None),
        P(),
        P(None, "wa"),
        P(None, "wa"),
        P("wa", None),
    )
    out_specs = (P("seq", "wa"), P("seq", "wa", None, None))
    return jax.shard_map(local, mesh=mesh, in_specs=in_specs, out_specs=out_specs, check_vma=False)
```

```python
import jax
import jax.numpy as jnp
from jax import lax
from jax.sharding import PartitionSpec as P

HEAD = 128
GROUP = 64
REQS = 4


EPS = 1e-06
HIGH = lax.Precision.HIGH


def hi_lo(values):
    high = values.astype(jnp.bfloat16)
    return high, (values - high.astype(jnp.float32)).astype(jnp.bfloat16)


def entering(decay, state, axis):
    rows = state.shape[1]
    high, low = hi_lo(decay)
    packed = jnp.concatenate([state.astype(jnp.bfloat16), high[:, None, :], low[:, None, :]], axis=1)
    return lax.all_gather(packed, axis)


def prefix_at(every, target):
    count, rows = every.shape[0], every.shape[2] - 2
    decays = every[:, :, rows].astype(jnp.float32) + every[:, :, rows + 1].astype(jnp.float32)
    states = every[:, :, :rows].astype(jnp.float32)
    ranks = jnp.arange(count, dtype=jnp.int32)
    between = (ranks[None, :] > ranks[:, None]) & (ranks[None, :] < target)
    weights = jnp.prod(jnp.where(between[:, :, None, None], decays[None], 1.0), axis=1)
    weights = jnp.where((ranks < target)[:, None, None], weights, 0.0)
    return jnp.sum(weights[..., None] * states, axis=0)


def route_packets(packets, end_rows, owners, tok_rows, axis):
    count, mine = (lax.axis_size(axis), lax.axis_index(axis))
    left = [(i, (i - 1) % count) for i in range(count)]
    first = lax.ppermute(packets[0], axis, left)
    last = lax.ppermute(packets[-1], axis, [(count - 1, count // 2 - 1)])
    place = ((end_rows - 1) // tok_rows)[1:-1]
    offset = (owners[1:-1] - place) % count

    def shifter(shift):
        pairs = [(i, (i + shift) % count) for i in range(count)]
        return lambda packet: lax.ppermute(packet, axis, pairs) if shift else packet

    branches = [shifter(shift) for shift in range(count)]
    middle = [lax.switch(offset[slot], branches, packets[1 + slot]) for slot in range(REQS - 2)]
    zero = jnp.zeros_like(first)
    held = jnp.where(owners[0] == mine, first, zero) + jnp.where(owners[-1] == mine, last, zero)
    for part in middle:
        held = held + part
    return held


def rms_rows(matrix, scaling):
    matrix = matrix.astype(jnp.float32)
    rescale = lax.rsqrt(jnp.mean(matrix * matrix, axis=-1, keepdims=True) + EPS)
    return (matrix * rescale * scaling).astype(jnp.bfloat16)


def project(matrix, weight):
    return jnp.dot(matrix, weight, preferred_element_type=jnp.float32)


def widen_rows(shard_part):
    return lax.all_gather(shard_part, "wa", axis=1, tiled=True)


def narrow_sum(partial_terms):
    rows, cols = partial_terms.shape
    count = lax.axis_size("wa")
    pieces = partial_terms.astype(jnp.bfloat16).reshape(rows, count, cols // count)
    got = lax.all_to_all(pieces, "wa", 1, 1)
    return jnp.sum(got.astype(jnp.float32), axis=1)


def local(
    hidden_in,
    request_spans,
    owners,
    mixer_gain,
    query_weight,
    forget_weight,
    input_weight,
    gate_weight,
    forget_bias,
    output_weight,
    swiglu_gain,
    swiglu_gate,
    swiglu_up,
    swiglu_down,
):
    tok_rows = hidden_in.shape[0]
    head_count = query_weight.shape[1] // HEAD
    block_count = tok_rows // GROUP
    half = tok_rows // 2
    count = lax.axis_size("wa")
    lower = hidden_in[half:]
    copies = jnp.broadcast_to(lower[None], (count,) + lower.shape)
    spread = lax.all_to_all(copies, "wa", 0, 0)
    spread = jnp.moveaxis(spread, 0, 1).reshape(tok_rows - half, count * lower.shape[1])
    gathered = jnp.concatenate([widen_rows(hidden_in[:half]), spread], axis=0)
    normed = rms_rows(gathered, mixer_gain)

    def heads(weight):
        split = weight.reshape(weight.shape[0], head_count, HEAD)
        return jnp.einsum("tk,khd->htd", normed, split, preferred_element_type=jnp.float32)

    queries = jax.nn.silu(heads(query_weight))
    forget_logit = heads(forget_weight) + forget_bias.reshape(head_count, 1, HEAD)
    log_decay = jax.nn.log_sigmoid(forget_logit)
    key_rows = jax.nn.sigmoid(-forget_logit)
    value_rows = heads(input_weight)
    gate_logit = heads(gate_weight)
    first_row = lax.axis_index("seq") * tok_rows
    position = first_row + jnp.arange(tok_rows, dtype=jnp.int32)
    start_rows = request_spans[:, 0]
    end_rows = request_spans[:, 1]
    is_start = jnp.any(position[:, None] == start_rows[None, :], axis=1)
    segment = jnp.sum((start_rows[None, :] <= position[:, None]).astype(jnp.int32), axis=1) - 1
    shape_four = (head_count, block_count, GROUP, HEAD)
    query_parts = queries.reshape(shape_four)
    key_parts = key_rows.reshape(shape_four)
    value_parts = value_rows.reshape(shape_four)
    segment_parts = segment.reshape(block_count, GROUP)
    keep_mask = (1.0 - is_start.astype(jnp.float32)).reshape(block_count, GROUP)
    cum_decay = jnp.cumsum(log_decay.reshape(shape_four), axis=2)
    surviving = jnp.cumprod(keep_mask, axis=1)
    query_tilde = query_parts * jnp.exp(cum_decay)
    key_tilde = key_parts * jnp.exp(-cum_decay)
    offsets = jnp.arange(GROUP, dtype=jnp.int32)
    causal = offsets[:, None] >= offsets[None, :]
    same_doc = causal[None] & (segment_parts[:, :, None] == segment_parts[:, None, :])
    scores = jnp.einsum("hnic,hnjc->hnij", query_tilde, key_tilde, precision=HIGH)
    scores = jnp.where(same_doc[None], scores, 0.0)
    inner_out = jnp.einsum("hnij,hnjd->hnid", scores, value_parts, precision=HIGH)
    tail_mask = (segment_parts == segment_parts[:, -1:]).astype(jnp.float32)
    last_decay = jnp.exp(cum_decay[:, :, -1])
    fresh = last_decay[..., None] * jnp.einsum(
        "hnjc,hnjd->hncd", key_tilde * tail_mask[None, :, :, None], value_parts, precision=HIGH
    )
    shrink = surviving[:, -1][None, :, None] * last_decay
    running = jnp.zeros((head_count, HEAD, HEAD), jnp.float32)
    product = jnp.ones((head_count, HEAD), jnp.float32)
    starts, carries = [], []
    for block in range(block_count):
        starts.append(running)
        carries.append(product)
        running = shrink[:, block, :, None] * running + fresh[:, block]
        product = product * shrink[:, block]
    local_state, device_decay = running, product
    start_state = jnp.stack(starts, axis=1)
    start_decay = jnp.stack(carries, axis=1)

    packets = []
    for request in range(REQS):
        local_end = end_rows[request] - 1 - first_row
        inside = (local_end >= 0) & (local_end < tok_rows)
        end_row = jnp.clip(local_end, 0, tok_rows - 1)
        block_index = end_row // GROUP
        within = end_row % GROUP
        decay_block = lax.dynamic_index_in_dim(cum_decay, block_index, 1, keepdims=False)
        key_block = lax.dynamic_index_in_dim(key_tilde, block_index, 1, keepdims=False)
        value_block = lax.dynamic_index_in_dim(value_parts, block_index, 1, keepdims=False)
        segment_block = lax.dynamic_index_in_dim(segment_parts, block_index, 0, keepdims=False)
        alive_block = lax.dynamic_index_in_dim(surviving, block_index, 0, keepdims=False)
        start_block = lax.dynamic_index_in_dim(start_state, block_index, 1, keepdims=False)
        carry_block = lax.dynamic_index_in_dim(start_decay, block_index, 1, keepdims=False)
        decay_end = lax.dynamic_index_in_dim(decay_block, within, 1, keepdims=False)
        segment_end = lax.dynamic_index_in_dim(segment_block, within, 0, keepdims=False)
        alive_end = lax.dynamic_index_in_dim(alive_block, within, 0, keepdims=False)
        upto_mask = ((offsets <= within) & (segment_block == segment_end)).astype(jnp.float32)
        partial_end = jnp.einsum(
            "hjc,hjd->hcd", key_block * upto_mask[None, :, None], value_block, precision=HIGH
        )
        grow = jnp.exp(decay_end)
        local_part = grow[..., None] * (alive_end * start_block + partial_end)
        high, low = hi_lo(grow * alive_end * carry_block)
        packet = jnp.concatenate(
            [local_part.astype(jnp.bfloat16), high[:, None, :], low[:, None, :]], axis=1
        )
        packets.append(jnp.where(inside, packet, jnp.zeros_like(packet)))
    held = route_packets(jnp.stack(packets), end_rows, owners, tok_rows, "seq")
    mine = lax.axis_index("seq")
    owned_source = jnp.sum(jnp.where(owners == mine, (end_rows - 1) // tok_rows, 0))
    every = entering(device_decay, local_state, "seq")
    incoming = prefix_at(every, mine)
    block_state = start_state + start_decay[..., None] * incoming[:, None]
    carried_out = jnp.einsum("hnic,hncd->hnid", query_tilde, block_state, precision=HIGH)
    mixer_out = (inner_out + surviving[None, :, :, None] * carried_out).reshape(
        head_count, tok_rows, HEAD
    )
    rescale = lax.rsqrt(jnp.mean(mixer_out * mixer_out, axis=-1, keepdims=True) + EPS)
    mixed = (mixer_out * rescale * jax.nn.silu(gate_logit)).astype(jnp.bfloat16)
    out_split = output_weight.reshape(head_count, HEAD, output_weight.shape[1])
    partial_terms = jnp.einsum("htd,hdo->to", mixed, out_split, preferred_element_type=jnp.float32)
    every, partial_terms = lax.optimization_barrier((every, partial_terms))
    owned_incoming = prefix_at(every, owned_source)
    held_coeff = held[:, HEAD].astype(jnp.float32) + held[:, HEAD + 1].astype(jnp.float32)
    handed_state = (held[:, :HEAD].astype(jnp.float32) + held_coeff[..., None] * owned_incoming)[None]
    residual = (hidden_in.astype(jnp.float32) + narrow_sum(partial_terms)).astype(jnp.bfloat16)
    widened = widen_rows(residual)
    normed_ffn = rms_rows(widened, swiglu_gain)
    hidden = (
        jax.nn.silu(project(normed_ffn, swiglu_gate)) * project(normed_ffn, swiglu_up)
    ).astype(jnp.bfloat16)
    hidden_out = (residual.astype(jnp.float32) + narrow_sum(project(hidden, swiglu_down))).astype(
        jnp.bfloat16
    )
    return (hidden_out, handed_state)


def solution(mesh):
    in_specs = (
        P("seq", "wa"),
        P(),
        P(),
        P(),
        P(None, "wa"),
        P(None, "wa"),
        P(None, "wa"),
        P(None, "wa"),
        P("wa"),
        P("wa", None),
        P(),
        P(None, "wa"),
        P(None, "wa"),
        P("wa", None),
    )
    out_specs = (P("seq", "wa"), P("seq", "wa", None, None))
    return jax.shard_map(local, mesh=mesh, in_specs=in_specs, out_specs=out_specs, check_vma=False)
```

```python
import jax
import jax.numpy as jnp
from jax import lax
from jax.sharding import PartitionSpec as P

HEAD = 128
GROUP = 64
REQS = 4


EPS = 1e-06
HIGH = lax.Precision.HIGH


def hi_lo(values):
    high = values.astype(jnp.bfloat16)
    return high, (values - high.astype(jnp.float32)).astype(jnp.bfloat16)


def entering(decay, state, axis, targets):
    count = lax.axis_size(axis)
    rows = state.shape[1]
    high, low = hi_lo(decay)
    packed = jnp.concatenate([state.astype(jnp.bfloat16), high[:, None, :], low[:, None, :]], axis=1)
    every = lax.all_gather(packed, axis)
    decays = every[:, :, rows].astype(jnp.float32) + every[:, :, rows + 1].astype(jnp.float32)
    states = every[:, :, :rows].astype(jnp.float32)
    ranks = jnp.arange(count, dtype=jnp.int32)
    results = []
    for target in targets:
        between = (ranks[None, :] > ranks[:, None]) & (ranks[None, :] < target)
        weights = jnp.prod(jnp.where(between[:, :, None, None], decays[None], 1.0), axis=1)
        weights = jnp.where((ranks < target)[:, None, None], weights, 0.0)
        results.append(jnp.sum(weights[..., None] * states, axis=0))
    return results


def route_packets(packets, end_rows, owners, tok_rows, axis):
    count, mine = (lax.axis_size(axis), lax.axis_index(axis))
    left = [(i, (i - 1) % count) for i in range(count)]
    first = lax.ppermute(packets[0], axis, left)
    last = lax.ppermute(packets[-1], axis, [(count - 1, count // 2 - 1)])
    place = ((end_rows - 1) // tok_rows)[1:-1]
    offset = (owners[1:-1] - place) % count

    def shifter(shift):
        pairs = [(i, (i + shift) % count) for i in range(count)]
        return lambda packet: lax.ppermute(packet, axis, pairs) if shift else packet

    branches = [shifter(shift) for shift in range(count)]
    middle = [lax.switch(offset[slot], branches, packets[1 + slot]) for slot in range(REQS - 2)]
    zero = jnp.zeros_like(first)
    held = jnp.where(owners[0] == mine, first, zero) + jnp.where(owners[-1] == mine, last, zero)
    for part in middle:
        held = held + part
    return held


def rms_rows(matrix, scaling):
    matrix = matrix.astype(jnp.float32)
    rescale = lax.rsqrt(jnp.mean(matrix * matrix, axis=-1, keepdims=True) + EPS)
    return (matrix * rescale * scaling).astype(jnp.bfloat16)


def project(matrix, weight):
    return jnp.dot(matrix, weight, preferred_element_type=jnp.float32)


def widen_rows(shard_part):
    return lax.all_gather(shard_part, "wa", axis=1, tiled=True)


def narrow_sum(partial_terms):
    rows, cols = partial_terms.shape
    count = lax.axis_size("wa")
    pieces = partial_terms.astype(jnp.bfloat16).reshape(rows, count, cols // count)
    got = lax.all_to_all(pieces, "wa", 1, 1)
    return jnp.sum(got.astype(jnp.float32), axis=1)


def local(
    hidden_in,
    request_spans,
    owners,
    mixer_gain,
    query_weight,
    forget_weight,
    input_weight,
    gate_weight,
    forget_bias,
    output_weight,
    swiglu_gain,
    swiglu_gate,
    swiglu_up,
    swiglu_down,
):
    tok_rows = hidden_in.shape[0]
    head_count = query_weight.shape[1] // HEAD
    block_count = tok_rows // GROUP
    half = tok_rows // 2
    count = lax.axis_size("wa")
    lower = hidden_in[half:]
    copies = jnp.broadcast_to(lower[None], (count,) + lower.shape)
    spread = lax.all_to_all(copies, "wa", 0, 0)
    spread = jnp.moveaxis(spread, 0, 1).reshape(tok_rows - half, count * lower.shape[1])
    gathered = jnp.concatenate([widen_rows(hidden_in[:half]), spread], axis=0)
    normed = rms_rows(gathered, mixer_gain)

    def heads(weight):
        split = weight.reshape(weight.shape[0], head_count, HEAD)
        return jnp.einsum("tk,khd->htd", normed, split, preferred_element_type=jnp.float32)

    queries = jax.nn.silu(heads(query_weight))
    forget_logit = heads(forget_weight) + forget_bias.reshape(head_count, 1, HEAD)
    log_decay = jax.nn.log_sigmoid(forget_logit)
    key_rows = jax.nn.sigmoid(-forget_logit)
    value_rows = heads(input_weight)
    gate_logit = heads(gate_weight)
    first_row = lax.axis_index("seq") * tok_rows
    position = first_row + jnp.arange(tok_rows, dtype=jnp.int32)
    start_rows = request_spans[:, 0]
    end_rows = request_spans[:, 1]
    is_start = jnp.any(position[:, None] == start_rows[None, :], axis=1)
    segment = jnp.sum((start_rows[None, :] <= position[:, None]).astype(jnp.int32), axis=1) - 1
    shape_four = (head_count, block_count, GROUP, HEAD)
    query_parts = queries.reshape(shape_four)
    key_parts = key_rows.reshape(shape_four)
    value_parts = value_rows.reshape(shape_four)
    segment_parts = segment.reshape(block_count, GROUP)
    keep_mask = (1.0 - is_start.astype(jnp.float32)).reshape(block_count, GROUP)
    cum_decay = jnp.cumsum(log_decay.reshape(shape_four), axis=2)
    surviving = jnp.cumprod(keep_mask, axis=1)
    query_tilde = query_parts * jnp.exp(cum_decay)
    key_tilde = key_parts * jnp.exp(-cum_decay)
    offsets = jnp.arange(GROUP, dtype=jnp.int32)
    causal = offsets[:, None] >= offsets[None, :]
    same_doc = causal[None] & (segment_parts[:, :, None] == segment_parts[:, None, :])
    scores = jnp.einsum("hnic,hnjc->hnij", query_tilde, key_tilde, precision=HIGH)
    scores = jnp.where(same_doc[None], scores, 0.0)
    inner_out = jnp.einsum("hnij,hnjd->hnid", scores, value_parts, precision=HIGH)
    tail_mask = (segment_parts == segment_parts[:, -1:]).astype(jnp.float32)
    last_decay = jnp.exp(cum_decay[:, :, -1])
    fresh = last_decay[..., None] * jnp.einsum(
        "hnjc,hnjd->hncd", key_tilde * tail_mask[None, :, :, None], value_parts, precision=HIGH
    )
    shrink = surviving[:, -1][None, :, None] * last_decay
    running = jnp.zeros((head_count, HEAD, HEAD), jnp.float32)
    product = jnp.ones((head_count, HEAD), jnp.float32)
    starts, carries = [], []
    for block in range(block_count):
        starts.append(running)
        carries.append(product)
        running = shrink[:, block, :, None] * running + fresh[:, block]
        product = product * shrink[:, block]
    local_state, device_decay = running, product
    start_state = jnp.stack(starts, axis=1)
    start_decay = jnp.stack(carries, axis=1)

    packets = []
    for request in range(REQS):
        local_end = end_rows[request] - 1 - first_row
        inside = (local_end >= 0) & (local_end < tok_rows)
        end_row = jnp.clip(local_end, 0, tok_rows - 1)
        block_index = end_row // GROUP
        within = end_row % GROUP
        decay_block = lax.dynamic_index_in_dim(cum_decay, block_index, 1, keepdims=False)
        key_block = lax.dynamic_index_in_dim(key_tilde, block_index, 1, keepdims=False)
        value_block = lax.dynamic_index_in_dim(value_parts, block_index, 1, keepdims=False)
        segment_block = lax.dynamic_index_in_dim(segment_parts, block_index, 0, keepdims=False)
        alive_block = lax.dynamic_index_in_dim(surviving, block_index, 0, keepdims=False)
        start_block = lax.dynamic_index_in_dim(start_state, block_index, 1, keepdims=False)
        carry_block = lax.dynamic_index_in_dim(start_decay, block_index, 1, keepdims=False)
        decay_end = lax.dynamic_index_in_dim(decay_block, within, 1, keepdims=False)
        segment_end = lax.dynamic_index_in_dim(segment_block, within, 0, keepdims=False)
        alive_end = lax.dynamic_index_in_dim(alive_block, within, 0, keepdims=False)
        upto_mask = ((offsets <= within) & (segment_block == segment_end)).astype(jnp.float32)
        partial_end = jnp.einsum(
            "hjc,hjd->hcd", key_block * upto_mask[None, :, None], value_block, precision=HIGH
        )
        grow = jnp.exp(decay_end)
        local_part = grow[..., None] * (alive_end * start_block + partial_end)
        high, low = hi_lo(grow * alive_end * carry_block)
        packet = jnp.concatenate(
            [local_part.astype(jnp.bfloat16), high[:, None, :], low[:, None, :]], axis=1
        )
        packets.append(jnp.where(inside, packet, jnp.zeros_like(packet)))
    held = route_packets(jnp.stack(packets), end_rows, owners, tok_rows, "seq")
    mine = lax.axis_index("seq")
    owned_source = jnp.sum(jnp.where(owners == mine, (end_rows - 1) // tok_rows, 0))
    incoming, owned_incoming = entering(device_decay, local_state, "seq", (mine, owned_source))
    held_coeff = held[:, HEAD].astype(jnp.float32) + held[:, HEAD + 1].astype(jnp.float32)
    handed_state = (held[:, :HEAD].astype(jnp.float32) + held_coeff[..., None] * owned_incoming)[None]
    block_state = start_state + start_decay[..., None] * incoming[:, None]
    carried_out = jnp.einsum("hnic,hncd->hnid", query_tilde, block_state, precision=HIGH)
    mixer_out = (inner_out + surviving[None, :, :, None] * carried_out).reshape(
        head_count, tok_rows, HEAD
    )
    rescale = lax.rsqrt(jnp.mean(mixer_out * mixer_out, axis=-1, keepdims=True) + EPS)
    mixed = (mixer_out * rescale * jax.nn.silu(gate_logit)).astype(jnp.bfloat16)
    out_split = output_weight.reshape(head_count, HEAD, output_weight.shape[1])
    partial_terms = jnp.einsum("htd,hdo->to", mixed, out_split, preferred_element_type=jnp.float32)
    residual = (hidden_in.astype(jnp.float32) + narrow_sum(partial_terms)).astype(jnp.bfloat16)
    widened = widen_rows(residual)
    normed_ffn = rms_rows(widened, swiglu_gain)
    hidden = (
        jax.nn.silu(project(normed_ffn, swiglu_gate)) * project(normed_ffn, swiglu_up)
    ).astype(jnp.bfloat16)
    down = project(hidden, swiglu_down)
    half = down.shape[0] // 2
    upper = lax.psum_scatter(down[:half].astype(jnp.bfloat16), "wa", scatter_dimension=1, tiled=True)
    summed = jnp.concatenate([upper.astype(jnp.float32), narrow_sum(down[half:])], axis=0)
    hidden_out = (residual.astype(jnp.float32) + summed).astype(jnp.bfloat16)
    return (hidden_out, handed_state)


def solution(mesh):
    in_specs = (
        P("seq", "wa"),
        P(),
        P(),
        P(),
        P(None, "wa"),
        P(None, "wa"),
        P(None, "wa"),
        P(None, "wa"),
        P("wa"),
        P("wa", None),
        P(),
        P(None, "wa"),
        P(None, "wa"),
        P("wa", None),
    )
    out_specs = (P("seq", "wa"), P("seq", "wa", None, None))
    return jax.shard_map(local, mesh=mesh, in_specs=in_specs, out_specs=out_specs, check_vma=False)
```

```python
import jax
import jax.numpy as jnp
from jax import lax
from jax.sharding import PartitionSpec as P

HEAD = 128
GROUP = 64
REQS = 4


EPS = 1e-06
HIGH = lax.Precision.HIGH


def hi_lo(values):
    high = values.astype(jnp.bfloat16)
    return high, (values - high.astype(jnp.float32)).astype(jnp.bfloat16)


def entering(decay, state, axis, targets):
    count = lax.axis_size(axis)
    rows = state.shape[1]
    high, low = hi_lo(decay)
    packed = jnp.concatenate([state.astype(jnp.bfloat16), high[:, None, :], low[:, None, :]], axis=1)
    every = lax.all_gather(packed, axis)
    decays = every[:, :, rows].astype(jnp.float32) + every[:, :, rows + 1].astype(jnp.float32)
    states = every[:, :, :rows].astype(jnp.float32)
    ranks = jnp.arange(count, dtype=jnp.int32)
    results = []
    for target in targets:
        earlier = (ranks < target)[:, None, None]
        masked = jnp.where(earlier, decays, 1.0)
        after = jnp.concatenate([lax.cumprod(masked, axis=0, reverse=True)[1:], jnp.ones_like(masked[:1])])
        weights = jnp.where(earlier, after, 0.0)
        results.append(jnp.sum(weights[..., None] * states, axis=0))
    return results


def route_packets(packets, end_rows, owners, tok_rows, axis):
    count, mine = (lax.axis_size(axis), lax.axis_index(axis))
    left = [(i, (i - 1) % count) for i in range(count)]
    first = lax.ppermute(packets[0], axis, left)
    last = lax.ppermute(packets[-1], axis, [(count - 1, count // 2 - 1)])
    place = ((end_rows - 1) // tok_rows)[1:-1]
    offset = (owners[1:-1] - place) % count

    def shifter(shift):
        pairs = [(i, (i + shift) % count) for i in range(count)]
        return lambda packet: lax.ppermute(packet, axis, pairs) if shift else packet

    branches = [shifter(shift) for shift in range(count)]
    middle = [lax.switch(offset[slot], branches, packets[1 + slot]) for slot in range(REQS - 2)]
    zero = jnp.zeros_like(first)
    held = jnp.where(owners[0] == mine, first, zero) + jnp.where(owners[-1] == mine, last, zero)
    for part in middle:
        held = held + part
    return held


def rms_rows(matrix, scaling):
    matrix = matrix.astype(jnp.float32)
    rescale = lax.rsqrt(jnp.mean(matrix * matrix, axis=-1, keepdims=True) + EPS)
    return (matrix * rescale * scaling).astype(jnp.bfloat16)


def project(matrix, weight):
    return jnp.dot(matrix, weight, preferred_element_type=jnp.float32)


def widen_rows(shard_part):
    return lax.all_gather(shard_part, "wa", axis=1, tiled=True)


def narrow_sum(partial_terms):
    rows, cols = partial_terms.shape
    count = lax.axis_size("wa")
    pieces = partial_terms.astype(jnp.bfloat16).reshape(rows, count, cols // count)
    got = lax.all_to_all(pieces, "wa", 1, 1)
    return jnp.sum(got.astype(jnp.float32), axis=1)


def local(
    hidden_in,
    request_spans,
    owners,
    mixer_gain,
    query_weight,
    forget_weight,
    input_weight,
    gate_weight,
    forget_bias,
    output_weight,
    swiglu_gain,
    swiglu_gate,
    swiglu_up,
    swiglu_down,
):
    tok_rows = hidden_in.shape[0]
    head_count = query_weight.shape[1] // HEAD
    block_count = tok_rows // GROUP
    half = tok_rows // 2
    count = lax.axis_size("wa")
    lower = hidden_in[half:]
    copies = jnp.broadcast_to(lower[None], (count,) + lower.shape)
    spread = lax.all_to_all(copies, "wa", 0, 0)
    spread = jnp.moveaxis(spread, 0, 1).reshape(tok_rows - half, count * lower.shape[1])
    gathered = jnp.concatenate([widen_rows(hidden_in[:half]), spread], axis=0)
    normed = rms_rows(gathered, mixer_gain)

    def heads(weight):
        split = weight.reshape(weight.shape[0], head_count, HEAD)
        return jnp.einsum("tk,khd->htd", normed, split, preferred_element_type=jnp.float32)

    queries = jax.nn.silu(heads(query_weight))
    forget_logit = heads(forget_weight) + forget_bias.reshape(head_count, 1, HEAD)
    log_decay = jax.nn.log_sigmoid(forget_logit)
    key_rows = jax.nn.sigmoid(-forget_logit)
    value_rows = heads(input_weight)
    gate_logit = heads(gate_weight)
    first_row = lax.axis_index("seq") * tok_rows
    position = first_row + jnp.arange(tok_rows, dtype=jnp.int32)
    start_rows = request_spans[:, 0]
    end_rows = request_spans[:, 1]
    is_start = jnp.any(position[:, None] == start_rows[None, :], axis=1)
    segment = jnp.sum((start_rows[None, :] <= position[:, None]).astype(jnp.int32), axis=1) - 1
    shape_four = (head_count, block_count, GROUP, HEAD)
    query_parts = queries.reshape(shape_four)
    key_parts = key_rows.reshape(shape_four)
    value_parts = value_rows.reshape(shape_four)
    segment_parts = segment.reshape(block_count, GROUP)
    keep_mask = (1.0 - is_start.astype(jnp.float32)).reshape(block_count, GROUP)
    cum_decay = jnp.cumsum(log_decay.reshape(shape_four), axis=2)
    surviving = jnp.cumprod(keep_mask, axis=1)
    query_tilde = query_parts * jnp.exp(cum_decay)
    key_tilde = key_parts * jnp.exp(-cum_decay)
    offsets = jnp.arange(GROUP, dtype=jnp.int32)
    causal = offsets[:, None] >= offsets[None, :]
    same_doc = causal[None] & (segment_parts[:, :, None] == segment_parts[:, None, :])
    scores = jnp.einsum("hnic,hnjc->hnij", query_tilde, key_tilde, precision=HIGH)
    scores = jnp.where(same_doc[None], scores, 0.0)
    inner_out = jnp.einsum("hnij,hnjd->hnid", scores, value_parts, precision=HIGH)
    tail_mask = (segment_parts == segment_parts[:, -1:]).astype(jnp.float32)
    last_decay = jnp.exp(cum_decay[:, :, -1])
    fresh = last_decay[..., None] * jnp.einsum(
        "hnjc,hnjd->hncd", key_tilde * tail_mask[None, :, :, None], value_parts, precision=HIGH
    )
    shrink = surviving[:, -1][None, :, None] * last_decay
    running = jnp.zeros((head_count, HEAD, HEAD), jnp.float32)
    product = jnp.ones((head_count, HEAD), jnp.float32)
    starts, carries = [], []
    for block in range(block_count):
        starts.append(running)
        carries.append(product)
        running = shrink[:, block, :, None] * running + fresh[:, block]
        product = product * shrink[:, block]
    local_state, device_decay = running, product
    start_state = jnp.stack(starts, axis=1)
    start_decay = jnp.stack(carries, axis=1)

    packets = []
    for request in range(REQS):
        local_end = end_rows[request] - 1 - first_row
        inside = (local_end >= 0) & (local_end < tok_rows)
        end_row = jnp.clip(local_end, 0, tok_rows - 1)
        block_index = end_row // GROUP
        within = end_row % GROUP
        decay_block = lax.dynamic_index_in_dim(cum_decay, block_index, 1, keepdims=False)
        key_block = lax.dynamic_index_in_dim(key_tilde, block_index, 1, keepdims=False)
        value_block = lax.dynamic_index_in_dim(value_parts, block_index, 1, keepdims=False)
        segment_block = lax.dynamic_index_in_dim(segment_parts, block_index, 0, keepdims=False)
        alive_block = lax.dynamic_index_in_dim(surviving, block_index, 0, keepdims=False)
        start_block = lax.dynamic_index_in_dim(start_state, block_index, 1, keepdims=False)
        carry_block = lax.dynamic_index_in_dim(start_decay, block_index, 1, keepdims=False)
        decay_end = lax.dynamic_index_in_dim(decay_block, within, 1, keepdims=False)
        segment_end = lax.dynamic_index_in_dim(segment_block, within, 0, keepdims=False)
        alive_end = lax.dynamic_index_in_dim(alive_block, within, 0, keepdims=False)
        upto_mask = ((offsets <= within) & (segment_block == segment_end)).astype(jnp.float32)
        partial_end = jnp.einsum(
            "hjc,hjd->hcd", key_block * upto_mask[None, :, None], value_block, precision=HIGH
        )
        grow = jnp.exp(decay_end)
        local_part = grow[..., None] * (alive_end * start_block + partial_end)
        high, low = hi_lo(grow * alive_end * carry_block)
        packet = jnp.concatenate(
            [local_part.astype(jnp.bfloat16), high[:, None, :], low[:, None, :]], axis=1
        )
        packets.append(jnp.where(inside, packet, jnp.zeros_like(packet)))
    held = route_packets(jnp.stack(packets), end_rows, owners, tok_rows, "seq")
    mine = lax.axis_index("seq")
    owned_source = jnp.sum(jnp.where(owners == mine, (end_rows - 1) // tok_rows, 0))
    incoming, owned_incoming = entering(device_decay, local_state, "seq", (mine, owned_source))
    held_coeff = held[:, HEAD].astype(jnp.float32) + held[:, HEAD + 1].astype(jnp.float32)
    handed_state = (held[:, :HEAD].astype(jnp.float32) + held_coeff[..., None] * owned_incoming)[None]
    block_state = start_state + start_decay[..., None] * incoming[:, None]
    carried_out = jnp.einsum("hnic,hncd->hnid", query_tilde, block_state, precision=HIGH)
    mixer_out = (inner_out + surviving[None, :, :, None] * carried_out).reshape(
        head_count, tok_rows, HEAD
    )
    rescale = lax.rsqrt(jnp.mean(mixer_out * mixer_out, axis=-1, keepdims=True) + EPS)
    mixed = (mixer_out * rescale * jax.nn.silu(gate_logit)).astype(jnp.bfloat16)
    out_split = output_weight.reshape(head_count, HEAD, output_weight.shape[1])
    partial_terms = jnp.einsum("htd,hdo->to", mixed, out_split, preferred_element_type=jnp.float32)
    residual = (hidden_in.astype(jnp.float32) + narrow_sum(partial_terms)).astype(jnp.bfloat16)
    widened = widen_rows(residual)
    normed_ffn = rms_rows(widened, swiglu_gain)
    hidden = (
        jax.nn.silu(project(normed_ffn, swiglu_gate)) * project(normed_ffn, swiglu_up)
    ).astype(jnp.bfloat16)
    hidden_out = (residual.astype(jnp.float32) + narrow_sum(project(hidden, swiglu_down))).astype(
        jnp.bfloat16
    )
    return (hidden_out, handed_state)


def solution(mesh):
    in_specs = (
        P("seq", "wa"),
        P(),
        P(),
        P(),
        P(None, "wa"),
        P(None, "wa"),
        P(None, "wa"),
        P(None, "wa"),
        P("wa"),
        P("wa", None),
        P(),
        P(None, "wa"),
        P(None, "wa"),
        P("wa", None),
    )
    out_specs = (P("seq", "wa"), P("seq", "wa", None, None))
    return jax.shard_map(local, mesh=mesh, in_specs=in_specs, out_specs=out_specs, check_vma=False)
```

```python
import jax
import jax.numpy as jnp
from jax import lax
from jax.sharding import PartitionSpec as P

HEAD = 128
GROUP = 64
REQS = 4


EPS = 1e-06
HIGH = lax.Precision.HIGH


def hi_lo(values):
    high = values.astype(jnp.bfloat16)
    return high, (values - high.astype(jnp.float32)).astype(jnp.bfloat16)


def entering(decay, state, axis, targets):
    count = lax.axis_size(axis)
    rows = state.shape[1]
    high, low = hi_lo(decay)
    packed = jnp.concatenate([state.astype(jnp.bfloat16), high[:, None, :], low[:, None, :]], axis=1)
    every = lax.all_gather(packed, axis)
    decays = every[:, :, rows].astype(jnp.float32) + every[:, :, rows + 1].astype(jnp.float32)
    states = every[:, :, :rows].astype(jnp.float32)
    ranks = jnp.arange(count, dtype=jnp.int32)
    results = []
    for target in targets:
        between = (ranks[None, :] > ranks[:, None]) & (ranks[None, :] < target)
        weights = jnp.prod(jnp.where(between[:, :, None, None], decays[None], 1.0), axis=1)
        weights = jnp.where((ranks < target)[:, None, None], weights, 0.0)
        results.append(jnp.sum(weights[..., None] * states, axis=0))
    return results


def route_packets(packets, end_rows, owners, tok_rows, axis):
    count, mine = (lax.axis_size(axis), lax.axis_index(axis))
    left = [(i, (i - 1) % count) for i in range(count)]
    first = lax.ppermute(packets[0], axis, left)
    last = lax.ppermute(packets[-1], axis, [(count - 1, count // 2 - 1)])
    place = ((end_rows - 1) // tok_rows)[1:-1]
    offset = (owners[1:-1] - place) % count

    def shifter(shift):
        pairs = [(i, (i + shift) % count) for i in range(count)]
        return lambda packet: lax.ppermute(packet, axis, pairs) if shift else packet

    branches = [shifter(shift) for shift in range(count)]
    middle = [lax.switch(offset[slot], branches, packets[1 + slot]) for slot in range(REQS - 2)]
    zero = jnp.zeros_like(first)
    held = jnp.where(owners[0] == mine, first, zero) + jnp.where(owners[-1] == mine, last, zero)
    for part in middle:
        held = held + part
    return held


def rms_rows(matrix, scaling):
    matrix = matrix.astype(jnp.float32)
    rescale = lax.rsqrt(jnp.mean(matrix * matrix, axis=-1, keepdims=True) + EPS)
    return (matrix * rescale * scaling).astype(jnp.bfloat16)


def project(matrix, weight):
    return jnp.dot(matrix, weight, preferred_element_type=jnp.float32)


def widen_rows(shard_part):
    return lax.all_gather(shard_part, "wa", axis=1, tiled=True)


def narrow_sum(blocks):
    got = lax.all_to_all(blocks.astype(jnp.bfloat16), "wa", 0, 0)
    return jnp.sum(got.astype(jnp.float32), axis=0)


def local(
    hidden_in,
    request_spans,
    owners,
    mixer_gain,
    query_weight,
    forget_weight,
    input_weight,
    gate_weight,
    forget_bias,
    output_weight,
    swiglu_gain,
    swiglu_gate,
    swiglu_up,
    swiglu_down,
):
    tok_rows = hidden_in.shape[0]
    head_count = query_weight.shape[1] // HEAD
    block_count = tok_rows // GROUP
    half = tok_rows // 2
    count = lax.axis_size("wa")
    lower = hidden_in[half:]
    copies = jnp.broadcast_to(lower[None], (count,) + lower.shape)
    spread = lax.all_to_all(copies, "wa", 0, 0)
    spread = jnp.moveaxis(spread, 0, 1).reshape(tok_rows - half, count * lower.shape[1])
    gathered = jnp.concatenate([widen_rows(hidden_in[:half]), spread], axis=0)
    normed = rms_rows(gathered, mixer_gain)

    def heads(weight):
        split = weight.reshape(weight.shape[0], head_count, HEAD)
        return jnp.einsum("tk,khd->htd", normed, split, preferred_element_type=jnp.float32)

    queries = jax.nn.silu(heads(query_weight))
    forget_logit = heads(forget_weight) + forget_bias.reshape(head_count, 1, HEAD)
    log_decay = jax.nn.log_sigmoid(forget_logit)
    key_rows = jax.nn.sigmoid(-forget_logit)
    value_rows = heads(input_weight)
    gate_logit = heads(gate_weight)
    first_row = lax.axis_index("seq") * tok_rows
    position = first_row + jnp.arange(tok_rows, dtype=jnp.int32)
    start_rows = request_spans[:, 0]
    end_rows = request_spans[:, 1]
    is_start = jnp.any(position[:, None] == start_rows[None, :], axis=1)
    segment = jnp.sum((start_rows[None, :] <= position[:, None]).astype(jnp.int32), axis=1) - 1
    shape_four = (head_count, block_count, GROUP, HEAD)
    query_parts = queries.reshape(shape_four)
    key_parts = key_rows.reshape(shape_four)
    value_parts = value_rows.reshape(shape_four)
    segment_parts = segment.reshape(block_count, GROUP)
    keep_mask = (1.0 - is_start.astype(jnp.float32)).reshape(block_count, GROUP)
    cum_decay = jnp.cumsum(log_decay.reshape(shape_four), axis=2)
    surviving = jnp.cumprod(keep_mask, axis=1)
    query_tilde = query_parts * jnp.exp(cum_decay)
    key_tilde = key_parts * jnp.exp(-cum_decay)
    offsets = jnp.arange(GROUP, dtype=jnp.int32)
    causal = offsets[:, None] >= offsets[None, :]
    same_doc = causal[None] & (segment_parts[:, :, None] == segment_parts[:, None, :])
    scores = jnp.einsum("hnic,hnjc->hnij", query_tilde, key_tilde, precision=HIGH)
    scores = jnp.where(same_doc[None], scores, 0.0)
    inner_out = jnp.einsum("hnij,hnjd->hnid", scores, value_parts, precision=HIGH)
    tail_mask = (segment_parts == segment_parts[:, -1:]).astype(jnp.float32)
    last_decay = jnp.exp(cum_decay[:, :, -1])
    fresh = last_decay[..., None] * jnp.einsum(
        "hnjc,hnjd->hncd", key_tilde * tail_mask[None, :, :, None], value_parts, precision=HIGH
    )
    shrink = surviving[:, -1][None, :, None] * last_decay
    running = jnp.zeros((head_count, HEAD, HEAD), jnp.float32)
    product = jnp.ones((head_count, HEAD), jnp.float32)
    starts, carries = [], []
    for block in range(block_count):
        starts.append(running)
        carries.append(product)
        running = shrink[:, block, :, None] * running + fresh[:, block]
        product = product * shrink[:, block]
    local_state, device_decay = running, product
    start_state = jnp.stack(starts, axis=1)
    start_decay = jnp.stack(carries, axis=1)

    packets = []
    for request in range(REQS):
        local_end = end_rows[request] - 1 - first_row
        inside = (local_end >= 0) & (local_end < tok_rows)
        end_row = jnp.clip(local_end, 0, tok_rows - 1)
        block_index = end_row // GROUP
        within = end_row % GROUP
        decay_block = lax.dynamic_index_in_dim(cum_decay, block_index, 1, keepdims=False)
        key_block = lax.dynamic_index_in_dim(key_tilde, block_index, 1, keepdims=False)
        value_block = lax.dynamic_index_in_dim(value_parts, block_index, 1, keepdims=False)
        segment_block = lax.dynamic_index_in_dim(segment_parts, block_index, 0, keepdims=False)
        alive_block = lax.dynamic_index_in_dim(surviving, block_index, 0, keepdims=False)
        start_block = lax.dynamic_index_in_dim(start_state, block_index, 1, keepdims=False)
        carry_block = lax.dynamic_index_in_dim(start_decay, block_index, 1, keepdims=False)
        decay_end = lax.dynamic_index_in_dim(decay_block, within, 1, keepdims=False)
        segment_end = lax.dynamic_index_in_dim(segment_block, within, 0, keepdims=False)
        alive_end = lax.dynamic_index_in_dim(alive_block, within, 0, keepdims=False)
        upto_mask = ((offsets <= within) & (segment_block == segment_end)).astype(jnp.float32)
        partial_end = jnp.einsum(
            "hjc,hjd->hcd", key_block * upto_mask[None, :, None], value_block, precision=HIGH
        )
        grow = jnp.exp(decay_end)
        local_part = grow[..., None] * (alive_end * start_block + partial_end)
        high, low = hi_lo(grow * alive_end * carry_block)
        packet = jnp.concatenate(
            [local_part.astype(jnp.bfloat16), high[:, None, :], low[:, None, :]], axis=1
        )
        packets.append(jnp.where(inside, packet, jnp.zeros_like(packet)))
    held = route_packets(jnp.stack(packets), end_rows, owners, tok_rows, "seq")
    mine = lax.axis_index("seq")
    owned_source = jnp.sum(jnp.where(owners == mine, (end_rows - 1) // tok_rows, 0))
    incoming, owned_incoming = entering(device_decay, local_state, "seq", (mine, owned_source))
    held_coeff = held[:, HEAD].astype(jnp.float32) + held[:, HEAD + 1].astype(jnp.float32)
    handed_state = (held[:, :HEAD].astype(jnp.float32) + held_coeff[..., None] * owned_incoming)[None]
    block_state = start_state + start_decay[..., None] * incoming[:, None]
    carried_out = jnp.einsum("hnic,hncd->hnid", query_tilde, block_state, precision=HIGH)
    mixer_out = (inner_out + surviving[None, :, :, None] * carried_out).reshape(
        head_count, tok_rows, HEAD
    )
    rescale = lax.rsqrt(jnp.mean(mixer_out * mixer_out, axis=-1, keepdims=True) + EPS)
    mixed = (mixer_out * rescale * jax.nn.silu(gate_logit)).astype(jnp.bfloat16)
    count = lax.axis_size("wa")
    out_split = output_weight.reshape(head_count, HEAD, count, output_weight.shape[1] // count)
    partial_terms = jnp.einsum("htd,hdjc->jtc", mixed, out_split, preferred_element_type=jnp.float32)
    residual = (hidden_in.astype(jnp.float32) + narrow_sum(partial_terms)).astype(jnp.bfloat16)
    widened = widen_rows(residual)
    normed_ffn = rms_rows(widened, swiglu_gain)
    hidden = (
        jax.nn.silu(project(normed_ffn, swiglu_gate)) * project(normed_ffn, swiglu_up)
    ).astype(jnp.bfloat16)
    down_split = swiglu_down.reshape(swiglu_down.shape[0], count, swiglu_down.shape[1] // count)
    down = jnp.einsum("tk,kjc->jtc", hidden, down_split, preferred_element_type=jnp.float32)
    hidden_out = (residual.astype(jnp.float32) + narrow_sum(down)).astype(jnp.bfloat16)
    return (hidden_out, handed_state)


def solution(mesh):
    in_specs = (
        P("seq", "wa"),
        P(),
        P(),
        P(),
        P(None, "wa"),
        P(None, "wa"),
        P(None, "wa"),
        P(None, "wa"),
        P("wa"),
        P("wa", None),
        P(),
        P(None, "wa"),
        P(None, "wa"),
        P("wa", None),
    )
    out_specs = (P("seq", "wa"), P("seq", "wa", None, None))
    return jax.shard_map(local, mesh=mesh, in_specs=in_specs, out_specs=out_specs, check_vma=False)
```

```python
import jax
import jax.numpy as jnp
from jax import lax
from jax.sharding import PartitionSpec as P

HEAD = 128
GROUP = 64
REQS = 4


EPS = 1e-06
HIGH = lax.Precision.HIGH


def hi_lo(values):
    high = values.astype(jnp.bfloat16)
    return high, (values - high.astype(jnp.float32)).astype(jnp.bfloat16)


def entering(decay, state, axis, targets):
    count = lax.axis_size(axis)
    rows = state.shape[1]
    high, low = hi_lo(decay)
    packed = jnp.concatenate([state.astype(jnp.bfloat16), high[:, None, :], low[:, None, :]], axis=1)
    every = lax.all_gather(packed, axis)
    decays = every[:, :, rows].astype(jnp.float32) + every[:, :, rows + 1].astype(jnp.float32)
    states = every[:, :, :rows].astype(jnp.float32)
    ranks = jnp.arange(count, dtype=jnp.int32)
    results = []
    for target in targets:
        between = (ranks[None, :] > ranks[:, None]) & (ranks[None, :] < target)
        weights = jnp.prod(jnp.where(between[:, :, None, None], decays[None], 1.0), axis=1)
        weights = jnp.where((ranks < target)[:, None, None], weights, 0.0)
        results.append(jnp.sum(weights[..., None] * states, axis=0))
    return results


def route_packets(packets, end_rows, owners, tok_rows, axis):
    count, mine = (lax.axis_size(axis), lax.axis_index(axis))
    left = [(i, (i - 1) % count) for i in range(count)]
    first = lax.ppermute(packets[0], axis, left)
    last = lax.ppermute(packets[-1], axis, [(count - 1, count // 2 - 1)])
    place = ((end_rows - 1) // tok_rows)[1:-1]
    offset = (owners[1:-1] - place) % count

    def shifter(shift):
        pairs = [(i, (i + shift) % count) for i in range(count)]
        return lambda packet: lax.ppermute(packet, axis, pairs) if shift else packet

    branches = [shifter(shift) for shift in range(count)]
    middle = [lax.switch(offset[slot], branches, packets[1 + slot]) for slot in range(REQS - 2)]
    zero = jnp.zeros_like(first)
    held = jnp.where(owners[0] == mine, first, zero) + jnp.where(owners[-1] == mine, last, zero)
    for part in middle:
        held = held + part
    return held


def rms_rows(matrix, scaling):
    matrix = matrix.astype(jnp.float32)
    rescale = lax.rsqrt(jnp.mean(matrix * matrix, axis=-1, keepdims=True) + EPS)
    return (matrix * rescale * scaling).astype(jnp.bfloat16)


def project(matrix, weight):
    return jnp.dot(matrix, weight, preferred_element_type=jnp.float32)


def widen_rows(shard_part):
    return lax.all_gather(shard_part, "wa", axis=1, tiled=True)


def narrow_sum(blocks):
    got = lax.all_to_all(blocks.astype(jnp.bfloat16), "wa", 0, 0)
    return jnp.sum(got.astype(jnp.float32), axis=0)


def local(
    hidden_in,
    request_spans,
    owners,
    mixer_gain,
    query_weight,
    forget_weight,
    input_weight,
    gate_weight,
    forget_bias,
    output_weight,
    swiglu_gain,
    swiglu_gate,
    swiglu_up,
    swiglu_down,
):
    tok_rows = hidden_in.shape[0]
    head_count = query_weight.shape[1] // HEAD
    block_count = tok_rows // GROUP
    half = tok_rows // 2
    count = lax.axis_size("wa")
    lower = hidden_in[half:]
    copies = jnp.broadcast_to(lower[None], (count,) + lower.shape)
    spread = lax.all_to_all(copies, "wa", 0, 0)
    spread = jnp.moveaxis(spread, 0, 1).reshape(tok_rows - half, count * lower.shape[1])
    gathered = jnp.concatenate([widen_rows(hidden_in[:half]), spread], axis=0)
    normed = rms_rows(gathered, mixer_gain)

    def heads(weight):
        split = weight.reshape(weight.shape[0], head_count, HEAD)
        return jnp.einsum("tk,khd->htd", normed, split, preferred_element_type=jnp.float32)

    queries = jax.nn.silu(heads(query_weight))
    forget_logit = heads(forget_weight) + forget_bias.reshape(head_count, 1, HEAD)
    log_decay = jax.nn.log_sigmoid(forget_logit)
    key_rows = jax.nn.sigmoid(-forget_logit)
    value_rows = heads(input_weight)
    gate_logit = heads(gate_weight)
    first_row = lax.axis_index("seq") * tok_rows
    position = first_row + jnp.arange(tok_rows, dtype=jnp.int32)
    start_rows = request_spans[:, 0]
    end_rows = request_spans[:, 1]
    is_start = jnp.any(position[:, None] == start_rows[None, :], axis=1)
    segment = jnp.sum((start_rows[None, :] <= position[:, None]).astype(jnp.int32), axis=1) - 1
    shape_four = (head_count, block_count, GROUP, HEAD)
    query_parts = queries.reshape(shape_four)
    key_parts = key_rows.reshape(shape_four)
    value_parts = value_rows.reshape(shape_four)
    segment_parts = segment.reshape(block_count, GROUP)
    keep_mask = (1.0 - is_start.astype(jnp.float32)).reshape(block_count, GROUP)
    cum_decay = jnp.cumsum(log_decay.reshape(shape_four), axis=2)
    surviving = jnp.cumprod(keep_mask, axis=1)
    query_tilde = query_parts * jnp.exp(cum_decay)
    key_tilde = key_parts * jnp.exp(-cum_decay)
    offsets = jnp.arange(GROUP, dtype=jnp.int32)
    causal = offsets[:, None] >= offsets[None, :]
    same_doc = causal[None] & (segment_parts[:, :, None] == segment_parts[:, None, :])
    scores = jnp.einsum("hnic,hnjc->hnij", query_tilde, key_tilde, precision=HIGH)
    scores = jnp.where(same_doc[None], scores, 0.0)
    inner_out = jnp.einsum("hnij,hnjd->hnid", scores, value_parts, precision=HIGH)
    tail_mask = (segment_parts == segment_parts[:, -1:]).astype(jnp.float32)
    last_decay = jnp.exp(cum_decay[:, :, -1])
    fresh = last_decay[..., None] * jnp.einsum(
        "hnjc,hnjd->hncd", key_tilde * tail_mask[None, :, :, None], value_parts, precision=HIGH
    )
    shrink = surviving[:, -1][None, :, None] * last_decay
    steps = jnp.arange(block_count + 1, dtype=jnp.int32)
    blocks = steps[:block_count]
    between = (blocks[None, None, :] > blocks[None, :, None]) & (blocks[None, None, :] < steps[:, None, None])
    spans = jnp.prod(jnp.where(between[None, ..., None], shrink[:, None, None], 1.0), axis=3)
    spans = jnp.where((blocks[None, :] < steps[:, None])[None, :, :, None], spans, 0.0)
    sums = jnp.sum(spans[..., None] * fresh[:, None], axis=2)
    before = (blocks[None, :] < steps[:, None])[None, :, :, None]
    carries = jnp.prod(jnp.where(before, shrink[:, None], 1.0), axis=2)
    start_state, local_state = sums[:, :block_count], sums[:, block_count]
    start_decay, device_decay = carries[:, :block_count], carries[:, block_count]

    packets = []
    for request in range(REQS):
        local_end = end_rows[request] - 1 - first_row
        inside = (local_end >= 0) & (local_end < tok_rows)
        end_row = jnp.clip(local_end, 0, tok_rows - 1)
        block_index = end_row // GROUP
        within = end_row % GROUP
        decay_block = lax.dynamic_index_in_dim(cum_decay, block_index, 1, keepdims=False)
        key_block = lax.dynamic_index_in_dim(key_tilde, block_index, 1, keepdims=False)
        value_block = lax.dynamic_index_in_dim(value_parts, block_index, 1, keepdims=False)
        segment_block = lax.dynamic_index_in_dim(segment_parts, block_index, 0, keepdims=False)
        alive_block = lax.dynamic_index_in_dim(surviving, block_index, 0, keepdims=False)
        start_block = lax.dynamic_index_in_dim(start_state, block_index, 1, keepdims=False)
        carry_block = lax.dynamic_index_in_dim(start_decay, block_index, 1, keepdims=False)
        decay_end = lax.dynamic_index_in_dim(decay_block, within, 1, keepdims=False)
        segment_end = lax.dynamic_index_in_dim(segment_block, within, 0, keepdims=False)
        alive_end = lax.dynamic_index_in_dim(alive_block, within, 0, keepdims=False)
        upto_mask = ((offsets <= within) & (segment_block == segment_end)).astype(jnp.float32)
        partial_end = jnp.einsum(
            "hjc,hjd->hcd", key_block * upto_mask[None, :, None], value_block, precision=HIGH
        )
        grow = jnp.exp(decay_end)
        local_part = grow[..., None] * (alive_end * start_block + partial_end)
        high, low = hi_lo(grow * alive_end * carry_block)
        packet = jnp.concatenate(
            [local_part.astype(jnp.bfloat16), high[:, None, :], low[:, None, :]], axis=1
        )
        packets.append(jnp.where(inside, packet, jnp.zeros_like(packet)))
    held = route_packets(jnp.stack(packets), end_rows, owners, tok_rows, "seq")
    mine = lax.axis_index("seq")
    owned_source = jnp.sum(jnp.where(owners == mine, (end_rows - 1) // tok_rows, 0))
    incoming, owned_incoming = entering(device_decay, local_state, "seq", (mine, owned_source))
    held_coeff = held[:, HEAD].astype(jnp.float32) + held[:, HEAD + 1].astype(jnp.float32)
    handed_state = (held[:, :HEAD].astype(jnp.float32) + held_coeff[..., None] * owned_incoming)[None]
    block_state = start_state + start_decay[..., None] * incoming[:, None]
    carried_out = jnp.einsum("hnic,hncd->hnid", query_tilde, block_state, precision=HIGH)
    mixer_out = (inner_out + surviving[None, :, :, None] * carried_out).reshape(
        head_count, tok_rows, HEAD
    )
    rescale = lax.rsqrt(jnp.mean(mixer_out * mixer_out, axis=-1, keepdims=True) + EPS)
    mixed = (mixer_out * rescale * jax.nn.silu(gate_logit)).astype(jnp.bfloat16)
    count = lax.axis_size("wa")
    out_split = output_weight.reshape(head_count, HEAD, count, output_weight.shape[1] // count)
    partial_terms = jnp.einsum("htd,hdjc->jtc", mixed, out_split, preferred_element_type=jnp.float32)
    residual = (hidden_in.astype(jnp.float32) + narrow_sum(partial_terms)).astype(jnp.bfloat16)
    widened = widen_rows(residual)
    normed_ffn = rms_rows(widened, swiglu_gain)
    hidden = (
        jax.nn.silu(project(normed_ffn, swiglu_gate)) * project(normed_ffn, swiglu_up)
    ).astype(jnp.bfloat16)
    down_split = swiglu_down.reshape(swiglu_down.shape[0], count, swiglu_down.shape[1] // count)
    down = jnp.einsum("tk,kjc->jtc", hidden, down_split, preferred_element_type=jnp.float32)
    hidden_out = (residual.astype(jnp.float32) + narrow_sum(down)).astype(jnp.bfloat16)
    return (hidden_out, handed_state)


def solution(mesh):
    in_specs = (
        P("seq", "wa"),
        P(),
        P(),
        P(),
        P(None, "wa"),
        P(None, "wa"),
        P(None, "wa"),
        P(None, "wa"),
        P("wa"),
        P("wa", None),
        P(),
        P(None, "wa"),
        P(None, "wa"),
        P("wa", None),
    )
    out_specs = (P("seq", "wa"), P("seq", "wa", None, None))
    return jax.shard_map(local, mesh=mesh, in_specs=in_specs, out_specs=out_specs, check_vma=False)
```

```python
import jax
import jax.numpy as jnp
from jax import lax
from jax.sharding import PartitionSpec as P

HEAD = 128
GROUP = 64
REQS = 4


EPS = 1e-06
HIGH = lax.Precision.HIGH


def hi_lo(values):
    high = values.astype(jnp.bfloat16)
    return high, (values - high.astype(jnp.float32)).astype(jnp.bfloat16)


def entering(decay, state, axis, targets):
    count = lax.axis_size(axis)
    rows = state.shape[1]
    high, low = hi_lo(decay)
    packed = jnp.concatenate([state.astype(jnp.bfloat16), high[:, None, :], low[:, None, :]], axis=1)
    every = lax.all_gather(packed, axis)
    decays = every[:, :, rows].astype(jnp.float32) + every[:, :, rows + 1].astype(jnp.float32)
    states = every[:, :, :rows].astype(jnp.float32)
    ranks = jnp.arange(count, dtype=jnp.int32)
    results = []
    for target in targets:
        between = (ranks[None, :] > ranks[:, None]) & (ranks[None, :] < target)
        weights = jnp.prod(jnp.where(between[:, :, None, None], decays[None], 1.0), axis=1)
        weights = jnp.where((ranks < target)[:, None, None], weights, 0.0)
        results.append(jnp.sum(weights[..., None] * states, axis=0))
    return results


def route_packets(packets, end_rows, owners, tok_rows, axis):
    count, mine = (lax.axis_size(axis), lax.axis_index(axis))
    left = [(i, (i - 1) % count) for i in range(count)]
    first = lax.ppermute(packets[0], axis, left)
    last = lax.ppermute(packets[-1], axis, [(count - 1, count // 2 - 1)])
    place = ((end_rows - 1) // tok_rows)[1:-1]
    offset = (owners[1:-1] - place) % count

    def shifter(shift):
        pairs = [(i, (i + shift) % count) for i in range(count)]
        return lambda packet: lax.ppermute(packet, axis, pairs) if shift else packet

    branches = [shifter(shift) for shift in range(count)]
    middle = [lax.switch(offset[slot], branches, packets[1 + slot]) for slot in range(REQS - 2)]
    zero = jnp.zeros_like(first)
    held = jnp.where(owners[0] == mine, first, zero) + jnp.where(owners[-1] == mine, last, zero)
    for part in middle:
        held = held + part
    return held


def rms_rows(matrix, scaling):
    matrix = matrix.astype(jnp.float32)
    rescale = lax.rsqrt(jnp.mean(matrix * matrix, axis=-1, keepdims=True) + EPS)
    return (matrix * rescale * scaling).astype(jnp.bfloat16)


def project(matrix, weight):
    return jnp.dot(matrix, weight, preferred_element_type=jnp.float32)


def widen_rows(shard_part):
    return lax.all_gather(shard_part, "wa", axis=1, tiled=True)


def narrow_sum(blocks):
    got = lax.all_to_all(blocks.astype(jnp.bfloat16), "wa", 0, 0)
    return jnp.sum(got.astype(jnp.float32), axis=0)


def local(
    hidden_in,
    request_spans,
    owners,
    mixer_gain,
    query_weight,
    forget_weight,
    input_weight,
    gate_weight,
    forget_bias,
    output_weight,
    swiglu_gain,
    swiglu_gate,
    swiglu_up,
    swiglu_down,
):
    tok_rows = hidden_in.shape[0]
    head_count = query_weight.shape[1] // HEAD
    block_count = tok_rows // GROUP
    half = tok_rows // 2
    count = lax.axis_size("wa")
    lower = hidden_in[half:]
    copies = jnp.broadcast_to(lower[None], (count,) + lower.shape)
    spread = lax.all_to_all(copies, "wa", 0, 0)
    spread = jnp.moveaxis(spread, 0, 1).reshape(tok_rows - half, count * lower.shape[1])
    gathered = jnp.concatenate([widen_rows(hidden_in[:half]), spread], axis=0)
    normed = rms_rows(gathered, mixer_gain)

    def heads(weight):
        split = weight.reshape(weight.shape[0], head_count, HEAD)
        return jnp.einsum("tk,khd->htd", normed, split, preferred_element_type=jnp.float32)

    queries = jax.nn.silu(heads(query_weight))
    forget_logit = heads(forget_weight) + forget_bias.reshape(head_count, 1, HEAD)
    log_decay = jax.nn.log_sigmoid(forget_logit)
    key_rows = jax.nn.sigmoid(-forget_logit)
    value_rows = heads(input_weight)
    gate_logit = heads(gate_weight)
    first_row = lax.axis_index("seq") * tok_rows
    position = first_row + jnp.arange(tok_rows, dtype=jnp.int32)
    start_rows = request_spans[:, 0]
    end_rows = request_spans[:, 1]
    is_start = jnp.any(position[:, None] == start_rows[None, :], axis=1)
    segment = jnp.sum((start_rows[None, :] <= position[:, None]).astype(jnp.int32), axis=1) - 1
    shape_four = (head_count, block_count, GROUP, HEAD)
    query_parts = queries.reshape(shape_four)
    key_parts = key_rows.reshape(shape_four)
    value_parts = value_rows.reshape(shape_four)
    segment_parts = segment.reshape(block_count, GROUP)
    keep_mask = (1.0 - is_start.astype(jnp.float32)).reshape(block_count, GROUP)
    cum_decay = jnp.cumsum(log_decay.reshape(shape_four), axis=2)
    surviving = jnp.cumprod(keep_mask, axis=1)
    query_tilde = query_parts * jnp.exp(cum_decay)
    key_tilde = key_parts * jnp.exp(-cum_decay)
    offsets = jnp.arange(GROUP, dtype=jnp.int32)
    causal = offsets[:, None] >= offsets[None, :]
    same_doc = causal[None] & (segment_parts[:, :, None] == segment_parts[:, None, :])
    scores = jnp.einsum("hnic,hnjc->hnij", query_tilde, key_tilde, precision=HIGH)
    scores = jnp.where(same_doc[None], scores, 0.0)
    inner_out = jnp.einsum("hnij,hnjd->hnid", scores, value_parts, precision=HIGH)
    tail_mask = (segment_parts == segment_parts[:, -1:]).astype(jnp.float32)
    last_decay = jnp.exp(cum_decay[:, :, -1])
    fresh = last_decay[..., None] * jnp.einsum(
        "hnjc,hnjd->hncd", key_tilde * tail_mask[None, :, :, None], value_parts, precision=HIGH
    )
    shrink = surviving[:, -1][None, :, None] * last_decay
    running = jnp.zeros((head_count, HEAD, HEAD), jnp.float32)
    product = jnp.ones((head_count, HEAD), jnp.float32)
    starts, carries = [], []
    for block in range(block_count):
        starts.append(running)
        carries.append(product)
        running = shrink[:, block, :, None] * running + fresh[:, block]
        product = product * shrink[:, block]
    local_state, device_decay = running, product
    start_state = jnp.stack(starts, axis=1)
    start_decay = jnp.stack(carries, axis=1)

    packets = []
    for request in range(REQS):
        local_end = end_rows[request] - 1 - first_row
        inside = (local_end >= 0) & (local_end < tok_rows)
        end_row = jnp.clip(local_end, 0, tok_rows - 1)
        block_index = end_row // GROUP
        within = end_row % GROUP
        decay_block = lax.dynamic_index_in_dim(cum_decay, block_index, 1, keepdims=False)
        key_block = lax.dynamic_index_in_dim(key_tilde, block_index, 1, keepdims=False)
        value_block = lax.dynamic_index_in_dim(value_parts, block_index, 1, keepdims=False)
        segment_block = lax.dynamic_index_in_dim(segment_parts, block_index, 0, keepdims=False)
        alive_block = lax.dynamic_index_in_dim(surviving, block_index, 0, keepdims=False)
        start_block = lax.dynamic_index_in_dim(start_state, block_index, 1, keepdims=False)
        carry_block = lax.dynamic_index_in_dim(start_decay, block_index, 1, keepdims=False)
        decay_end = lax.dynamic_index_in_dim(decay_block, within, 1, keepdims=False)
        segment_end = lax.dynamic_index_in_dim(segment_block, within, 0, keepdims=False)
        alive_end = lax.dynamic_index_in_dim(alive_block, within, 0, keepdims=False)
        upto_mask = ((offsets <= within) & (segment_block == segment_end)).astype(jnp.float32)
        partial_end = jnp.einsum(
            "hjc,hjd->hcd", key_block * upto_mask[None, :, None], value_block, precision=HIGH
        )
        grow = jnp.exp(decay_end)
        local_part = grow[..., None] * (alive_end * start_block + partial_end)
        high, low = hi_lo(grow * alive_end * carry_block)
        packet = jnp.concatenate(
            [local_part.astype(jnp.bfloat16), high[:, None, :], low[:, None, :]], axis=1
        )
        packets.append(jnp.where(inside, packet, jnp.zeros_like(packet)))
    held = route_packets(jnp.stack(packets), end_rows, owners, tok_rows, "seq")
    mine = lax.axis_index("seq")
    owned_source = jnp.sum(jnp.where(owners == mine, (end_rows - 1) // tok_rows, 0))
    incoming, owned_incoming = entering(device_decay, local_state, "seq", (mine, owned_source))
    held_coeff = held[:, HEAD].astype(jnp.float32) + held[:, HEAD + 1].astype(jnp.float32)
    handed_state = (held[:, :HEAD].astype(jnp.float32) + held_coeff[..., None] * owned_incoming)[None]
    block_state = start_state + start_decay[..., None] * incoming[:, None]
    carried_out = jnp.einsum("hnic,hncd->hnid", query_tilde, block_state, precision=HIGH)
    mixer_out = (inner_out + surviving[None, :, :, None] * carried_out).reshape(
        head_count, tok_rows, HEAD
    )
    rescale = lax.rsqrt(jnp.mean(mixer_out * mixer_out, axis=-1, keepdims=True) + EPS)
    mixed = (mixer_out * rescale * jax.nn.silu(gate_logit)).astype(jnp.bfloat16)
    count = lax.axis_size("wa")
    out_split = output_weight.reshape(head_count, HEAD, count, output_weight.shape[1] // count)
    partial_terms = jnp.einsum("htd,hdjc->jtc", mixed, out_split, preferred_element_type=jnp.float32)
    residual = (hidden_in.astype(jnp.float32) + narrow_sum(partial_terms)).astype(jnp.bfloat16)
    widened = widen_rows(residual)
    normed_ffn = rms_rows(widened, swiglu_gain)
    units = swiglu_gate.shape[1]
    both = project(normed_ffn, jnp.concatenate([swiglu_gate, swiglu_up], axis=1))
    hidden = (jax.nn.silu(both[:, :units]) * both[:, units:]).astype(jnp.bfloat16)
    down_split = swiglu_down.reshape(swiglu_down.shape[0], count, swiglu_down.shape[1] // count)
    down = jnp.einsum("tk,kjc->jtc", hidden, down_split, preferred_element_type=jnp.float32)
    hidden_out = (residual.astype(jnp.float32) + narrow_sum(down)).astype(jnp.bfloat16)
    return (hidden_out, handed_state)


def solution(mesh):
    in_specs = (
        P("seq", "wa"),
        P(),
        P(),
        P(),
        P(None, "wa"),
        P(None, "wa"),
        P(None, "wa"),
        P(None, "wa"),
        P("wa"),
        P("wa", None),
        P(),
        P(None, "wa"),
        P(None, "wa"),
        P("wa", None),
    )
    out_specs = (P("seq", "wa"), P("seq", "wa", None, None))
    return jax.shard_map(local, mesh=mesh, in_specs=in_specs, out_specs=out_specs, check_vma=False)
```
